128 devices in a mesh: rec: 16 (over x, y), chan: 8 (over z, core).
Axes of the slice: x: 4, y: 4, z: 4, core: 2. Of those that a mesh axis runs over, the one named last changes fastest.
Arguments:
- signal: bfloat16 [4, 128, 614400], P(None, 'chan', 'rec'), may hold values from -6 to 6
- montage: int32 [4, 8, 16], P(None, 'chan'), may hold values from 0 to 15, each once within a row
- channels: int32 [4], replicated, may hold values from 19 to 128
- lengths: int32 [4], replicated, may hold values from 1537 to 3072
- boundary: int32 [4, 3072], P(None, 'rec'), may hold values 0 or 1
- conv_in: bfloat16 [16, 8, 5, 200, 128], P('rec', 'chan'), may hold values from -0.1875 to 0.1875
- conv_hid: bfloat16 [16, 8, 2, 5, 128, 128], P('rec', 'chan'), may hold values from -0.25 to 0.25
- mix_weight: bfloat16 [16, 8, 128, 512], P(None, 'chan'), may hold values from -0.046875 to 0.046875
- norm_gain: float32 [512], replicated, may hold values from 0.1 to 1.9
- emit_weight: float32 [512, 5], replicated, may hold values from -1 to 1
- trans_within: float32 [5, 5], replicated, may hold values from -3 to 3
- trans_between: float32 [5, 5], replicated, may hold values from -2 to 102
- initial: float32 [5], replicated, may hold values from -6 to 6
Outputs:
- filtered: float32 [4, 5, 3072], P(None, None, 'rec')
- log_rate: float32 [4], replicated
The draws below stay inside these ranges and needn't reach their ends.
All inputs are finite; a program needn't handle non-finite values. No bound on the sum of `boundary` on one device may be relied on, other than what follows from the above.
Results may differ from the reference program's by a relative error of at most 0.011.
Values may be sent and summed in bfloat16 or wider, within the bound.
No kernel may reach another device: no remote copies, remote signals or barrier semaphores. Data moves between devices by JAX's collectives and lax.ppermute only.
A program may use at most 128 MiB of HBM per device.

```python
import jax
import jax.numpy as jnp
from jax import lax

SAMP = 200
EMB = 128
MIX = 512
TAPS = 5
LAYERS = 2
STATES = 5
RECS = 4
GROUP = 16
TYPES = 128
NPATCH = 3072
NSAMP = 614400
N_CHAN = 8


def draw_trans_within(key, part):
    keys = jax.random.split(key, 2)
    diagonal_part = jax.random.uniform(keys[0], (STATES, STATES), jnp.float32, 1.0, 3.0)
    off_part = jax.random.uniform(keys[1], (STATES, STATES), jnp.float32, -3.0, -0.5)
    identity = jnp.eye(STATES, dtype=jnp.float32)
    return identity * diagonal_part + (1.0 - identity) * off_part


def draw_trans_between(key, part):
    base_values = jax.random.uniform(key, (STATES, STATES), jnp.float32, -2.0, 2.0)
    return base_values


def plant(values, key, low, largest):
    spot = [jax.random.randint(jax.random.fold_in(key, axis), (), 0, length) for axis, length in enumerate(values.shape)]
    longest = values.shape.index(max(values.shape))
    neighbour = spot[:longest] + [(spot[longest] + 1) % values.shape[longest]] + spot[longest + 1:]
    return values.at[tuple(spot)].set(low).at[tuple(neighbour)].set(largest)


def block_scale(key, extent, shards, smallest, largest):
    factor_of = 1.0
    for dim, blocks in shards:
        steps = jax.random.uniform(jax.random.fold_in(jax.random.fold_in(key, 6), dim), (blocks,), jnp.float32, smallest / len(shards), largest / len(shards))
        factor_of = factor_of * jnp.repeat(jnp.exp(steps), extent[dim] // blocks).reshape((-1,) + (1,) * (len(extent) - 1 - dim))
    return factor_of


def noise(rng, dims, spread, bound, cuts=(), kind=jnp.bfloat16):
    factor_of = block_scale(rng, dims, cuts, -0.22, 0.18) if cuts else 1.0
    values = jax.random.normal(rng, dims, jnp.float32) * spread * factor_of
    return jnp.minimum(jnp.maximum(values, -bound), bound).astype(kind)


def setup_inputs(seed: int = 0) -> dict:
    arg_keys = jax.random.split(jax.random.key(seed), 14)
    signal = noise(arg_keys[0], (RECS, TYPES, NSAMP), 1.0, 6.0, ((1, 8), (2, 16)))
    montage = jax.vmap(lambda own: jax.random.permutation(own, GROUP))(jax.random.split(arg_keys[1], RECS * N_CHAN)).reshape((RECS, N_CHAN, GROUP)).astype(jnp.int32)
    channels = plant(jax.random.randint(arg_keys[2], (RECS,), 19, TYPES + 1), jax.random.fold_in(arg_keys[2], 1), 19, TYPES).astype(jnp.int32)
    lengths = plant(jax.random.randint(arg_keys[3], (RECS,), NPATCH // 2 + 1, NPATCH + 1), jax.random.fold_in(arg_keys[3], 1), NPATCH // 2 + 1, NPATCH).astype(jnp.int32)
    boundary = plant((jax.random.randint(arg_keys[4], (RECS, NPATCH), 0, 8) < 1).astype(jnp.int32), jax.random.fold_in(arg_keys[4], 1), 0, 1)
    conv_in = noise(arg_keys[5], (GROUP, N_CHAN, TAPS, SAMP, EMB), (TAPS * SAMP) ** -0.5, 0.1875, ((0, 16), (1, 8)))
    conv_hid = noise(arg_keys[6], (GROUP, N_CHAN, LAYERS, TAPS, EMB, EMB), (TAPS * EMB) ** -0.5, 0.25, ((0, 16), (1, 8)))
    mix_weight = noise(arg_keys[7], (GROUP, N_CHAN, EMB, MIX), (TYPES * EMB) ** -0.5, 0.046875, ((1, 8),))
    norm_gain = jnp.clip(1.0 + 0.18 * jax.random.normal(arg_keys[8], (MIX,), jnp.float32), 0.1, 1.9)
    emit_weight = noise(arg_keys[9], (MIX, STATES), (MIX // 16) ** -0.5, 1.0, (), jnp.float32)
    trans_within = draw_trans_within(jax.random.fold_in(arg_keys[13], 71), 0)
    trans_between = draw_trans_between(jax.random.fold_in(arg_keys[13], 71), 0)
    initial = noise(arg_keys[12], (STATES,), 1.5, 6.0, (), jnp.float32)
    return {"signal": signal, "montage": montage, "channels": channels, "lengths": lengths, "boundary": boundary, "conv_in": conv_in, "conv_hid": conv_hid, "mix_weight": mix_weight, "norm_gain": norm_gain, "emit_weight": emit_weight, "trans_within": trans_within, "trans_between": trans_between, "initial": initial}


EPSILON = 1e-05

def log_sum_exp(values, along):
    peak_value = lax.optimization_barrier(jnp.max(values, axis=along, keepdims=True))
    return jnp.squeeze(peak_value, along) + jnp.log(lax.optimization_barrier(jnp.sum(jnp.exp(values - peak_value), axis=along)))

def temporal(patch_rows, taps):
    row_count, length, in_width = patch_rows.shape
    half_taps = taps.shape[0] // 2
    padded = jnp.pad(patch_rows, ((0, 0), (half_taps, half_taps), (0, 0)))
    accumulated = jnp.zeros((row_count * length, taps.shape[2]), jnp.float32)
    for offset in range(taps.shape[0]):
        window = padded[:, offset:offset + length].reshape(row_count * length, in_width)
        accumulated = accumulated + jnp.dot(window, taps[offset], preferred_element_type=jnp.float32)
    return accumulated.reshape(row_count, length, taps.shape[2])

def conv_stack(patch_rows, first_taps, hidden_taps):
    current = jax.nn.gelu(temporal(patch_rows, first_taps)).astype(jnp.bfloat16)
    for depth_index in range(hidden_taps.shape[0]):
        update = jax.nn.gelu(temporal(current, hidden_taps[depth_index]))
        current = (current.astype(jnp.float32) + update).astype(jnp.bfloat16)
    return current

def reference(signal, montage, channels, lengths, boundary, conv_in, conv_hid, mix_weight, norm_gain, emit_weight, trans_within, trans_between, initial):
    slot_ids = jnp.arange(TYPES, dtype=jnp.int32)
    live_slots = slot_ids[None, :] < channels[:, None]
    cleaned = jnp.where(live_slots[:, :, None], signal, jnp.zeros((), jnp.bfloat16))
    cleaned = cleaned.reshape(RECS, N_CHAN, GROUP, NPATCH, SAMP)
    places = jnp.arange(GROUP, dtype=jnp.int32)
    matches = montage[:, :, :, None] == places[None, None, None, :]
    inverse = lax.optimization_barrier(jnp.sum(jnp.where(matches, places[None, None, :, None], 0), axis=2)).astype(jnp.int32)

    def one_type(mixed_sum, type_index):
        owner = type_index // N_CHAN
        column = type_index % N_CHAN
        group_rows = lax.dynamic_index_in_dim(cleaned, column, 1, keepdims=False)
        picked = lax.dynamic_index_in_dim(inverse, column, 1, keepdims=False)
        slot_pick = lax.dynamic_index_in_dim(picked, owner, 1, keepdims=False).astype(jnp.int32)
        patch_rows = jnp.take_along_axis(group_rows, slot_pick[:, None, None, None], axis=1)[:, 0]
        encoded = conv_stack(patch_rows, conv_in[owner, column], conv_hid[owner, column])
        mixed_sum = mixed_sum + jnp.dot(encoded.reshape(RECS * NPATCH, EMB), mix_weight[owner, column], preferred_element_type=jnp.float32)
        return (mixed_sum, None)
    mixed, _ = lax.scan(one_type, jnp.zeros((RECS * NPATCH, MIX), jnp.float32), jnp.arange(TYPES, dtype=jnp.int32))
    average = lax.optimization_barrier(jnp.mean(mixed, axis=-1, keepdims=True))
    centred = mixed - average
    variance = lax.optimization_barrier(jnp.mean(centred * centred, axis=-1, keepdims=True))
    activated = jax.nn.gelu(centred * lax.rsqrt(variance + EPSILON) * norm_gain)
    emission = jnp.dot(activated, emit_weight, precision=lax.Precision.HIGHEST).reshape(RECS, NPATCH, STATES)
    prior = initial - log_sum_exp(initial, 0)
    start_state = jnp.broadcast_to(prior, (RECS, STATES))
    positions = jnp.arange(NPATCH, dtype=jnp.int32)
    valid = positions[None, :] < lengths[:, None]
    cross = boundary == 1

    def advance(carried, inputs):
        current, running = carried
        emit_now, cross_now, valid_now = inputs
        transition = jnp.where(cross_now[:, None, None], trans_between[None], trans_within[None])
        moved = log_sum_exp(current[:, :, None] + transition, 1) + emit_now
        log_level = log_sum_exp(moved, 1)
        current = jnp.where(valid_now[:, None], moved - log_level[:, None], current)
        running = running + jnp.where(valid_now, log_level, jnp.zeros_like(log_level))
        return ((current, running), current)
    (last_state, running), history = lax.scan(advance, (start_state, jnp.zeros((RECS,), jnp.float32)), (jnp.transpose(emission, (1, 0, 2)), cross.T, valid.T))
    filtered = jnp.transpose(history, (1, 2, 0))
    log_rate = running / lengths.astype(jnp.float32)
    return (filtered, log_rate)
```

```python
import functools

import jax
import jax.numpy as jnp
from jax import lax
from jax.experimental import pallas as pl
from jax.sharding import PartitionSpec as P

SAMP = 200
EMB = 128
STATES = 5


EPSILON = 1e-05
NEGATIVE = -1e30


def log_sum_exp(values, along):
    peak_value = jnp.max(values, axis=along, keepdims=True)
    return jnp.squeeze(peak_value, along) + jnp.log(
        jnp.sum(jnp.exp(values - peak_value), axis=along)
    )


def temporal(patch_rows, taps):
    row_count, length, in_width = patch_rows.shape
    half_taps = taps.shape[0] // 2
    padded = jnp.pad(patch_rows, ((0, 0), (half_taps, half_taps), (0, 0)))
    accumulated = jnp.zeros((row_count * length, taps.shape[2]), jnp.float32)
    for offset in range(taps.shape[0]):
        window = padded[:, offset : offset + length].reshape(row_count * length, in_width)
        accumulated = accumulated + jnp.dot(
            window, taps[offset], preferred_element_type=jnp.float32
        )
    return accumulated.reshape(row_count, length, taps.shape[2])


def conv_stack(patch_rows, first_taps, hidden_taps):
    current = jax.nn.gelu(temporal(patch_rows, first_taps)).astype(jnp.bfloat16)
    for depth_index in range(hidden_taps.shape[0]):
        update = jax.nn.gelu(temporal(current, hidden_taps[depth_index]))
        current = (current.astype(jnp.float32) + update).astype(jnp.bfloat16)
    return current


LANES = 128


def forward_step(state, matrices, extra):
    terms = [state[i : i + 1, :] + matrices[i] for i in range(len(matrices))]
    peak = functools.reduce(jnp.maximum, terms)
    total = functools.reduce(lambda x, y: x + y, [jnp.exp(t - peak) for t in terms])
    moved = peak + jnp.log(total)
    if extra is not None:
        moved = moved + extra
    top = jnp.max(moved, axis=0, keepdims=True)
    level = top + jnp.log(jnp.sum(jnp.exp(moved - top), axis=0, keepdims=True))
    return moved - level, level


def prefix_kernel(within_ref, between_ref, start_ref, emit_ref, cross_ref, valid_ref, prefix_ref, offset_ref):
    patches = emit_ref.shape[0]
    within = [within_ref[i] for i in range(STATES)]
    between = [between_ref[i] for i in range(STATES)]

    def body(p, carry):
        state, offset = carry
        crossing = cross_ref[p] > 0.5
        counted = valid_ref[p] > 0.5
        matrices = [jnp.where(crossing, between[i], within[i]) for i in range(STATES)]
        moved, level = forward_step(state, matrices, emit_ref[p])
        state = jnp.where(counted, moved, state)
        offset = offset + jnp.where(counted, level, 0.0)
        prefix_ref[p] = state
        offset_ref[p] = offset
        return state, offset

    lax.fori_loop(0, patches, body, (start_ref[...], jnp.zeros((1, LANES), jnp.float32)))


def chain_kernel(prior_ref, mats_ref, incoming_ref, total_ref):
    count = mats_ref.shape[0]

    def body(k, carry):
        state, total = carry
        incoming_ref[k] = state
        matrices = [mats_ref[k, j] for j in range(STATES)]
        moved, level = forward_step(state, matrices, None)
        return moved, total + level

    _, total = lax.fori_loop(0, count, body, (prior_ref[...], jnp.zeros((1, LANES), jnp.float32)))
    total_ref[...] = total


def lanes_padded(values):
    pad = [(0, 0)] * (values.ndim - 1) + [(0, LANES - values.shape[-1])]
    return jnp.pad(values, pad)


def crf_forward(emission, cross, valid, trans_within, trans_between, initial, rec_index):
    recordings, patches, _ = emission.shape
    width = STATES * recordings
    emit_in = lanes_padded(jnp.tile(jnp.transpose(emission, (1, 2, 0)), (1, 1, STATES)))
    cross_in = lanes_padded(jnp.tile(cross.T.astype(jnp.float32), (1, STATES)))[:, None, :]
    valid_in = lanes_padded(jnp.tile(valid.T.astype(jnp.float32), (1, STATES)))[:, None, :]
    lane_start = jnp.arange(width, dtype=jnp.int32) // recordings
    basis = jnp.arange(STATES, dtype=jnp.int32)[:, None] == lane_start[None, :]
    start = lanes_padded(jnp.where(basis, 0.0, NEGATIVE).astype(jnp.float32))
    within_in = jnp.broadcast_to(trans_within[:, :, None], (STATES, STATES, LANES))
    between_in = jnp.broadcast_to(trans_between[:, :, None], (STATES, STATES, LANES))
    prefix, offset = pl.pallas_call(
        prefix_kernel,
        out_shape=(
            jax.ShapeDtypeStruct((patches, STATES, LANES), jnp.float32),
            jax.ShapeDtypeStruct((patches, 1, LANES), jnp.float32),
        ),
        cost_estimate=pl.CostEstimate(
            flops=patches * 80 * LANES * 8, transcendentals=patches * 8 * LANES * 8,
            bytes_accessed=patches * 14 * LANES * 4,
        ),
    )(within_in, between_in, start, emit_in, cross_in, valid_in)
    prefix_sj = prefix[:, :, :width].reshape(patches, STATES, STATES, recordings)
    offset_j = offset[:, 0, :width].reshape(patches, STATES, recordings)
    transfer = prefix_sj[patches - 1] + offset_j[patches - 1][None]
    transfer = jnp.transpose(transfer, (1, 0, 2))
    gathered = lax.all_gather(transfer, "rec")
    mats = lanes_padded(gathered)
    prior = initial - log_sum_exp(initial, 0)
    prior_in = lanes_padded(jnp.broadcast_to(prior[:, None], (STATES, recordings)))
    groups = gathered.shape[0]
    incoming, total = pl.pallas_call(
        chain_kernel,
        out_shape=(
            jax.ShapeDtypeStruct((groups, STATES, LANES), jnp.float32),
            jax.ShapeDtypeStruct((1, LANES), jnp.float32),
        ),
    )(prior_in, mats)
    here = lax.dynamic_index_in_dim(incoming, rec_index, 0, keepdims=False)[:, :recordings]
    weights = here[None, None] + offset_j[:, None] + prefix_sj
    reached = log_sum_exp(weights, 2)
    totals = log_sum_exp(reached, 1)
    filtered = jnp.transpose(reached - totals[:, None], (2, 1, 0))
    return filtered, total[0, :recordings]


def prefix_kernel(within_ref, between_ref, start_ref, emit_ref, cross_ref, valid_ref, prefix_ref, offset_ref):
    patches = emit_ref.shape[0]
    within = [within_ref[i] for i in range(STATES)]
    between = [between_ref[i] for i in range(STATES)]

    def body(p, carry):
        state, offset = carry
        crossing = cross_ref[p] > 0.5
        counted = valid_ref[p] > 0.5
        matrices = [jnp.where(crossing, between[i], within[i]) for i in range(STATES)]
        moved, level = forward_step(state, matrices, emit_ref[p])
        state = jnp.where(counted, moved, state)
        offset = offset + jnp.where(counted, level, 0.0)
        prefix_ref[p] = state
        offset_ref[p] = offset
        return state, offset

    lax.fori_loop(0, patches, body, (start_ref[...], jnp.zeros((1, LANES), jnp.float32)))


def chain_kernel(prior_ref, mats_ref, incoming_ref, total_ref):
    count = mats_ref.shape[0]

    def body(k, carry):
        state, total = carry
        incoming_ref[k] = state
        matrices = [mats_ref[k, j] for j in range(STATES)]
        moved, level = forward_step(state, matrices, None)
        return moved, total + level

    _, total = lax.fori_loop(0, count, body, (prior_ref[...], jnp.zeros((1, LANES), jnp.float32)))
    total_ref[...] = total


def lanes_padded(values):
    pad = [(0, 0)] * (values.ndim - 1) + [(0, LANES - values.shape[-1])]
    return jnp.pad(values, pad)


def crf_forward(emission, cross, valid, trans_within, trans_between, initial, rec_index):
    recordings, patches, _ = emission.shape
    width = STATES * recordings
    emit_in = lanes_padded(jnp.tile(jnp.transpose(emission, (1, 2, 0)), (1, 1, STATES)))
    cross_in = lanes_padded(jnp.tile(cross.T.astype(jnp.float32), (1, STATES)))[:, None, :]
    valid_in = lanes_padded(jnp.tile(valid.T.astype(jnp.float32), (1, STATES)))[:, None, :]
    lane_start = jnp.arange(width, dtype=jnp.int32) // recordings
    basis = jnp.arange(STATES, dtype=jnp.int32)[:, None] == lane_start[None, :]
    start = lanes_padded(jnp.where(basis, 0.0, NEGATIVE).astype(jnp.float32))
    within_in = jnp.broadcast_to(trans_within[:, :, None], (STATES, STATES, LANES))
    between_in = jnp.broadcast_to(trans_between[:, :, None], (STATES, STATES, LANES))
    prefix, offset = pl.pallas_call(
        prefix_kernel,
        out_shape=(
            jax.ShapeDtypeStruct((patches, STATES, LANES), jnp.float32),
            jax.ShapeDtypeStruct((patches, 1, LANES), jnp.float32),
        ),
        cost_estimate=pl.CostEstimate(
            flops=patches * 80 * LANES * 8, transcendentals=patches * 8 * LANES * 8,
            bytes_accessed=patches * 14 * LANES * 4,
        ),
    )(within_in, between_in, start, emit_in, cross_in, valid_in)
    prefix_sj = prefix[:, :, :width].reshape(patches, STATES, STATES, recordings)
    offset_j = offset[:, 0, :width].reshape(patches, STATES, recordings)
    transfer = prefix_sj[patches - 1] + offset_j[patches - 1][None]
    transfer = jnp.transpose(transfer, (1, 0, 2))
    gathered = lax.all_gather(transfer, "rec")
    mats = lanes_padded(gathered)
    prior = initial - log_sum_exp(initial, 0)
    prior_in = lanes_padded(jnp.broadcast_to(prior[:, None], (STATES, recordings)))
    groups = gathered.shape[0]
    incoming, total = pl.pallas_call(
        chain_kernel,
        out_shape=(
            jax.ShapeDtypeStruct((groups, STATES, LANES), jnp.float32),
            jax.ShapeDtypeStruct((1, LANES), jnp.float32),
        ),
    )(prior_in, mats)
    here = lax.dynamic_index_in_dim(incoming, rec_index, 0, keepdims=False)[:, :recordings]
    weights = here[None, None] + offset_j[:, None] + prefix_sj
    reached = log_sum_exp(weights, 2)
    totals = log_sum_exp(reached, 1)
    filtered = jnp.transpose(reached - totals[:, None], (2, 1, 0))
    return filtered, total[0, :recordings]


def local(
    signal,
    montage,
    channels,
    lengths,
    boundary,
    conv_in,
    conv_hid,
    mix_weight,
    norm_gain,
    emit_weight,
    trans_within,
    trans_between,
    initial,
):
    groups = lax.axis_size("rec")
    chan_index = lax.axis_index("chan")
    rec_index = lax.axis_index("rec")
    recordings = signal.shape[0]
    patches = signal.shape[2] // SAMP
    slot_ids = chan_index * groups + jnp.arange(groups, dtype=jnp.int32)
    live_slots = slot_ids[None, :] < channels[:, None]
    cleaned = jnp.where(live_slots[:, :, None], signal, jnp.zeros((), jnp.bfloat16))
    places = jnp.arange(groups, dtype=jnp.int32)
    matches = montage[:, 0, :, None] == places[None, None, :]
    inverse = jnp.sum(jnp.where(matches, places[None, :, None], 0), axis=1)
    outgoing = jnp.take_along_axis(cleaned, inverse[:, :, None], axis=1)
    received = lax.all_to_all(outgoing, "rec", split_axis=1, concat_axis=1, tiled=True)
    item_count = received.shape[0]
    patch_rows = received.reshape(item_count, groups * patches, SAMP)
    encoded = conv_stack(patch_rows, conv_in[0, 0], conv_hid[0, 0])
    shards = encoded.reshape(item_count, groups, patches, EMB)
    arrived = shards
    arrived = lax.all_to_all(arrived, "rec", split_axis=1, concat_axis=1, tiled=True)
    partial_value = jnp.einsum(
        "bkpe,keo->bpo", arrived, mix_weight[:, 0], preferred_element_type=jnp.float32
    )
    summed = lax.psum(partial_value, "chan")
    average = jnp.mean(summed, axis=-1, keepdims=True)
    centred = summed - average
    variance = jnp.mean(centred * centred, axis=-1, keepdims=True)
    activated = jax.nn.gelu(centred * lax.rsqrt(variance + EPSILON) * norm_gain)
    emission = jnp.einsum("bpo,os->bps", activated, emit_weight, precision=lax.Precision.HIGHEST)
    positions = rec_index * patches + jnp.arange(patches, dtype=jnp.int32)
    valid = positions[None, :] < lengths[:, None]
    cross = boundary == 1
    filtered, log_partition = crf_forward(
        emission, cross, valid, trans_within, trans_between, initial, rec_index
    )
    return (filtered, log_partition / lengths.astype(jnp.float32))


def solution(mesh):
    placed = (
        P(None, "chan", "rec"),
        P(None, "chan", None),
        P(),
        P(),
        P(None, "rec"),
        P("rec", "chan", None, None, None),
        P("rec", "chan", None, None, None, None),
        P(None, "chan", None, None),
        P(),
        P(),
        P(),
        P(),
        P(),
    )
    return jax.shard_map(
        local, mesh=mesh, in_specs=placed, out_specs=(P(None, None, "rec"), P()), check_vma=False
    )
```

```python
import functools

import jax
import jax.numpy as jnp
from jax import lax
from jax.experimental import pallas as pl
from jax.sharding import PartitionSpec as P

SAMP = 200
EMB = 128
STATES = 5


EPSILON = 1e-05
NEGATIVE = -1e30


def log_sum_exp(values, along):
    peak_value = jnp.max(values, axis=along, keepdims=True)
    return jnp.squeeze(peak_value, along) + jnp.log(
        jnp.sum(jnp.exp(values - peak_value), axis=along)
    )


LANES = 128


def forward_step(state, matrices, extra):
    terms = [state[i : i + 1, :] + matrices[i] for i in range(len(matrices))]
    peak = functools.reduce(jnp.maximum, terms)
    total = functools.reduce(lambda x, y: x + y, [jnp.exp(t - peak) for t in terms])
    moved = peak + jnp.log(total)
    if extra is not None:
        moved = moved + extra
    top = jnp.max(moved, axis=0, keepdims=True)
    level = top + jnp.log(jnp.sum(jnp.exp(moved - top), axis=0, keepdims=True))
    return moved - level, level


def prefix_kernel(within_ref, between_ref, start_ref, emit_ref, cross_ref, valid_ref, prefix_ref, offset_ref):
    patches = emit_ref.shape[0]
    within = [within_ref[i] for i in range(STATES)]
    between = [between_ref[i] for i in range(STATES)]

    def body(p, carry):
        state, offset = carry
        crossing = cross_ref[p] > 0.5
        counted = valid_ref[p] > 0.5
        matrices = [jnp.where(crossing, between[i], within[i]) for i in range(STATES)]
        moved, level = forward_step(state, matrices, emit_ref[p])
        state = jnp.where(counted, moved, state)
        offset = offset + jnp.where(counted, level, 0.0)
        prefix_ref[p] = state
        offset_ref[p] = offset
        return state, offset

    lax.fori_loop(0, patches, body, (start_ref[...], jnp.zeros((1, LANES), jnp.float32)))


def chain_kernel(prior_ref, mats_ref, incoming_ref, total_ref):
    count = mats_ref.shape[0]

    def body(k, carry):
        state, total = carry
        incoming_ref[k] = state
        matrices = [mats_ref[k, j] for j in range(STATES)]
        moved, level = forward_step(state, matrices, None)
        return moved, total + level

    _, total = lax.fori_loop(0, count, body, (prior_ref[...], jnp.zeros((1, LANES), jnp.float32)))
    total_ref[...] = total


def lanes_padded(values):
    pad = [(0, 0)] * (values.ndim - 1) + [(0, LANES - values.shape[-1])]
    return jnp.pad(values, pad)


def crf_forward(emission, cross, valid, trans_within, trans_between, initial, rec_index):
    recordings, patches, _ = emission.shape
    width = STATES * recordings
    emit_in = lanes_padded(jnp.tile(jnp.transpose(emission, (1, 2, 0)), (1, 1, STATES)))
    cross_in = lanes_padded(jnp.tile(cross.T.astype(jnp.float32), (1, STATES)))[:, None, :]
    valid_in = lanes_padded(jnp.tile(valid.T.astype(jnp.float32), (1, STATES)))[:, None, :]
    lane_start = jnp.arange(width, dtype=jnp.int32) // recordings
    basis = jnp.arange(STATES, dtype=jnp.int32)[:, None] == lane_start[None, :]
    start = lanes_padded(jnp.where(basis, 0.0, NEGATIVE).astype(jnp.float32))
    within_in = jnp.broadcast_to(trans_within[:, :, None], (STATES, STATES, LANES))
    between_in = jnp.broadcast_to(trans_between[:, :, None], (STATES, STATES, LANES))
    prefix, offset = pl.pallas_call(
        prefix_kernel,
        out_shape=(
            jax.ShapeDtypeStruct((patches, STATES, LANES), jnp.float32),
            jax.ShapeDtypeStruct((patches, 1, LANES), jnp.float32),
        ),
        cost_estimate=pl.CostEstimate(
            flops=patches * 80 * LANES * 8, transcendentals=patches * 8 * LANES * 8,
            bytes_accessed=patches * 14 * LANES * 4,
        ),
    )(within_in, between_in, start, emit_in, cross_in, valid_in)
    prefix_sj = prefix[:, :, :width].reshape(patches, STATES, STATES, recordings)
    offset_j = offset[:, 0, :width].reshape(patches, STATES, recordings)
    transfer = prefix_sj[patches - 1] + offset_j[patches - 1][None]
    transfer = jnp.transpose(transfer, (1, 0, 2))
    gathered = lax.all_gather(transfer, "rec")
    mats = lanes_padded(gathered)
    prior = initial - log_sum_exp(initial, 0)
    prior_in = lanes_padded(jnp.broadcast_to(prior[:, None], (STATES, recordings)))
    groups = gathered.shape[0]
    incoming, total = pl.pallas_call(
        chain_kernel,
        out_shape=(
            jax.ShapeDtypeStruct((groups, STATES, LANES), jnp.float32),
            jax.ShapeDtypeStruct((1, LANES), jnp.float32),
        ),
    )(prior_in, mats)
    here = lax.dynamic_index_in_dim(incoming, rec_index, 0, keepdims=False)[:, :recordings]
    weights = here[None, None] + offset_j[:, None] + prefix_sj
    reached = log_sum_exp(weights, 2)
    totals = log_sum_exp(reached, 1)
    filtered = jnp.transpose(reached - totals[:, None], (2, 1, 0))
    return filtered, total[0, :recordings]


def neighbour_shift(block, axis, distance):
    devices = range(lax.axis_size(axis))
    route = [(i - distance, i) for i in devices if i - distance in devices]
    return lax.ppermute(block, axis, route)


def valid_temporal(rows, taps):
    length = rows.shape[2] - taps.shape[1] + 1
    accumulated = None
    for offset in range(taps.shape[1]):
        term = jnp.einsum(
            "mbqc,mce->mbqe", rows[:, :, offset : offset + length], taps[:, offset],
            preferred_element_type=jnp.float32,
        )
        accumulated = term if accumulated is None else accumulated + term
    return accumulated


def halo_conv_stack(patch_rows, first_taps, hidden_taps, rec_index):
    patches = patch_rows.shape[2]
    reach = first_taps.shape[1] // 2
    layers = hidden_taps.shape[1]
    halo = reach * (layers + 1)
    total = patches * lax.axis_size("rec")
    from_left = neighbour_shift(patch_rows[:, :, patches - halo :], "rec", 1)
    from_right = neighbour_shift(patch_rows[:, :, :halo], "rec", -1)
    extended = jnp.concatenate([from_left, patch_rows, from_right], axis=2)

    def masked(values, margin):
        spot = rec_index * patches - margin + jnp.arange(values.shape[2], dtype=jnp.int32)
        keep = (spot >= 0) & (spot < total)
        return jnp.where(keep[None, None, :, None], values, jnp.zeros((), values.dtype))

    margin = halo - reach
    current = masked(jax.nn.gelu(valid_temporal(extended, first_taps)).astype(jnp.bfloat16), margin)
    for depth_index in range(layers):
        update = jax.nn.gelu(valid_temporal(current, hidden_taps[:, depth_index]))
        margin = margin - reach
        current = (current[:, :, reach : current.shape[2] - reach].astype(jnp.float32) + update).astype(jnp.bfloat16)
        if margin > 0:
            current = masked(current, margin)
    return current


def local(
    signal,
    montage,
    channels,
    lengths,
    boundary,
    conv_in,
    conv_hid,
    mix_weight,
    norm_gain,
    emit_weight,
    trans_within,
    trans_between,
    initial,
):
    groups = lax.axis_size("rec")
    chan_index = lax.axis_index("chan")
    rec_index = lax.axis_index("rec")
    recordings = signal.shape[0]
    patches = signal.shape[2] // SAMP
    slot_ids = chan_index * groups + jnp.arange(groups, dtype=jnp.int32)
    live_slots = slot_ids[None, :] < channels[:, None]
    places = jnp.arange(groups, dtype=jnp.int32)
    pick = (montage[:, 0, None, :] == places[None, :, None]) & live_slots[:, None, :]
    rows = jnp.einsum(
        "bms,bst->mbt", pick.astype(jnp.bfloat16), signal, preferred_element_type=jnp.float32
    ).astype(jnp.bfloat16)
    patch_rows = rows.reshape(groups, recordings, patches, SAMP)
    first_taps = lax.all_gather(conv_in[:, 0], "rec", tiled=True)
    hidden_taps = lax.all_gather(conv_hid[:, 0], "rec", tiled=True)
    encoded = halo_conv_stack(patch_rows, first_taps, hidden_taps, rec_index)
    partial_value = jnp.einsum(
        "mbpe,meo->bpo", encoded, mix_weight[:, 0], preferred_element_type=jnp.float32
    )
    summed = lax.psum(partial_value, "chan")
    average = jnp.mean(summed, axis=-1, keepdims=True)
    centred = summed - average
    variance = jnp.mean(centred * centred, axis=-1, keepdims=True)
    activated = jax.nn.gelu(centred * lax.rsqrt(variance + EPSILON) * norm_gain)
    emission = jnp.einsum("bpo,os->bps", activated, emit_weight, precision=lax.Precision.HIGHEST)
    positions = rec_index * patches + jnp.arange(patches, dtype=jnp.int32)
    valid = positions[None, :] < lengths[:, None]
    cross = boundary == 1
    filtered, log_partition = crf_forward(
        emission, cross, valid, trans_within, trans_between, initial, rec_index
    )
    return (filtered, log_partition / lengths.astype(jnp.float32))


def solution(mesh):
    placed = (
        P(None, "chan", "rec"),
        P(None, "chan", None),
        P(),
        P(),
        P(None, "rec"),
        P("rec", "chan", None, None, None),
        P("rec", "chan", None, None, None, None),
        P(None, "chan", None, None),
        P(),
        P(),
        P(),
        P(),
        P(),
    )
    return jax.shard_map(
        local, mesh=mesh, in_specs=placed, out_specs=(P(None, None, "rec"), P()), check_vma=False
    )
```

```python
import functools

import jax
import jax.numpy as jnp
from jax import lax
from jax.experimental import pallas as pl
from jax.experimental.pallas import tpu as pltpu
from jax.sharding import PartitionSpec as P

SAMP = 200
EMB = 128
STATES = 5


EPSILON = 1e-05
NEGATIVE = -1e30


def log_sum_exp(values, along):
    peak_value = jnp.max(values, axis=along, keepdims=True)
    return jnp.squeeze(peak_value, along) + jnp.log(
        jnp.sum(jnp.exp(values - peak_value), axis=along)
    )


LANES = 128


def forward_step(state, matrices, extra):
    terms = [state[i : i + 1, :] + matrices[i] for i in range(len(matrices))]
    peak = functools.reduce(jnp.maximum, terms)
    total = functools.reduce(lambda x, y: x + y, [jnp.exp(t - peak) for t in terms])
    moved = peak + jnp.log(total)
    if extra is not None:
        moved = moved + extra
    top = jnp.max(moved, axis=0, keepdims=True)
    level = top + jnp.log(jnp.sum(jnp.exp(moved - top), axis=0, keepdims=True))
    return moved - level, level


def prefix_kernel(within_ref, between_ref, start_ref, emit_ref, cross_ref, valid_ref, prefix_ref, offset_ref):
    patches = emit_ref.shape[0]
    within = [within_ref[i] for i in range(STATES)]
    between = [between_ref[i] for i in range(STATES)]

    def body(p, carry):
        state, offset = carry
        crossing = cross_ref[p] > 0.5
        counted = valid_ref[p] > 0.5
        matrices = [jnp.where(crossing, between[i], within[i]) for i in range(STATES)]
        moved, level = forward_step(state, matrices, emit_ref[p])
        state = jnp.where(counted, moved, state)
        offset = offset + jnp.where(counted, level, 0.0)
        prefix_ref[p] = state
        offset_ref[p] = offset
        return state, offset

    lax.fori_loop(0, patches, body, (start_ref[...], jnp.zeros((1, LANES), jnp.float32)))


def chain_kernel(prior_ref, mats_ref, incoming_ref, total_ref):
    count = mats_ref.shape[0]

    def body(k, carry):
        state, total = carry
        incoming_ref[k] = state
        matrices = [mats_ref[k, j] for j in range(STATES)]
        moved, level = forward_step(state, matrices, None)
        return moved, total + level

    _, total = lax.fori_loop(0, count, body, (prior_ref[...], jnp.zeros((1, LANES), jnp.float32)))
    total_ref[...] = total


def lanes_padded(values):
    pad = [(0, 0)] * (values.ndim - 1) + [(0, LANES - values.shape[-1])]
    return jnp.pad(values, pad)


def crf_forward(emission, cross, valid, trans_within, trans_between, initial, rec_index):
    recordings, patches, _ = emission.shape
    width = STATES * recordings
    emit_in = lanes_padded(jnp.tile(jnp.transpose(emission, (1, 2, 0)), (1, 1, STATES)))
    cross_in = lanes_padded(jnp.tile(cross.T.astype(jnp.float32), (1, STATES)))[:, None, :]
    valid_in = lanes_padded(jnp.tile(valid.T.astype(jnp.float32), (1, STATES)))[:, None, :]
    lane_start = jnp.arange(width, dtype=jnp.int32) // recordings
    basis = jnp.arange(STATES, dtype=jnp.int32)[:, None] == lane_start[None, :]
    start = lanes_padded(jnp.where(basis, 0.0, NEGATIVE).astype(jnp.float32))
    within_in = jnp.broadcast_to(trans_within[:, :, None], (STATES, STATES, LANES))
    between_in = jnp.broadcast_to(trans_between[:, :, None], (STATES, STATES, LANES))
    prefix, offset = pl.pallas_call(
        prefix_kernel,
        out_shape=(
            jax.ShapeDtypeStruct((patches, STATES, LANES), jnp.float32),
            jax.ShapeDtypeStruct((patches, 1, LANES), jnp.float32),
        ),
        cost_estimate=pl.CostEstimate(
            flops=patches * 80 * LANES * 8, transcendentals=patches * 8 * LANES * 8,
            bytes_accessed=patches * 14 * LANES * 4,
        ),
    )(within_in, between_in, start, emit_in, cross_in, valid_in)
    prefix_sj = prefix[:, :, :width].reshape(patches, STATES, STATES, recordings)
    offset_j = offset[:, 0, :width].reshape(patches, STATES, recordings)
    transfer = prefix_sj[patches - 1] + offset_j[patches - 1][None]
    transfer = jnp.transpose(transfer, (1, 0, 2))
    gathered = lax.all_gather(transfer, "rec")
    mats = lanes_padded(gathered)
    prior = initial - log_sum_exp(initial, 0)
    prior_in = lanes_padded(jnp.broadcast_to(prior[:, None], (STATES, recordings)))
    groups = gathered.shape[0]
    incoming, total = pl.pallas_call(
        chain_kernel,
        out_shape=(
            jax.ShapeDtypeStruct((groups, STATES, LANES), jnp.float32),
            jax.ShapeDtypeStruct((1, LANES), jnp.float32),
        ),
    )(prior_in, mats)
    here = lax.dynamic_index_in_dim(incoming, rec_index, 0, keepdims=False)[:, :recordings]
    weights = here[None, None] + offset_j[:, None] + prefix_sj
    reached = log_sum_exp(weights, 2)
    totals = log_sum_exp(reached, 1)
    filtered = jnp.transpose(reached - totals[:, None], (2, 1, 0))
    return filtered, total[0, :recordings]


def neighbour_shift(block, axis, distance):
    devices = range(lax.axis_size(axis))
    route = [(i - distance, i) for i in devices if i - distance in devices]
    return lax.ppermute(block, axis, route)


def halo_rows(patch_rows):
    patches = patch_rows.shape[2]
    halo = 6
    from_left = neighbour_shift(patch_rows[:, :, patches - halo :], "rec", 1)
    from_right = neighbour_shift(patch_rows[:, :, :halo], "rec", -1)
    return jnp.concatenate([from_left, patch_rows, from_right], axis=2)

def tap_sum(rows, weight_of, taps, length):
    accumulated = None
    for offset in range(taps):
        product = jnp.dot(rows, weight_of(offset), preferred_element_type=jnp.float32)
        product = product[offset : offset + length]
        accumulated = product if accumulated is None else accumulated + product
    return accumulated


def conv_mix_kernel(rows_ref, first_ref, hidden_ref, mix_ref, keep_a_ref, keep_b_ref, out_ref):
    @pl.when(pl.program_id(0) == 0)
    def _():
        out_ref[...] = jnp.zeros_like(out_ref)

    taps = first_ref.shape[1]
    reach = taps // 2
    layers = hidden_ref.shape[1]
    keeps = [keep_a_ref[...] > 0.5, keep_b_ref[...] > 0.5]
    for item in range(rows_ref.shape[1]):
        rows = rows_ref[0, item]
        length = rows.shape[0] - 2 * reach
        current = jax.nn.gelu(
            tap_sum(rows, lambda k: first_ref[0, k], taps, length)
        ).astype(jnp.bfloat16)
        current = jnp.where(keeps[0], current, jnp.zeros((), jnp.bfloat16))
        for depth_index in range(layers):
            length = length - 2 * reach
            update = jax.nn.gelu(
                tap_sum(current, lambda k: hidden_ref[0, depth_index, k], taps, length)
            )
            current = (current[reach : reach + length].astype(jnp.float32) + update).astype(jnp.bfloat16)
            if depth_index + 1 < len(keeps):
                current = jnp.where(keeps[depth_index + 1], current, jnp.zeros((), jnp.bfloat16))
        out_ref[item] += jnp.dot(current, mix_ref[0], preferred_element_type=jnp.float32)


def conv_mix(extended, first_taps, hidden_taps, mix, rec_index, patches):
    types, recordings, span, width = extended.shape
    taps = first_taps.shape[1]
    reach = taps // 2
    layers = hidden_taps.shape[1]
    total = patches * lax.axis_size("rec")
    keeps = []
    for depth_index in range(layers):
        margin = reach * (layers - depth_index)
        length = span - 2 * reach * (depth_index + 1)
        spot = rec_index * patches - margin + jnp.arange(length, dtype=jnp.int32)
        keep = ((spot >= 0) & (spot < total)).astype(jnp.float32)
        keeps.append(jnp.broadcast_to(keep[:, None], (length, EMB)))
    mix_width = mix.shape[-1]
    flops = 2 * types * recordings * (span * width * EMB * taps + 2 * span * EMB * EMB * taps + patches * EMB * mix_width)
    return pl.pallas_call(
        conv_mix_kernel,
        grid=(types,),
        in_specs=[
            pl.BlockSpec((1, recordings, span, width), lambda m: (m, 0, 0, 0)),
            pl.BlockSpec((1,) + first_taps.shape[1:], lambda m: (m, 0, 0, 0)),
            pl.BlockSpec((1,) + hidden_taps.shape[1:], lambda m: (m, 0, 0, 0, 0)),
            pl.BlockSpec((1,) + mix.shape[1:], lambda m: (m, 0, 0)),
            pl.BlockSpec(keeps[0].shape, lambda m: (0, 0)),
            pl.BlockSpec(keeps[1].shape, lambda m: (0, 0)),
        ],
        out_specs=pl.BlockSpec((recordings, patches, mix_width), lambda m: (0, 0, 0)),
        out_shape=jax.ShapeDtypeStruct((recordings, patches, mix_width), jnp.float32),
        compiler_params=pltpu.CompilerParams(dimension_semantics=("arbitrary",)),
        cost_estimate=pl.CostEstimate(
            flops=flops, transcendentals=types * recordings * span * EMB * (layers + 1),
            bytes_accessed=extended.size * 2 + first_taps.size * 2 + hidden_taps.size * 2 + mix.size * 2 + recordings * patches * mix_width * 4,
        ),
    )(extended, first_taps, hidden_taps, mix, keeps[0], keeps[1])


def local(
    signal,
    montage,
    channels,
    lengths,
    boundary,
    conv_in,
    conv_hid,
    mix_weight,
    norm_gain,
    emit_weight,
    trans_within,
    trans_between,
    initial,
):
    groups = lax.axis_size("rec")
    chan_index = lax.axis_index("chan")
    rec_index = lax.axis_index("rec")
    recordings = signal.shape[0]
    patches = signal.shape[2] // SAMP
    slot_ids = chan_index * groups + jnp.arange(groups, dtype=jnp.int32)
    live_slots = slot_ids[None, :] < channels[:, None]
    places = jnp.arange(groups, dtype=jnp.int32)
    pick = (montage[:, 0, None, :] == places[None, :, None]) & live_slots[:, None, :]
    rows = jnp.einsum(
        "bms,bst->mbt", pick.astype(jnp.bfloat16), signal, preferred_element_type=jnp.float32
    ).astype(jnp.bfloat16)
    patch_rows = rows.reshape(groups, recordings, patches, SAMP)
    first_taps = lax.all_gather(conv_in[:, 0], "rec", tiled=True)
    hidden_taps = lax.all_gather(conv_hid[:, 0], "rec", tiled=True)
    extended = halo_rows(patch_rows)
    partial_value = conv_mix(extended, first_taps, hidden_taps, mix_weight[:, 0], rec_index, patches)
    summed = lax.psum(partial_value, "chan")
    average = jnp.mean(summed, axis=-1, keepdims=True)
    centred = summed - average
    variance = jnp.mean(centred * centred, axis=-1, keepdims=True)
    activated = jax.nn.gelu(centred * lax.rsqrt(variance + EPSILON) * norm_gain)
    emission = jnp.einsum("bpo,os->bps", activated, emit_weight, precision=lax.Precision.HIGHEST)
    positions = rec_index * patches + jnp.arange(patches, dtype=jnp.int32)
    valid = positions[None, :] < lengths[:, None]
    cross = boundary == 1
    filtered, log_partition = crf_forward(
        emission, cross, valid, trans_within, trans_between, initial, rec_index
    )
    return (filtered, log_partition / lengths.astype(jnp.float32))


def solution(mesh):
    placed = (
        P(None, "chan", "rec"),
        P(None, "chan", None),
        P(),
        P(),
        P(None, "rec"),
        P("rec", "chan", None, None, None),
        P("rec", "chan", None, None, None, None),
        P(None, "chan", None, None),
        P(),
        P(),
        P(),
        P(),
        P(),
    )
    return jax.shard_map(
        local, mesh=mesh, in_specs=placed, out_specs=(P(None, None, "rec"), P()), check_vma=False
    )
```

```python
import functools

import jax
import jax.numpy as jnp
from jax import lax
from jax.experimental import pallas as pl
from jax.experimental.pallas import tpu as pltpu
from jax.sharding import PartitionSpec as P

SAMP = 200
EMB = 128
STATES = 5


EPSILON = 1e-05
NEGATIVE = -1e30


def log_sum_exp(values, along):
    peak_value = jnp.max(values, axis=along, keepdims=True)
    return jnp.squeeze(peak_value, along) + jnp.log(
        jnp.sum(jnp.exp(values - peak_value), axis=along)
    )


LANES = 128


def forward_step(state, matrices, extra):
    terms = [state[i : i + 1, :] + matrices[i] for i in range(len(matrices))]
    peak = functools.reduce(jnp.maximum, terms)
    total = functools.reduce(lambda x, y: x + y, [jnp.exp(t - peak) for t in terms])
    moved = peak + jnp.log(total)
    if extra is not None:
        moved = moved + extra
    top = jnp.max(moved, axis=0, keepdims=True)
    level = top + jnp.log(jnp.sum(jnp.exp(moved - top), axis=0, keepdims=True))
    return moved - level, level


def prefix_kernel(within_ref, between_ref, start_ref, emit_ref, cross_ref, valid_ref, prefix_ref, offset_ref):
    patches = emit_ref.shape[0]
    within = [within_ref[i] for i in range(STATES)]
    between = [between_ref[i] for i in range(STATES)]

    def body(p, carry):
        state, offset = carry
        crossing = cross_ref[p] > 0.5
        counted = valid_ref[p] > 0.5
        matrices = [jnp.where(crossing, between[i], within[i]) for i in range(STATES)]
        moved, level = forward_step(state, matrices, emit_ref[p])
        state = jnp.where(counted, moved, state)
        offset = offset + jnp.where(counted, level, 0.0)
        prefix_ref[p] = state
        offset_ref[p] = offset
        return state, offset

    lax.fori_loop(0, patches, body, (start_ref[...], jnp.zeros((1, LANES), jnp.float32)))


def chain_kernel(prior_ref, mats_ref, incoming_ref, total_ref):
    count = mats_ref.shape[0]

    def body(k, carry):
        state, total = carry
        incoming_ref[k] = state
        matrices = [mats_ref[k, j] for j in range(STATES)]
        moved, level = forward_step(state, matrices, None)
        return moved, total + level

    _, total = lax.fori_loop(0, count, body, (prior_ref[...], jnp.zeros((1, LANES), jnp.float32)))
    total_ref[...] = total


def lanes_padded(values):
    pad = [(0, 0)] * (values.ndim - 1) + [(0, LANES - values.shape[-1])]
    return jnp.pad(values, pad)


def crf_forward(emission, cross, valid, trans_within, trans_between, initial, rec_index):
    recordings, patches, _ = emission.shape
    width = STATES * recordings
    emit_in = lanes_padded(jnp.tile(jnp.transpose(emission, (1, 2, 0)), (1, 1, STATES)))
    cross_in = lanes_padded(jnp.tile(cross.T.astype(jnp.float32), (1, STATES)))[:, None, :]
    valid_in = lanes_padded(jnp.tile(valid.T.astype(jnp.float32), (1, STATES)))[:, None, :]
    lane_start = jnp.arange(width, dtype=jnp.int32) // recordings
    basis = jnp.arange(STATES, dtype=jnp.int32)[:, None] == lane_start[None, :]
    start = lanes_padded(jnp.where(basis, 0.0, NEGATIVE).astype(jnp.float32))
    within_in = jnp.broadcast_to(trans_within[:, :, None], (STATES, STATES, LANES))
    between_in = jnp.broadcast_to(trans_between[:, :, None], (STATES, STATES, LANES))
    prefix, offset = pl.pallas_call(
        prefix_kernel,
        out_shape=(
            jax.ShapeDtypeStruct((patches, STATES, LANES), jnp.float32),
            jax.ShapeDtypeStruct((patches, 1, LANES), jnp.float32),
        ),
        cost_estimate=pl.CostEstimate(
            flops=patches * 80 * LANES * 8, transcendentals=patches * 8 * LANES * 8,
            bytes_accessed=patches * 14 * LANES * 4,
        ),
    )(within_in, between_in, start, emit_in, cross_in, valid_in)
    prefix_sj = prefix[:, :, :width].reshape(patches, STATES, STATES, recordings)
    offset_j = offset[:, 0, :width].reshape(patches, STATES, recordings)
    transfer = prefix_sj[patches - 1] + offset_j[patches - 1][None]
    transfer = jnp.transpose(transfer, (1, 0, 2))
    gathered = lax.all_gather(transfer, "rec")
    mats = lanes_padded(gathered)
    prior = initial - log_sum_exp(initial, 0)
    prior_in = lanes_padded(jnp.broadcast_to(prior[:, None], (STATES, recordings)))
    groups = gathered.shape[0]
    incoming, total = pl.pallas_call(
        chain_kernel,
        out_shape=(
            jax.ShapeDtypeStruct((groups, STATES, LANES), jnp.float32),
            jax.ShapeDtypeStruct((1, LANES), jnp.float32),
        ),
    )(prior_in, mats)
    here = lax.dynamic_index_in_dim(incoming, rec_index, 0, keepdims=False)[:, :recordings]
    weights = here[None, None] + offset_j[:, None] + prefix_sj
    reached = log_sum_exp(weights, 2)
    totals = log_sum_exp(reached, 1)
    filtered = jnp.transpose(reached - totals[:, None], (2, 1, 0))
    return filtered, total[0, :recordings]


def neighbour_shift(block, axis, distance):
    devices = range(lax.axis_size(axis))
    route = [(i - distance, i) for i in devices if i - distance in devices]
    return lax.ppermute(block, axis, route)


def halo_rows(patch_rows):
    patches = patch_rows.shape[2]
    halo = 6
    from_left = neighbour_shift(patch_rows[:, :, patches - halo :], "rec", 1)
    from_right = neighbour_shift(patch_rows[:, :, :halo], "rec", -1)
    return jnp.concatenate([from_left, patch_rows, from_right], axis=2)

def tap_sum(rows, weight_of, taps, length):
    accumulated = None
    for offset in range(taps):
        product = jnp.dot(rows, weight_of(offset), preferred_element_type=jnp.float32)
        product = product[offset : offset + length]
        accumulated = product if accumulated is None else accumulated + product
    return accumulated


def first_kernel(rows_ref, taps_ref, keep_ref, out_ref):
    taps = taps_ref.shape[1]
    keep = keep_ref[...] > 0.5
    for item in range(rows_ref.shape[1]):
        rows = rows_ref[0, item]
        length = rows.shape[0] - 2 * (taps // 2)
        value = jax.nn.gelu(tap_sum(rows, lambda k: taps_ref[0, k], taps, length)).astype(jnp.bfloat16)
        out_ref[0, item] = jnp.where(keep, value, jnp.zeros((), jnp.bfloat16))


def residual_layer(current, taps_ref, taps):
    reach = taps // 2
    length = current.shape[0] - 2 * reach
    update = jax.nn.gelu(tap_sum(current, lambda k: taps_ref[0, k], taps, length))
    return (current[reach : reach + length].astype(jnp.float32) + update).astype(jnp.bfloat16)


def hidden_kernel(rows_ref, taps_ref, keep_ref, out_ref):
    taps = taps_ref.shape[1]
    keep = keep_ref[...] > 0.5
    for item in range(rows_ref.shape[1]):
        value = residual_layer(rows_ref[0, item], taps_ref, taps)
        out_ref[0, item] = jnp.where(keep, value, jnp.zeros((), jnp.bfloat16))


def last_kernel(rows_ref, taps_ref, mix_ref, out_ref):
    @pl.when(pl.program_id(0) == 0)
    def _():
        out_ref[...] = jnp.zeros_like(out_ref)

    taps = taps_ref.shape[1]
    for item in range(rows_ref.shape[1]):
        value = residual_layer(rows_ref[0, item], taps_ref, taps)
        out_ref[item] += jnp.dot(value, mix_ref[0], preferred_element_type=jnp.float32)


def edge_keep(length, margin, rec_index, patches):
    total = patches * lax.axis_size("rec")
    spot = rec_index * patches - margin + jnp.arange(length, dtype=jnp.int32)
    keep = ((spot >= 0) & (spot < total)).astype(jnp.float32)
    return jnp.broadcast_to(keep[:, None], (length, EMB))


def per_type_call(kernel, rows, taps, side, out_block, out_shape, out_map, flops):
    types, recordings = rows.shape[:2]
    side_spec = (
        pl.BlockSpec((1,) + side.shape[1:], lambda m: (m, 0, 0))
        if side.ndim == 3 and side.shape[0] == types and kernel is last_kernel
        else pl.BlockSpec(side.shape, lambda m: (0, 0))
    )
    return pl.pallas_call(
        kernel,
        grid=(types,),
        in_specs=[
            pl.BlockSpec((1,) + rows.shape[1:], lambda m: (m, 0, 0, 0)),
            pl.BlockSpec((1,) + taps.shape[1:], lambda m: (m, 0, 0, 0)),
            side_spec,
        ],
        out_specs=pl.BlockSpec(out_block, out_map),
        out_shape=out_shape,
        compiler_params=pltpu.CompilerParams(dimension_semantics=("arbitrary",)),
        cost_estimate=pl.CostEstimate(
            flops=flops, transcendentals=rows.shape[0] * rows.shape[1] * rows.shape[2] * EMB,
            bytes_accessed=rows.size * 2 + taps.size * 2 + side.size * 2 + out_shape.size * 4,
        ),
    )(rows, taps, side)


def conv_mix(extended, first_taps, hidden_list, mix, rec_index, patches):
    types, recordings, span, width = extended.shape
    taps = first_taps.shape[1]
    reach = taps // 2
    layers = len(hidden_list)
    length = span - 2 * reach
    margin = reach * layers
    current = per_type_call(
        first_kernel, extended, first_taps, edge_keep(length, margin, rec_index, patches),
        (1, recordings, length, EMB), jax.ShapeDtypeStruct((types, recordings, length, EMB), jnp.bfloat16),
        lambda m: (m, 0, 0, 0), 2 * types * recordings * span * width * EMB * taps,
    )
    for depth_index in range(layers - 1):
        length = length - 2 * reach
        margin = margin - reach
        current = per_type_call(
            hidden_kernel, current, hidden_list[depth_index], edge_keep(length, margin, rec_index, patches),
            (1, recordings, length, EMB), jax.ShapeDtypeStruct((types, recordings, length, EMB), jnp.bfloat16),
            lambda m: (m, 0, 0, 0), 2 * types * recordings * span * EMB * EMB * taps,
        )
    mix_width = mix.shape[-1]
    return per_type_call(
        last_kernel, current, hidden_list[layers - 1], mix,
        (recordings, patches, mix_width), jax.ShapeDtypeStruct((recordings, patches, mix_width), jnp.float32),
        lambda m: (0, 0, 0), 2 * types * recordings * span * EMB * (EMB * taps + mix_width),
    )


def local(
    signal,
    montage,
    channels,
    lengths,
    boundary,
    conv_in,
    conv_hid,
    mix_weight,
    norm_gain,
    emit_weight,
    trans_within,
    trans_between,
    initial,
):
    groups = lax.axis_size("rec")
    chan_index = lax.axis_index("chan")
    rec_index = lax.axis_index("rec")
    recordings = signal.shape[0]
    patches = signal.shape[2] // SAMP
    slot_ids = chan_index * groups + jnp.arange(groups, dtype=jnp.int32)
    live_slots = slot_ids[None, :] < channels[:, None]
    places = jnp.arange(groups, dtype=jnp.int32)
    pick = (montage[:, 0, None, :] == places[None, :, None]) & live_slots[:, None, :]
    rows = jnp.einsum(
        "bms,bst->mbt", pick.astype(jnp.bfloat16), signal, preferred_element_type=jnp.float32
    ).astype(jnp.bfloat16)
    patch_rows = rows.reshape(groups, recordings, patches, SAMP)
    first_taps = lax.all_gather(conv_in[:, 0], "rec", tiled=True)
    hidden_list = [
        lax.all_gather(conv_hid[:, 0, depth_index], "rec", tiled=True)
        for depth_index in range(conv_hid.shape[2])
    ]
    extended = halo_rows(patch_rows)
    partial_value = conv_mix(extended, first_taps, hidden_list, mix_weight[:, 0], rec_index, patches)
    summed = lax.psum(partial_value, "chan")
    average = jnp.mean(summed, axis=-1, keepdims=True)
    centred = summed - average
    variance = jnp.mean(centred * centred, axis=-1, keepdims=True)
    activated = jax.nn.gelu(centred * lax.rsqrt(variance + EPSILON) * norm_gain)
    emission = jnp.einsum("bpo,os->bps", activated, emit_weight, precision=lax.Precision.HIGHEST)
    positions = rec_index * patches + jnp.arange(patches, dtype=jnp.int32)
    valid = positions[None, :] < lengths[:, None]
    cross = boundary == 1
    filtered, log_partition = crf_forward(
        emission, cross, valid, trans_within, trans_between, initial, rec_index
    )
    return (filtered, log_partition / lengths.astype(jnp.float32))


def solution(mesh):
    placed = (
        P(None, "chan", "rec"),
        P(None, "chan", None),
        P(),
        P(),
        P(None, "rec"),
        P("rec", "chan", None, None, None),
        P("rec", "chan", None, None, None, None),
        P(None, "chan", None, None),
        P(),
        P(),
        P(),
        P(),
        P(),
    )
    return jax.shard_map(
        local, mesh=mesh, in_specs=placed, out_specs=(P(None, None, "rec"), P()), check_vma=False
    )
```

```python
import functools

import jax
import jax.numpy as jnp
from jax import lax
from jax.experimental import pallas as pl
from jax.experimental.pallas import tpu as pltpu
from jax.sharding import PartitionSpec as P

SAMP = 200
EMB = 128
STATES = 5


EPSILON = 1e-05
NEGATIVE = -1e30


def log_sum_exp(values, along):
    peak_value = jnp.max(values, axis=along, keepdims=True)
    return jnp.squeeze(peak_value, along) + jnp.log(
        jnp.sum(jnp.exp(values - peak_value), axis=along)
    )


LANES = 128


def forward_step(state, matrices, extra):
    terms = [state[i : i + 1, :] + matrices[i] for i in range(len(matrices))]
    peak = functools.reduce(jnp.maximum, terms)
    total = functools.reduce(lambda x, y: x + y, [jnp.exp(t - peak) for t in terms])
    moved = peak + jnp.log(total)
    if extra is not None:
        moved = moved + extra
    top = jnp.max(moved, axis=0, keepdims=True)
    level = top + jnp.log(jnp.sum(jnp.exp(moved - top), axis=0, keepdims=True))
    return moved - level, level


def prefix_kernel(within_ref, between_ref, start_ref, emit_ref, cross_ref, valid_ref, prefix_ref, offset_ref):
    patches = emit_ref.shape[0]
    within = [within_ref[i] for i in range(STATES)]
    between = [between_ref[i] for i in range(STATES)]

    def body(p, carry):
        state, offset = carry
        crossing = cross_ref[p] > 0.5
        counted = valid_ref[p] > 0.5
        matrices = [jnp.where(crossing, between[i], within[i]) for i in range(STATES)]
        moved, level = forward_step(state, matrices, emit_ref[p])
        state = jnp.where(counted, moved, state)
        offset = offset + jnp.where(counted, level, 0.0)
        prefix_ref[p] = state
        offset_ref[p] = offset
        return state, offset

    lax.fori_loop(0, patches, body, (start_ref[...], jnp.zeros((1, LANES), jnp.float32)))


def chain_kernel(prior_ref, mats_ref, incoming_ref, total_ref):
    count = mats_ref.shape[0]

    def body(k, carry):
        state, total = carry
        incoming_ref[k] = state
        matrices = [mats_ref[k, j] for j in range(STATES)]
        moved, level = forward_step(state, matrices, None)
        return moved, total + level

    _, total = lax.fori_loop(0, count, body, (prior_ref[...], jnp.zeros((1, LANES), jnp.float32)))
    total_ref[...] = total


def lanes_padded(values):
    pad = [(0, 0)] * (values.ndim - 1) + [(0, LANES - values.shape[-1])]
    return jnp.pad(values, pad)


def crf_forward(emission, cross, valid, trans_within, trans_between, initial, rec_index):
    recordings, patches, _ = emission.shape
    width = STATES * recordings
    emit_in = lanes_padded(jnp.tile(jnp.transpose(emission, (1, 2, 0)), (1, 1, STATES)))
    cross_in = lanes_padded(jnp.tile(cross.T.astype(jnp.float32), (1, STATES)))[:, None, :]
    valid_in = lanes_padded(jnp.tile(valid.T.astype(jnp.float32), (1, STATES)))[:, None, :]
    lane_start = jnp.arange(width, dtype=jnp.int32) // recordings
    basis = jnp.arange(STATES, dtype=jnp.int32)[:, None] == lane_start[None, :]
    start = lanes_padded(jnp.where(basis, 0.0, NEGATIVE).astype(jnp.float32))
    within_in = jnp.broadcast_to(trans_within[:, :, None], (STATES, STATES, LANES))
    between_in = jnp.broadcast_to(trans_between[:, :, None], (STATES, STATES, LANES))
    prefix, offset = pl.pallas_call(
        prefix_kernel,
        out_shape=(
            jax.ShapeDtypeStruct((patches, STATES, LANES), jnp.float32),
            jax.ShapeDtypeStruct((patches, 1, LANES), jnp.float32),
        ),
        cost_estimate=pl.CostEstimate(
            flops=patches * 80 * LANES * 8, transcendentals=patches * 8 * LANES * 8,
            bytes_accessed=patches * 14 * LANES * 4,
        ),
    )(within_in, between_in, start, emit_in, cross_in, valid_in)
    prefix_sj = prefix[:, :, :width].reshape(patches, STATES, STATES, recordings)
    offset_j = offset[:, 0, :width].reshape(patches, STATES, recordings)
    transfer = prefix_sj[patches - 1] + offset_j[patches - 1][None]
    transfer = jnp.transpose(transfer, (1, 0, 2))
    gathered = lax.all_gather(transfer, "rec")
    mats = lanes_padded(gathered)
    prior = initial - log_sum_exp(initial, 0)
    prior_in = lanes_padded(jnp.broadcast_to(prior[:, None], (STATES, recordings)))
    groups = gathered.shape[0]
    incoming, total = pl.pallas_call(
        chain_kernel,
        out_shape=(
            jax.ShapeDtypeStruct((groups, STATES, LANES), jnp.float32),
            jax.ShapeDtypeStruct((1, LANES), jnp.float32),
        ),
    )(prior_in, mats)
    here = lax.dynamic_index_in_dim(incoming, rec_index, 0, keepdims=False)[:, :recordings]
    weights = here[None, None] + offset_j[:, None] + prefix_sj
    reached = log_sum_exp(weights, 2)
    totals = log_sum_exp(reached, 1)
    filtered = jnp.transpose(reached - totals[:, None], (2, 1, 0))
    return filtered, total[0, :recordings]


def neighbour_shift(block, axis, distance):
    devices = range(lax.axis_size(axis))
    route = [(i - distance, i) for i in devices if i - distance in devices]
    return lax.ppermute(block, axis, route)


def halo_rows(patch_rows):
    patches = patch_rows.shape[2]
    halo = 6
    from_left = neighbour_shift(patch_rows[:, :, patches - halo :], "rec", 1)
    from_right = neighbour_shift(patch_rows[:, :, :halo], "rec", -1)
    return jnp.concatenate([from_left, patch_rows, from_right], axis=2)

def tap_sum(rows, weight_of, taps, length):
    accumulated = None
    for offset in range(taps):
        product = jnp.dot(rows, weight_of(offset), preferred_element_type=jnp.float32)
        product = product[offset : offset + length]
        accumulated = product if accumulated is None else accumulated + product
    return accumulated


def first_kernel(rows_ref, taps_ref, keep_ref, out_ref):
    taps = taps_ref.shape[1]
    keep = keep_ref[...] > 0.5
    for item in range(rows_ref.shape[1]):
        rows = rows_ref[0, item]
        length = rows.shape[0] - 2 * (taps // 2)
        value = jax.nn.gelu(tap_sum(rows, lambda k: taps_ref[0, k], taps, length)).astype(jnp.bfloat16)
        out_ref[0, item] = jnp.where(keep, value, jnp.zeros((), jnp.bfloat16))


def residual_layer(current, taps_ref, taps):
    reach = taps // 2
    length = current.shape[0] - 2 * reach
    update = jax.nn.gelu(tap_sum(current, lambda k: taps_ref[0, k], taps, length))
    return (current[reach : reach + length].astype(jnp.float32) + update).astype(jnp.bfloat16)


def hidden_kernel(rows_ref, taps_ref, keep_ref, out_ref):
    taps = taps_ref.shape[1]
    keep = keep_ref[...] > 0.5
    for item in range(rows_ref.shape[1]):
        value = residual_layer(rows_ref[0, item], taps_ref, taps)
        out_ref[0, item] = jnp.where(keep, value, jnp.zeros((), jnp.bfloat16))


def last_kernel(rows_ref, taps_ref, mix_ref, out_ref):
    @pl.when(pl.program_id(0) == 0)
    def _():
        out_ref[...] = jnp.zeros_like(out_ref)

    taps = taps_ref.shape[1]
    for item in range(rows_ref.shape[1]):
        value = residual_layer(rows_ref[0, item], taps_ref, taps)
        out_ref[item] += jnp.dot(value, mix_ref[0], preferred_element_type=jnp.float32)


def edge_keep(length, margin, rec_index, patches):
    total = patches * lax.axis_size("rec")
    spot = rec_index * patches - margin + jnp.arange(length, dtype=jnp.int32)
    keep = ((spot >= 0) & (spot < total)).astype(jnp.float32)
    return jnp.broadcast_to(keep[:, None], (length, EMB))


def per_type_call(kernel, rows, taps, side, out_block, out_shape, out_map, flops):
    types, recordings = rows.shape[:2]
    side_spec = (
        pl.BlockSpec((1,) + side.shape[1:], lambda m: (m, 0, 0))
        if side.ndim == 3 and side.shape[0] == types and kernel is last_kernel
        else pl.BlockSpec(side.shape, lambda m: (0, 0))
    )
    return pl.pallas_call(
        kernel,
        grid=(types,),
        in_specs=[
            pl.BlockSpec((1,) + rows.shape[1:], lambda m: (m, 0, 0, 0)),
            pl.BlockSpec((1,) + taps.shape[1:], lambda m: (m, 0, 0, 0)),
            side_spec,
        ],
        out_specs=pl.BlockSpec(out_block, out_map),
        out_shape=out_shape,
        compiler_params=pltpu.CompilerParams(dimension_semantics=("arbitrary",)),
        cost_estimate=pl.CostEstimate(
            flops=flops, transcendentals=rows.shape[0] * rows.shape[1] * rows.shape[2] * EMB,
            bytes_accessed=rows.size * 2 + taps.size * 2 + side.size * 2 + out_shape.size * 4,
        ),
    )(rows, taps, side)


def conv_mix(extended, first_taps, hidden_list, mix, rec_index, patches):
    types, recordings, span, width = extended.shape
    taps = first_taps.shape[1]
    reach = taps // 2
    layers = len(hidden_list)
    length = span - 2 * reach
    margin = reach * layers
    current = per_type_call(
        first_kernel, extended, first_taps, edge_keep(length, margin, rec_index, patches),
        (1, recordings, length, EMB), jax.ShapeDtypeStruct((types, recordings, length, EMB), jnp.bfloat16),
        lambda m: (m, 0, 0, 0), 2 * types * recordings * span * width * EMB * taps,
    )
    for depth_index in range(layers - 1):
        length = length - 2 * reach
        margin = margin - reach
        current = per_type_call(
            hidden_kernel, current, hidden_list[depth_index], edge_keep(length, margin, rec_index, patches),
            (1, recordings, length, EMB), jax.ShapeDtypeStruct((types, recordings, length, EMB), jnp.bfloat16),
            lambda m: (m, 0, 0, 0), 2 * types * recordings * span * EMB * EMB * taps,
        )
    mix_width = mix.shape[-1]
    return per_type_call(
        last_kernel, current, hidden_list[layers - 1], mix,
        (recordings, patches, mix_width), jax.ShapeDtypeStruct((recordings, patches, mix_width), jnp.float32),
        lambda m: (0, 0, 0), 2 * types * recordings * span * EMB * (EMB * taps + mix_width),
    )


def local(
    signal,
    montage,
    channels,
    lengths,
    boundary,
    conv_in,
    conv_hid,
    mix_weight,
    norm_gain,
    emit_weight,
    trans_within,
    trans_between,
    initial,
):
    groups = lax.axis_size("rec")
    chan_index = lax.axis_index("chan")
    rec_index = lax.axis_index("rec")
    recordings = signal.shape[0]
    patches = signal.shape[2] // SAMP
    slot_ids = chan_index * groups + jnp.arange(groups, dtype=jnp.int32)
    live_slots = slot_ids[None, :] < channels[:, None]
    places = jnp.arange(groups, dtype=jnp.int32)
    pick = (montage[:, 0, None, :] == places[None, :, None]) & live_slots[:, None, :]
    rows = jnp.einsum(
        "bms,bst->mbt", pick.astype(jnp.bfloat16), signal, preferred_element_type=jnp.float32
    ).astype(jnp.bfloat16)
    patch_rows = rows.reshape(groups, recordings, patches, SAMP)
    first_taps = lax.all_gather(conv_in[:, 0], "rec", tiled=True)
    hidden_taps = lax.all_gather(jnp.swapaxes(conv_hid[:, 0], 0, 1), "rec", axis=1, tiled=True)
    hidden_list = [hidden_taps[depth_index] for depth_index in range(hidden_taps.shape[0])]
    extended = halo_rows(patch_rows)
    partial_value = conv_mix(extended, first_taps, hidden_list, mix_weight[:, 0], rec_index, patches)
    summed = lax.psum(partial_value, "chan")
    average = jnp.mean(summed, axis=-1, keepdims=True)
    centred = summed - average
    variance = jnp.mean(centred * centred, axis=-1, keepdims=True)
    activated = jax.nn.gelu(centred * lax.rsqrt(variance + EPSILON) * norm_gain)
    emission = jnp.einsum("bpo,os->bps", activated, emit_weight, precision=lax.Precision.HIGHEST)
    positions = rec_index * patches + jnp.arange(patches, dtype=jnp.int32)
    valid = positions[None, :] < lengths[:, None]
    cross = boundary == 1
    filtered, log_partition = crf_forward(
        emission, cross, valid, trans_within, trans_between, initial, rec_index
    )
    return (filtered, log_partition / lengths.astype(jnp.float32))


def solution(mesh):
    placed = (
        P(None, "chan", "rec"),
        P(None, "chan", None),
        P(),
        P(),
        P(None, "rec"),
        P("rec", "chan", None, None, None),
        P("rec", "chan", None, None, None, None),
        P(None, "chan", None, None),
        P(),
        P(),
        P(),
        P(),
        P(),
    )
    return jax.shard_map(
        local, mesh=mesh, in_specs=placed, out_specs=(P(None, None, "rec"), P()), check_vma=False
    )
```

```python
import functools

import jax
import jax.numpy as jnp
from jax import lax
from jax.experimental import pallas as pl
from jax.experimental.pallas import tpu as pltpu
from jax.sharding import PartitionSpec as P

SAMP = 200
EMB = 128
STATES = 5


EPSILON = 1e-05
NEGATIVE = -1e30
MESH_SIDE = 4


def log_sum_exp(values, along):
    peak_value = jnp.max(values, axis=along, keepdims=True)
    return jnp.squeeze(peak_value, along) + jnp.log(
        jnp.sum(jnp.exp(values - peak_value), axis=along)
    )


LANES = 128


def forward_step(state, matrices, extra):
    terms = [state[i : i + 1, :] + matrices[i] for i in range(len(matrices))]
    peak = functools.reduce(jnp.maximum, terms)
    total = functools.reduce(lambda x, y: x + y, [jnp.exp(t - peak) for t in terms])
    moved = peak + jnp.log(total)
    if extra is not None:
        moved = moved + extra
    top = jnp.max(moved, axis=0, keepdims=True)
    level = top + jnp.log(jnp.sum(jnp.exp(moved - top), axis=0, keepdims=True))
    return moved - level, level


def prefix_kernel(within_ref, between_ref, start_ref, emit_ref, cross_ref, valid_ref, prefix_ref, offset_ref):
    patches = emit_ref.shape[0]
    within = [within_ref[i] for i in range(STATES)]
    between = [between_ref[i] for i in range(STATES)]

    def body(p, carry):
        state, offset = carry
        crossing = cross_ref[p] > 0.5
        counted = valid_ref[p] > 0.5
        matrices = [jnp.where(crossing, between[i], within[i]) for i in range(STATES)]
        moved, level = forward_step(state, matrices, emit_ref[p])
        state = jnp.where(counted, moved, state)
        offset = offset + jnp.where(counted, level, 0.0)
        prefix_ref[p] = state
        offset_ref[p] = offset
        return state, offset

    lax.fori_loop(0, patches, body, (start_ref[...], jnp.zeros((1, LANES), jnp.float32)))


def chain_kernel(prior_ref, mats_ref, incoming_ref, total_ref):
    count = mats_ref.shape[0]

    def body(k, carry):
        state, total = carry
        incoming_ref[k] = state
        matrices = [mats_ref[k, j] for j in range(STATES)]
        moved, level = forward_step(state, matrices, None)
        return moved, total + level

    _, total = lax.fori_loop(0, count, body, (prior_ref[...], jnp.zeros((1, LANES), jnp.float32)))
    total_ref[...] = total


def lanes_padded(values):
    pad = [(0, 0)] * (values.ndim - 1) + [(0, LANES - values.shape[-1])]
    return jnp.pad(values, pad)


def crf_forward(emission, cross, valid, trans_within, trans_between, initial, rec_index):
    recordings, patches, _ = emission.shape
    width = STATES * recordings
    emit_in = lanes_padded(jnp.tile(jnp.transpose(emission, (1, 2, 0)), (1, 1, STATES)))
    cross_in = lanes_padded(jnp.tile(cross.T.astype(jnp.float32), (1, STATES)))[:, None, :]
    valid_in = lanes_padded(jnp.tile(valid.T.astype(jnp.float32), (1, STATES)))[:, None, :]
    lane_start = jnp.arange(width, dtype=jnp.int32) // recordings
    basis = jnp.arange(STATES, dtype=jnp.int32)[:, None] == lane_start[None, :]
    start = lanes_padded(jnp.where(basis, 0.0, NEGATIVE).astype(jnp.float32))
    within_in = jnp.broadcast_to(trans_within[:, :, None], (STATES, STATES, LANES))
    between_in = jnp.broadcast_to(trans_between[:, :, None], (STATES, STATES, LANES))
    prefix, offset = pl.pallas_call(
        prefix_kernel,
        out_shape=(
            jax.ShapeDtypeStruct((patches, STATES, LANES), jnp.float32),
            jax.ShapeDtypeStruct((patches, 1, LANES), jnp.float32),
        ),
        cost_estimate=pl.CostEstimate(
            flops=patches * 80 * LANES * 8, transcendentals=patches * 8 * LANES * 8,
            bytes_accessed=patches * 14 * LANES * 4,
        ),
    )(within_in, between_in, start, emit_in, cross_in, valid_in)
    prefix_sj = prefix[:, :, :width].reshape(patches, STATES, STATES, recordings)
    offset_j = offset[:, 0, :width].reshape(patches, STATES, recordings)
    transfer = prefix_sj[patches - 1] + offset_j[patches - 1][None]
    transfer = jnp.transpose(transfer, (1, 0, 2))
    gathered = lax.all_gather(transfer, "rec")
    mats = lanes_padded(gathered)
    prior = initial - log_sum_exp(initial, 0)
    prior_in = lanes_padded(jnp.broadcast_to(prior[:, None], (STATES, recordings)))
    groups = gathered.shape[0]
    incoming, total = pl.pallas_call(
        chain_kernel,
        out_shape=(
            jax.ShapeDtypeStruct((groups, STATES, LANES), jnp.float32),
            jax.ShapeDtypeStruct((1, LANES), jnp.float32),
        ),
    )(prior_in, mats)
    here = lax.dynamic_index_in_dim(incoming, rec_index, 0, keepdims=False)[:, :recordings]
    weights = here[None, None] + offset_j[:, None] + prefix_sj
    reached = log_sum_exp(weights, 2)
    totals = log_sum_exp(reached, 1)
    filtered = jnp.transpose(reached - totals[:, None], (2, 1, 0))
    return filtered, total[0, :recordings]


def neighbour_shift(block, axis, distance):
    devices = range(lax.axis_size(axis))
    route = [(i - distance, i) for i in devices if i - distance in devices]
    return lax.ppermute(block, axis, route)


def halo_rows(patch_rows):
    patches = patch_rows.shape[2]
    halo = 6
    from_left = neighbour_shift(patch_rows[:, :, patches - halo :], "rec", 1)
    from_right = neighbour_shift(patch_rows[:, :, :halo], "rec", -1)
    return jnp.concatenate([from_left, patch_rows, from_right], axis=2)

def tap_sum(rows, weight_of, taps, length):
    accumulated = None
    for offset in range(taps):
        product = jnp.dot(rows, weight_of(offset), preferred_element_type=jnp.float32)
        product = product[offset : offset + length]
        accumulated = product if accumulated is None else accumulated + product
    return accumulated


def first_kernel(rows_ref, taps_ref, keep_ref, out_ref):
    taps = taps_ref.shape[1]
    keep = keep_ref[...] > 0.5
    for item in range(rows_ref.shape[1]):
        rows = rows_ref[0, item]
        length = rows.shape[0] - 2 * (taps // 2)
        value = jax.nn.gelu(tap_sum(rows, lambda k: taps_ref[0, k], taps, length)).astype(jnp.bfloat16)
        out_ref[0, item] = jnp.where(keep, value, jnp.zeros((), jnp.bfloat16))


def residual_layer(current, taps_ref, taps):
    reach = taps // 2
    length = current.shape[0] - 2 * reach
    update = jax.nn.gelu(tap_sum(current, lambda k: taps_ref[0, 0, k], taps, length))
    return (current[reach : reach + length].astype(jnp.float32) + update).astype(jnp.bfloat16)


def hidden_kernel(rows_ref, taps_ref, keep_ref, out_ref):
    taps = taps_ref.shape[2]
    keep = keep_ref[...] > 0.5
    for item in range(rows_ref.shape[1]):
        value = residual_layer(rows_ref[0, item], taps_ref, taps)
        out_ref[0, item] = jnp.where(keep, value, jnp.zeros((), jnp.bfloat16))


def last_kernel(rows_ref, taps_ref, mix_ref, out_ref):
    @pl.when(pl.program_id(0) == 0)
    def _():
        out_ref[...] = jnp.zeros_like(out_ref)

    taps = taps_ref.shape[2]
    for item in range(rows_ref.shape[1]):
        value = residual_layer(rows_ref[0, item], taps_ref, taps)
        out_ref[item] += jnp.dot(value, mix_ref[0], preferred_element_type=jnp.float32)


def edge_keep(length, margin, rec_index, patches):
    total = patches * lax.axis_size("rec")
    spot = rec_index * patches - margin + jnp.arange(length, dtype=jnp.int32)
    keep = ((spot >= 0) & (spot < total)).astype(jnp.float32)
    return jnp.broadcast_to(keep[:, None], (length, EMB))


def per_type_call(kernel, rows, taps, side, out_block, out_shape, out_map, flops, layer=None):
    types, recordings = rows.shape[:2]
    side_spec = (
        pl.BlockSpec((1,) + side.shape[1:], lambda m: (m, 0, 0))
        if side.ndim == 3 and side.shape[0] == types and kernel is last_kernel
        else pl.BlockSpec(side.shape, lambda m: (0, 0))
    )
    return pl.pallas_call(
        kernel,
        grid=(types,),
        in_specs=[
            pl.BlockSpec((1,) + rows.shape[1:], lambda m: (m, 0, 0, 0)),
            pl.BlockSpec((1,) + taps.shape[1:], lambda m: (m, 0, 0, 0))
            if layer is None
            else pl.BlockSpec((1, 1) + taps.shape[2:], lambda m: (m, layer, 0, 0, 0)),
            side_spec,
        ],
        out_specs=pl.BlockSpec(out_block, out_map),
        out_shape=out_shape,
        compiler_params=pltpu.CompilerParams(dimension_semantics=("arbitrary",)),
        cost_estimate=pl.CostEstimate(
            flops=flops, transcendentals=rows.shape[0] * rows.shape[1] * rows.shape[2] * EMB,
            bytes_accessed=rows.size * 2 + taps.size * 2 // (1 if layer is None else taps.shape[1]) + side.size * 2 + out_shape.size * 4,
        ),
    )(rows, taps, side)


def conv_mix(extended, first_taps, hidden_taps, mix, rec_index, patches):
    types, recordings, span, width = extended.shape
    taps = first_taps.shape[1]
    reach = taps // 2
    layers = hidden_taps.shape[1]
    length = span - 2 * reach
    margin = reach * layers
    current = per_type_call(
        first_kernel, extended, first_taps, edge_keep(length, margin, rec_index, patches),
        (1, recordings, length, EMB), jax.ShapeDtypeStruct((types, recordings, length, EMB), jnp.bfloat16),
        lambda m: (m, 0, 0, 0), 2 * types * recordings * span * width * EMB * taps,
    )
    for depth_index in range(layers - 1):
        length = length - 2 * reach
        margin = margin - reach
        current = per_type_call(
            hidden_kernel, current, hidden_taps, edge_keep(length, margin, rec_index, patches),
            (1, recordings, length, EMB), jax.ShapeDtypeStruct((types, recordings, length, EMB), jnp.bfloat16),
            lambda m: (m, 0, 0, 0), 2 * types * recordings * span * EMB * EMB * taps, depth_index,
        )
    mix_width = mix.shape[-1]
    return per_type_call(
        last_kernel, current, hidden_taps, mix,
        (recordings, patches, mix_width), jax.ShapeDtypeStruct((recordings, patches, mix_width), jnp.float32),
        lambda m: (0, 0, 0), 2 * types * recordings * span * EMB * (EMB * taps + mix_width), layers - 1,
    )


def torus_gather(block, rec_index, side):
    inner = rec_index % side
    outer = rec_index // side
    devices = side * side

    def shifted(values, step, stride):
        route = []
        for source in range(devices):
            row, col = source // side, source % side
            if stride == 1:
                target = row * side + (col + step) % side
            else:
                target = ((row + step) % side) * side + col
            route.append((source, target))
        return lax.ppermute(values, "rec", route)

    along = jnp.concatenate([block] + [shifted(block, step, 1) for step in range(1, side)], axis=0)
    whole = jnp.concatenate([along] + [shifted(along, step, side) for step in range(1, side)], axis=0)
    types = jnp.arange(devices, dtype=jnp.int32)
    position = ((outer - types // side) % side) * side + (inner - types % side) % side
    return jnp.take(whole, position, axis=0)


def local(
    signal,
    montage,
    channels,
    lengths,
    boundary,
    conv_in,
    conv_hid,
    mix_weight,
    norm_gain,
    emit_weight,
    trans_within,
    trans_between,
    initial,
):
    groups = lax.axis_size("rec")
    mesh_side = MESH_SIDE
    chan_index = lax.axis_index("chan")
    rec_index = lax.axis_index("rec")
    recordings = signal.shape[0]
    patches = signal.shape[2] // SAMP
    slot_ids = chan_index * groups + jnp.arange(groups, dtype=jnp.int32)
    live_slots = slot_ids[None, :] < channels[:, None]
    places = jnp.arange(groups, dtype=jnp.int32)
    pick = (montage[:, 0, None, :] == places[None, :, None]) & live_slots[:, None, :]
    rows = jnp.einsum(
        "bms,bst->mbt", pick.astype(jnp.bfloat16), signal, preferred_element_type=jnp.float32
    ).astype(jnp.bfloat16)
    patch_rows = rows.reshape(groups, recordings, patches, SAMP)
    first_taps = lax.all_gather(conv_in[:, 0], "rec", tiled=True)
    hidden_taps = torus_gather(conv_hid[:, 0], rec_index, mesh_side)
    extended = halo_rows(patch_rows)
    partial_value = conv_mix(extended, first_taps, hidden_taps, mix_weight[:, 0], rec_index, patches)
    summed = lax.psum(partial_value, "chan")
    average = jnp.mean(summed, axis=-1, keepdims=True)
    centred = summed - average
    variance = jnp.mean(centred * centred, axis=-1, keepdims=True)
    activated = jax.nn.gelu(centred * lax.rsqrt(variance + EPSILON) * norm_gain)
    emission = jnp.einsum("bpo,os->bps", activated, emit_weight, precision=lax.Precision.HIGHEST)
    positions = rec_index * patches + jnp.arange(patches, dtype=jnp.int32)
    valid = positions[None, :] < lengths[:, None]
    cross = boundary == 1
    filtered, log_partition = crf_forward(
        emission, cross, valid, trans_within, trans_between, initial, rec_index
    )
    return (filtered, log_partition / lengths.astype(jnp.float32))


def solution(mesh):
    placed = (
        P(None, "chan", "rec"),
        P(None, "chan", None),
        P(),
        P(),
        P(None, "rec"),
        P("rec", "chan", None, None, None),
        P("rec", "chan", None, None, None, None),
        P(None, "chan", None, None),
        P(),
        P(),
        P(),
        P(),
        P(),
    )
    return jax.shard_map(
        local, mesh=mesh, in_specs=placed, out_specs=(P(None, None, "rec"), P()), check_vma=False
    )
```

```python
import functools

import jax
import jax.numpy as jnp
from jax import lax
from jax.experimental import pallas as pl
from jax.experimental.pallas import tpu as pltpu
from jax.sharding import PartitionSpec as P

SAMP = 200
EMB = 128
STATES = 5


EPSILON = 1e-05
NEGATIVE = -1e30


def log_sum_exp(values, along):
    peak_value = jnp.max(values, axis=along, keepdims=True)
    return jnp.squeeze(peak_value, along) + jnp.log(
        jnp.sum(jnp.exp(values - peak_value), axis=along)
    )


LANES = 128


def forward_step(state, matrices, extra):
    terms = [state[i : i + 1, :] + matrices[i] for i in range(len(matrices))]
    peak = functools.reduce(jnp.maximum, terms)
    total = functools.reduce(lambda x, y: x + y, [jnp.exp(t - peak) for t in terms])
    moved = peak + jnp.log(total)
    if extra is not None:
        moved = moved + extra
    top = jnp.max(moved, axis=0, keepdims=True)
    level = top + jnp.log(jnp.sum(jnp.exp(moved - top), axis=0, keepdims=True))
    return moved - level, level


def prefix_kernel(within_ref, between_ref, start_ref, emit_ref, cross_ref, valid_ref, prefix_ref, offset_ref):
    patches = emit_ref.shape[0]
    within = [within_ref[i] for i in range(STATES)]
    between = [between_ref[i] for i in range(STATES)]

    def body(p, carry):
        state, offset = carry
        crossing = cross_ref[p] > 0.5
        counted = valid_ref[p] > 0.5
        matrices = [jnp.where(crossing, between[i], within[i]) for i in range(STATES)]
        moved, level = forward_step(state, matrices, emit_ref[p])
        state = jnp.where(counted, moved, state)
        offset = offset + jnp.where(counted, level, 0.0)
        prefix_ref[p] = state
        offset_ref[p] = offset
        return state, offset

    lax.fori_loop(0, patches, body, (start_ref[...], jnp.zeros((1, LANES), jnp.float32)))


def chain_kernel(prior_ref, mats_ref, incoming_ref, total_ref):
    count = mats_ref.shape[0]

    def body(k, carry):
        state, total = carry
        incoming_ref[k] = state
        matrices = [mats_ref[k, j] for j in range(STATES)]
        moved, level = forward_step(state, matrices, None)
        return moved, total + level

    _, total = lax.fori_loop(0, count, body, (prior_ref[...], jnp.zeros((1, LANES), jnp.float32)))
    total_ref[...] = total


def lanes_padded(values):
    pad = [(0, 0)] * (values.ndim - 1) + [(0, LANES - values.shape[-1])]
    return jnp.pad(values, pad)


def crf_forward(emission, cross, valid, trans_within, trans_between, initial, rec_index):
    recordings, patches, _ = emission.shape
    width = STATES * recordings
    emit_in = lanes_padded(jnp.tile(jnp.transpose(emission, (1, 2, 0)), (1, 1, STATES)))
    cross_in = lanes_padded(jnp.tile(cross.T.astype(jnp.float32), (1, STATES)))[:, None, :]
    valid_in = lanes_padded(jnp.tile(valid.T.astype(jnp.float32), (1, STATES)))[:, None, :]
    lane_start = jnp.arange(width, dtype=jnp.int32) // recordings
    basis = jnp.arange(STATES, dtype=jnp.int32)[:, None] == lane_start[None, :]
    start = lanes_padded(jnp.where(basis, 0.0, NEGATIVE).astype(jnp.float32))
    within_in = jnp.broadcast_to(trans_within[:, :, None], (STATES, STATES, LANES))
    between_in = jnp.broadcast_to(trans_between[:, :, None], (STATES, STATES, LANES))
    prefix, offset = pl.pallas_call(
        prefix_kernel,
        out_shape=(
            jax.ShapeDtypeStruct((patches, STATES, LANES), jnp.float32),
            jax.ShapeDtypeStruct((patches, 1, LANES), jnp.float32),
        ),
        cost_estimate=pl.CostEstimate(
            flops=patches * 80 * LANES * 8, transcendentals=patches * 8 * LANES * 8,
            bytes_accessed=patches * 14 * LANES * 4,
        ),
    )(within_in, between_in, start, emit_in, cross_in, valid_in)
    prefix_sj = prefix[:, :, :width].reshape(patches, STATES, STATES, recordings)
    offset_j = offset[:, 0, :width].reshape(patches, STATES, recordings)
    transfer = prefix_sj[patches - 1] + offset_j[patches - 1][None]
    transfer = jnp.transpose(transfer, (1, 0, 2))
    gathered = lax.all_gather(transfer, "rec")
    mats = lanes_padded(gathered)
    prior = initial - log_sum_exp(initial, 0)
    prior_in = lanes_padded(jnp.broadcast_to(prior[:, None], (STATES, recordings)))
    groups = gathered.shape[0]
    incoming, total = pl.pallas_call(
        chain_kernel,
        out_shape=(
            jax.ShapeDtypeStruct((groups, STATES, LANES), jnp.float32),
            jax.ShapeDtypeStruct((1, LANES), jnp.float32),
        ),
    )(prior_in, mats)
    here = lax.dynamic_index_in_dim(incoming, rec_index, 0, keepdims=False)[:, :recordings]
    weights = here[None, None] + offset_j[:, None] + prefix_sj
    reached = log_sum_exp(weights, 2)
    totals = log_sum_exp(reached, 1)
    filtered = jnp.transpose(reached - totals[:, None], (2, 1, 0))
    return filtered, total[0, :recordings]


def neighbour_shift(block, axis, distance):
    devices = range(lax.axis_size(axis))
    route = [(i - distance, i) for i in devices if i - distance in devices]
    return lax.ppermute(block, axis, route)


def halo_rows(patch_rows):
    patches = patch_rows.shape[2]
    halo = 6
    from_left = neighbour_shift(patch_rows[:, :, patches - halo :], "rec", 1)
    from_right = neighbour_shift(patch_rows[:, :, :halo], "rec", -1)
    return jnp.concatenate([from_left, patch_rows, from_right], axis=2)

def tap_sum(rows, weight_of, taps, length):
    accumulated = None
    for offset in range(taps):
        product = jnp.dot(rows, weight_of(offset), preferred_element_type=jnp.float32)
        product = product[offset : offset + length]
        accumulated = product if accumulated is None else accumulated + product
    return accumulated


def first_kernel(rows_ref, taps_ref, keep_ref, out_ref):
    taps = taps_ref.shape[1]
    keep = keep_ref[...] > 0.5
    for item in range(rows_ref.shape[1]):
        rows = rows_ref[0, item]
        length = rows.shape[0] - 2 * (taps // 2)
        value = jax.nn.gelu(tap_sum(rows, lambda k: taps_ref[0, k], taps, length)).astype(jnp.bfloat16)
        out_ref[0, item] = jnp.where(keep, value, jnp.zeros((), jnp.bfloat16))


def residual_layer(current, taps_ref, taps):
    reach = taps // 2
    length = current.shape[0] - 2 * reach
    update = jax.nn.gelu(tap_sum(current, lambda k: taps_ref[0, 0, k], taps, length))
    return (current[reach : reach + length].astype(jnp.float32) + update).astype(jnp.bfloat16)


def hidden_kernel(rows_ref, taps_ref, keep_ref, out_ref):
    taps = taps_ref.shape[2]
    keep = keep_ref[...] > 0.5
    for item in range(rows_ref.shape[1]):
        value = residual_layer(rows_ref[0, item], taps_ref, taps)
        out_ref[0, item] = jnp.where(keep, value, jnp.zeros((), jnp.bfloat16))


def last_kernel(rows_ref, taps_ref, mix_ref, out_ref):
    @pl.when(pl.program_id(0) == 0)
    def _():
        out_ref[...] = jnp.zeros_like(out_ref)

    taps = taps_ref.shape[2]
    for item in range(rows_ref.shape[1]):
        value = residual_layer(rows_ref[0, item], taps_ref, taps)
        out_ref[item] += jnp.dot(value, mix_ref[0], preferred_element_type=jnp.float32)


def edge_keep(length, margin, rec_index, patches):
    total = patches * lax.axis_size("rec")
    spot = rec_index * patches - margin + jnp.arange(length, dtype=jnp.int32)
    keep = ((spot >= 0) & (spot < total)).astype(jnp.float32)
    return jnp.broadcast_to(keep[:, None], (length, EMB))


def per_type_call(kernel, rows, taps, side, out_block, out_shape, out_map, flops, layer=None):
    types, recordings = rows.shape[:2]
    side_spec = (
        pl.BlockSpec((1,) + side.shape[1:], lambda m: (m, 0, 0))
        if side.ndim == 3 and side.shape[0] == types and kernel is last_kernel
        else pl.BlockSpec(side.shape, lambda m: (0, 0))
    )
    return pl.pallas_call(
        kernel,
        grid=(types,),
        in_specs=[
            pl.BlockSpec((1,) + rows.shape[1:], lambda m: (m, 0, 0, 0)),
            pl.BlockSpec((1,) + taps.shape[1:], lambda m: (m, 0, 0, 0))
            if layer is None
            else pl.BlockSpec((1, 1) + taps.shape[2:], lambda m: (layer, m, 0, 0, 0)),
            side_spec,
        ],
        out_specs=pl.BlockSpec(out_block, out_map),
        out_shape=out_shape,
        compiler_params=pltpu.CompilerParams(dimension_semantics=("arbitrary",)),
        cost_estimate=pl.CostEstimate(
            flops=flops, transcendentals=rows.shape[0] * rows.shape[1] * rows.shape[2] * EMB,
            bytes_accessed=rows.size * 2 + taps.size * 2 // (1 if layer is None else taps.shape[1]) + side.size * 2 + out_shape.size * 4,
        ),
    )(rows, taps, side)


def conv_mix(extended, first_taps, hidden_taps, mix, rec_index, patches):
    types, recordings, span, width = extended.shape
    taps = first_taps.shape[1]
    reach = taps // 2
    layers = hidden_taps.shape[0]
    length = span - 2 * reach
    margin = reach * layers
    current = per_type_call(
        first_kernel, extended, first_taps, edge_keep(length, margin, rec_index, patches),
        (1, recordings, length, EMB), jax.ShapeDtypeStruct((types, recordings, length, EMB), jnp.bfloat16),
        lambda m: (m, 0, 0, 0), 2 * types * recordings * span * width * EMB * taps,
    )
    for depth_index in range(layers - 1):
        length = length - 2 * reach
        margin = margin - reach
        current = per_type_call(
            hidden_kernel, current, hidden_taps, edge_keep(length, margin, rec_index, patches),
            (1, recordings, length, EMB), jax.ShapeDtypeStruct((types, recordings, length, EMB), jnp.bfloat16),
            lambda m: (m, 0, 0, 0), 2 * types * recordings * span * EMB * EMB * taps, depth_index,
        )
    mix_width = mix.shape[-1]
    return per_type_call(
        last_kernel, current, hidden_taps, mix,
        (recordings, patches, mix_width), jax.ShapeDtypeStruct((recordings, patches, mix_width), jnp.float32),
        lambda m: (0, 0, 0), 2 * types * recordings * span * EMB * (EMB * taps + mix_width), layers - 1,
    )


def local(
    signal,
    montage,
    channels,
    lengths,
    boundary,
    conv_in,
    conv_hid,
    mix_weight,
    norm_gain,
    emit_weight,
    trans_within,
    trans_between,
    initial,
):
    groups = lax.axis_size("rec")
    chan_index = lax.axis_index("chan")
    rec_index = lax.axis_index("rec")
    recordings = signal.shape[0]
    patches = signal.shape[2] // SAMP
    slot_ids = chan_index * groups + jnp.arange(groups, dtype=jnp.int32)
    live_slots = slot_ids[None, :] < channels[:, None]
    places = jnp.arange(groups, dtype=jnp.int32)
    pick = (montage[:, 0, None, :] == places[None, :, None]) & live_slots[:, None, :]
    rows = jnp.einsum(
        "bms,bst->mbt", pick.astype(jnp.bfloat16), signal, preferred_element_type=jnp.float32
    ).astype(jnp.bfloat16)
    patch_rows = rows.reshape(groups, recordings, patches, SAMP)
    first_taps = lax.all_gather(conv_in[:, 0], "rec", tiled=True)
    hidden_taps = lax.all_gather(jnp.swapaxes(conv_hid[:, 0], 0, 1), "rec", axis=1, tiled=True)
    extended = halo_rows(patch_rows)
    partial_value = conv_mix(extended, first_taps, hidden_taps, mix_weight[:, 0], rec_index, patches)
    summed = lax.psum(partial_value.astype(jnp.bfloat16), "chan").astype(jnp.float32)
    average = jnp.mean(summed, axis=-1, keepdims=True)
    centred = summed - average
    variance = jnp.mean(centred * centred, axis=-1, keepdims=True)
    activated = jax.nn.gelu(centred * lax.rsqrt(variance + EPSILON) * norm_gain)
    emission = jnp.einsum("bpo,os->bps", activated, emit_weight, precision=lax.Precision.HIGHEST)
    positions = rec_index * patches + jnp.arange(patches, dtype=jnp.int32)
    valid = positions[None, :] < lengths[:, None]
    cross = boundary == 1
    filtered, log_partition = crf_forward(
        emission, cross, valid, trans_within, trans_between, initial, rec_index
    )
    return (filtered, log_partition / lengths.astype(jnp.float32))


def solution(mesh):
    placed = (
        P(None, "chan", "rec"),
        P(None, "chan", None),
        P(),
        P(),
        P(None, "rec"),
        P("rec", "chan", None, None, None),
        P("rec", "chan", None, None, None, None),
        P(None, "chan", None, None),
        P(),
        P(),
        P(),
        P(),
        P(),
    )
    return jax.shard_map(
        local, mesh=mesh, in_specs=placed, out_specs=(P(None, None, "rec"), P()), check_vma=False
    )
```

```python
import functools

import jax
import jax.numpy as jnp
from jax import lax
from jax.experimental import pallas as pl
from jax.experimental.pallas import tpu as pltpu
from jax.sharding import PartitionSpec as P

SAMP = 200
EMB = 128
STATES = 5


EPSILON = 1e-05
NEGATIVE = -1e30
HALO = 8


def log_sum_exp(values, along):
    peak_value = jnp.max(values, axis=along, keepdims=True)
    return jnp.squeeze(peak_value, along) + jnp.log(
        jnp.sum(jnp.exp(values - peak_value), axis=along)
    )


LANES = 128


def forward_step(state, matrices, extra):
    terms = [state[i : i + 1, :] + matrices[i] for i in range(len(matrices))]
    peak = functools.reduce(jnp.maximum, terms)
    total = functools.reduce(lambda x, y: x + y, [jnp.exp(t - peak) for t in terms])
    moved = peak + jnp.log(total)
    if extra is not None:
        moved = moved + extra
    top = jnp.max(moved, axis=0, keepdims=True)
    level = top + jnp.log(jnp.sum(jnp.exp(moved - top), axis=0, keepdims=True))
    return moved - level, level


def prefix_kernel(within_ref, between_ref, start_ref, emit_ref, cross_ref, valid_ref, prefix_ref, offset_ref):
    patches = emit_ref.shape[0]
    within = [within_ref[i] for i in range(STATES)]
    between = [between_ref[i] for i in range(STATES)]

    def body(p, carry):
        state, offset = carry
        crossing = cross_ref[p] > 0.5
        counted = valid_ref[p] > 0.5
        matrices = [jnp.where(crossing, between[i], within[i]) for i in range(STATES)]
        moved, level = forward_step(state, matrices, emit_ref[p])
        state = jnp.where(counted, moved, state)
        offset = offset + jnp.where(counted, level, 0.0)
        prefix_ref[p] = state
        offset_ref[p] = offset
        return state, offset

    lax.fori_loop(0, patches, body, (start_ref[...], jnp.zeros((1, LANES), jnp.float32)))


def chain_kernel(prior_ref, mats_ref, incoming_ref, total_ref):
    count = mats_ref.shape[0]

    def body(k, carry):
        state, total = carry
        incoming_ref[k] = state
        matrices = [mats_ref[k, j] for j in range(STATES)]
        moved, level = forward_step(state, matrices, None)
        return moved, total + level

    _, total = lax.fori_loop(0, count, body, (prior_ref[...], jnp.zeros((1, LANES), jnp.float32)))
    total_ref[...] = total


def lanes_padded(values):
    pad = [(0, 0)] * (values.ndim - 1) + [(0, LANES - values.shape[-1])]
    return jnp.pad(values, pad)


def crf_forward(emission, cross, valid, trans_within, trans_between, initial, rec_index):
    recordings, patches, _ = emission.shape
    width = STATES * recordings
    emit_in = lanes_padded(jnp.tile(jnp.transpose(emission, (1, 2, 0)), (1, 1, STATES)))
    cross_in = lanes_padded(jnp.tile(cross.T.astype(jnp.float32), (1, STATES)))[:, None, :]
    valid_in = lanes_padded(jnp.tile(valid.T.astype(jnp.float32), (1, STATES)))[:, None, :]
    lane_start = jnp.arange(width, dtype=jnp.int32) // recordings
    basis = jnp.arange(STATES, dtype=jnp.int32)[:, None] == lane_start[None, :]
    start = lanes_padded(jnp.where(basis, 0.0, NEGATIVE).astype(jnp.float32))
    within_in = jnp.broadcast_to(trans_within[:, :, None], (STATES, STATES, LANES))
    between_in = jnp.broadcast_to(trans_between[:, :, None], (STATES, STATES, LANES))
    prefix, offset = pl.pallas_call(
        prefix_kernel,
        out_shape=(
            jax.ShapeDtypeStruct((patches, STATES, LANES), jnp.float32),
            jax.ShapeDtypeStruct((patches, 1, LANES), jnp.float32),
        ),
        cost_estimate=pl.CostEstimate(
            flops=patches * 80 * LANES * 8, transcendentals=patches * 8 * LANES * 8,
            bytes_accessed=patches * 14 * LANES * 4,
        ),
    )(within_in, between_in, start, emit_in, cross_in, valid_in)
    prefix_sj = prefix[:, :, :width].reshape(patches, STATES, STATES, recordings)
    offset_j = offset[:, 0, :width].reshape(patches, STATES, recordings)
    transfer = prefix_sj[patches - 1] + offset_j[patches - 1][None]
    transfer = jnp.transpose(transfer, (1, 0, 2))
    gathered = lax.all_gather(transfer, "rec")
    mats = lanes_padded(gathered)
    prior = initial - log_sum_exp(initial, 0)
    prior_in = lanes_padded(jnp.broadcast_to(prior[:, None], (STATES, recordings)))
    groups = gathered.shape[0]
    incoming, total = pl.pallas_call(
        chain_kernel,
        out_shape=(
            jax.ShapeDtypeStruct((groups, STATES, LANES), jnp.float32),
            jax.ShapeDtypeStruct((1, LANES), jnp.float32),
        ),
    )(prior_in, mats)
    here = lax.dynamic_index_in_dim(incoming, rec_index, 0, keepdims=False)[:, :recordings]
    weights = here[None, None] + offset_j[:, None] + prefix_sj
    reached = log_sum_exp(weights, 2)
    totals = log_sum_exp(reached, 1)
    filtered = jnp.transpose(reached - totals[:, None], (2, 1, 0))
    return filtered, total[0, :recordings]


def neighbour_shift(block, axis, distance):
    devices = range(lax.axis_size(axis))
    route = [(i - distance, i) for i in devices if i - distance in devices]
    return lax.ppermute(block, axis, route)


def halo_rows(patch_rows, halo):
    patches = patch_rows.shape[2]
    from_left = neighbour_shift(patch_rows[:, :, patches - halo :], "rec", 1)
    from_right = neighbour_shift(patch_rows[:, :, :halo], "rec", -1)
    return jnp.concatenate([from_left, patch_rows, from_right], axis=2)

def rolled_taps(rows, weight_of, taps):
    reach = taps // 2
    count = rows.shape[0]
    accumulated = None
    for offset in range(taps):
        product = jnp.dot(rows, weight_of(offset), preferred_element_type=jnp.float32)
        shift = (reach - offset) % count
        if shift:
            product = pltpu.roll(product, shift, 0)
        accumulated = product if accumulated is None else accumulated + product
    return accumulated


def merged(ref):
    shape = ref.shape
    return ref[0].reshape(shape[1] * shape[2], shape[3])


def first_kernel(rows_ref, taps_ref, keep_ref, out_ref):
    value = jax.nn.gelu(rolled_taps(merged(rows_ref), lambda k: taps_ref[0, k], taps_ref.shape[1]))
    value = jnp.where(keep_ref[...] > 0.5, value.astype(jnp.bfloat16), jnp.zeros((), jnp.bfloat16))
    out_ref[0] = value.reshape(out_ref.shape[1:])


def residual_layer(current, taps_ref):
    update = jax.nn.gelu(rolled_taps(current, lambda k: taps_ref[0, 0, k], taps_ref.shape[2]))
    return (current.astype(jnp.float32) + update).astype(jnp.bfloat16)


def hidden_kernel(rows_ref, taps_ref, keep_ref, out_ref):
    value = residual_layer(merged(rows_ref), taps_ref)
    value = jnp.where(keep_ref[...] > 0.5, value, jnp.zeros((), jnp.bfloat16))
    out_ref[0] = value.reshape(out_ref.shape[1:])


def last_kernel(rows_ref, taps_ref, mix_ref, out_ref):
    @pl.when(pl.program_id(0) == 0)
    def _():
        out_ref[...] = jnp.zeros_like(out_ref)

    span = rows_ref.shape[2]
    recordings, patches = out_ref.shape[:2]
    margin = (span - patches) // 2
    value = residual_layer(merged(rows_ref), taps_ref)
    mixed = jnp.dot(value, mix_ref[0], preferred_element_type=jnp.float32)
    for item in range(recordings):
        start = item * span + margin
        out_ref[item] += mixed[start : start + patches]


def edge_keep(span, margin, rec_index, patches, recordings):
    total = patches * lax.axis_size("rec")
    spot = rec_index * patches - margin + jnp.arange(span, dtype=jnp.int32)
    keep = ((spot >= 0) & (spot < total)).astype(jnp.float32)
    return jnp.tile(jnp.broadcast_to(keep[:, None], (span, EMB)), (recordings, 1))


def per_type_call(kernel, rows, taps, side, out_block, out_shape, out_map, flops, layer=None):
    types, recordings = rows.shape[:2]
    side_spec = (
        pl.BlockSpec((1,) + side.shape[1:], lambda m: (m, 0, 0))
        if kernel is last_kernel
        else pl.BlockSpec(side.shape, lambda m: (0, 0))
    )
    return pl.pallas_call(
        kernel,
        grid=(types,),
        in_specs=[
            pl.BlockSpec((1,) + rows.shape[1:], lambda m: (m, 0, 0, 0)),
            pl.BlockSpec((1,) + taps.shape[1:], lambda m: (m, 0, 0, 0))
            if layer is None
            else pl.BlockSpec((1, 1) + taps.shape[2:], lambda m: (layer, m, 0, 0, 0)),
            side_spec,
        ],
        out_specs=pl.BlockSpec(out_block, out_map),
        out_shape=out_shape,
        compiler_params=pltpu.CompilerParams(dimension_semantics=("arbitrary",)),
        cost_estimate=pl.CostEstimate(
            flops=flops, transcendentals=rows.shape[0] * rows.shape[1] * rows.shape[2] * EMB,
            bytes_accessed=rows.size * 2 + taps.size * 2 // (1 if layer is None else taps.shape[0]) + side.size * 2 + out_shape.size * 4,
        ),
    )(rows, taps, side)


def conv_mix(extended, first_taps, hidden_taps, mix, rec_index, patches):
    types, recordings, span, width = extended.shape
    taps = first_taps.shape[1]
    layers = hidden_taps.shape[0]
    margin = (span - patches) // 2
    keep = edge_keep(span, margin, rec_index, patches, recordings)
    block = (1, recordings, span, EMB)
    inner = jax.ShapeDtypeStruct((types, recordings, span, EMB), jnp.bfloat16)
    current = per_type_call(
        first_kernel, extended, first_taps, keep, block, inner,
        lambda m: (m, 0, 0, 0), 2 * types * recordings * span * width * EMB * taps,
    )
    for depth_index in range(layers - 1):
        current = per_type_call(
            hidden_kernel, current, hidden_taps, keep, block, inner,
            lambda m: (m, 0, 0, 0), 2 * types * recordings * span * EMB * EMB * taps, depth_index,
        )
    mix_width = mix.shape[-1]
    return per_type_call(
        last_kernel, current, hidden_taps, mix,
        (recordings, patches, mix_width), jax.ShapeDtypeStruct((recordings, patches, mix_width), jnp.float32),
        lambda m: (0, 0, 0), 2 * types * recordings * span * EMB * (EMB * taps + mix_width), layers - 1,
    )


def local(
    signal,
    montage,
    channels,
    lengths,
    boundary,
    conv_in,
    conv_hid,
    mix_weight,
    norm_gain,
    emit_weight,
    trans_within,
    trans_between,
    initial,
):
    groups = lax.axis_size("rec")
    chan_index = lax.axis_index("chan")
    rec_index = lax.axis_index("rec")
    recordings = signal.shape[0]
    patches = signal.shape[2] // SAMP
    slot_ids = chan_index * groups + jnp.arange(groups, dtype=jnp.int32)
    live_slots = slot_ids[None, :] < channels[:, None]
    places = jnp.arange(groups, dtype=jnp.int32)
    pick = (montage[:, 0, None, :] == places[None, :, None]) & live_slots[:, None, :]
    rows = jnp.einsum(
        "bms,bst->mbt", pick.astype(jnp.bfloat16), signal, preferred_element_type=jnp.float32
    ).astype(jnp.bfloat16)
    patch_rows = rows.reshape(groups, recordings, patches, SAMP)
    first_taps = lax.all_gather(conv_in[:, 0], "rec", tiled=True)
    hidden_taps = lax.all_gather(jnp.swapaxes(conv_hid[:, 0], 0, 1), "rec", axis=1, tiled=True)
    extended = halo_rows(patch_rows, HALO)
    partial_value = conv_mix(extended, first_taps, hidden_taps, mix_weight[:, 0], rec_index, patches)
    summed = lax.psum(partial_value, "chan")
    average = jnp.mean(summed, axis=-1, keepdims=True)
    centred = summed - average
    variance = jnp.mean(centred * centred, axis=-1, keepdims=True)
    activated = jax.nn.gelu(centred * lax.rsqrt(variance + EPSILON) * norm_gain)
    emission = jnp.einsum("bpo,os->bps", activated, emit_weight, precision=lax.Precision.HIGHEST)
    positions = rec_index * patches + jnp.arange(patches, dtype=jnp.int32)
    valid = positions[None, :] < lengths[:, None]
    cross = boundary == 1
    filtered, log_partition = crf_forward(
        emission, cross, valid, trans_within, trans_between, initial, rec_index
    )
    return (filtered, log_partition / lengths.astype(jnp.float32))


def solution(mesh):
    placed = (
        P(None, "chan", "rec"),
        P(None, "chan", None),
        P(),
        P(),
        P(None, "rec"),
        P("rec", "chan", None, None, None),
        P("rec", "chan", None, None, None, None),
        P(None, "chan", None, None),
        P(),
        P(),
        P(),
        P(),
        P(),
    )
    return jax.shard_map(
        local, mesh=mesh, in_specs=placed, out_specs=(P(None, None, "rec"), P()), check_vma=False
    )
```

```python
import functools

import jax
import jax.numpy as jnp
from jax import lax
from jax.experimental import pallas as pl
from jax.experimental.pallas import tpu as pltpu
from jax.sharding import PartitionSpec as P

SAMP = 200
EMB = 128
STATES = 5


EPSILON = 1e-05
NEGATIVE = -1e30
HALO = 8


def log_sum_exp(values, along):
    peak_value = jnp.max(values, axis=along, keepdims=True)
    return jnp.squeeze(peak_value, along) + jnp.log(
        jnp.sum(jnp.exp(values - peak_value), axis=along)
    )


LANES = 128


def forward_step(state, matrices, extra):
    terms = [state[i : i + 1, :] + matrices[i] for i in range(len(matrices))]
    peak = functools.reduce(jnp.maximum, terms)
    total = functools.reduce(lambda x, y: x + y, [jnp.exp(t - peak) for t in terms])
    moved = peak + jnp.log(total)
    if extra is not None:
        moved = moved + extra
    top = jnp.max(moved, axis=0, keepdims=True)
    level = top + jnp.log(jnp.sum(jnp.exp(moved - top), axis=0, keepdims=True))
    return moved - level, level


def prefix_kernel(within_ref, between_ref, start_ref, emit_ref, cross_ref, valid_ref, prefix_ref, offset_ref):
    patches = emit_ref.shape[0]
    within = [within_ref[i] for i in range(STATES)]
    between = [between_ref[i] for i in range(STATES)]

    def body(p, carry):
        state, offset = carry
        crossing = cross_ref[p] > 0.5
        counted = valid_ref[p] > 0.5
        matrices = [jnp.where(crossing, between[i], within[i]) for i in range(STATES)]
        moved, level = forward_step(state, matrices, emit_ref[p])
        state = jnp.where(counted, moved, state)
        offset = offset + jnp.where(counted, level, 0.0)
        prefix_ref[p] = state
        offset_ref[p] = offset
        return state, offset

    lax.fori_loop(0, patches, body, (start_ref[...], jnp.zeros((1, LANES), jnp.float32)))


def chain_kernel(prior_ref, mats_ref, incoming_ref, total_ref):
    count = mats_ref.shape[0]

    def body(k, carry):
        state, total = carry
        incoming_ref[k] = state
        matrices = [mats_ref[k, j] for j in range(STATES)]
        moved, level = forward_step(state, matrices, None)
        return moved, total + level

    _, total = lax.fori_loop(0, count, body, (prior_ref[...], jnp.zeros((1, LANES), jnp.float32)))
    total_ref[...] = total


def lanes_padded(values):
    pad = [(0, 0)] * (values.ndim - 1) + [(0, LANES - values.shape[-1])]
    return jnp.pad(values, pad)


def crf_forward(emission, cross, valid, trans_within, trans_between, initial, rec_index):
    recordings, patches, _ = emission.shape
    width = STATES * recordings
    emit_in = lanes_padded(jnp.tile(jnp.transpose(emission, (1, 2, 0)), (1, 1, STATES)))
    cross_in = lanes_padded(jnp.tile(cross.T.astype(jnp.float32), (1, STATES)))[:, None, :]
    valid_in = lanes_padded(jnp.tile(valid.T.astype(jnp.float32), (1, STATES)))[:, None, :]
    lane_start = jnp.arange(width, dtype=jnp.int32) // recordings
    basis = jnp.arange(STATES, dtype=jnp.int32)[:, None] == lane_start[None, :]
    start = lanes_padded(jnp.where(basis, 0.0, NEGATIVE).astype(jnp.float32))
    within_in = jnp.broadcast_to(trans_within[:, :, None], (STATES, STATES, LANES))
    between_in = jnp.broadcast_to(trans_between[:, :, None], (STATES, STATES, LANES))
    prefix, offset = pl.pallas_call(
        prefix_kernel,
        out_shape=(
            jax.ShapeDtypeStruct((patches, STATES, LANES), jnp.float32),
            jax.ShapeDtypeStruct((patches, 1, LANES), jnp.float32),
        ),
        cost_estimate=pl.CostEstimate(
            flops=patches * 80 * LANES * 8, transcendentals=patches * 8 * LANES * 8,
            bytes_accessed=patches * 14 * LANES * 4,
        ),
    )(within_in, between_in, start, emit_in, cross_in, valid_in)
    prefix_sj = prefix[:, :, :width].reshape(patches, STATES, STATES, recordings)
    offset_j = offset[:, 0, :width].reshape(patches, STATES, recordings)
    transfer = prefix_sj[patches - 1] + offset_j[patches - 1][None]
    transfer = jnp.transpose(transfer, (1, 0, 2))
    gathered = lax.all_gather(transfer, "rec")
    mats = lanes_padded(gathered)
    prior = initial - log_sum_exp(initial, 0)
    prior_in = lanes_padded(jnp.broadcast_to(prior[:, None], (STATES, recordings)))
    groups = gathered.shape[0]
    incoming, total = pl.pallas_call(
        chain_kernel,
        out_shape=(
            jax.ShapeDtypeStruct((groups, STATES, LANES), jnp.float32),
            jax.ShapeDtypeStruct((1, LANES), jnp.float32),
        ),
    )(prior_in, mats)
    here = lax.dynamic_index_in_dim(incoming, rec_index, 0, keepdims=False)[:, :recordings]
    weights = here[None, None] + offset_j[:, None] + prefix_sj
    reached = log_sum_exp(weights, 2)
    totals = log_sum_exp(reached, 1)
    filtered = jnp.transpose(reached - totals[:, None], (2, 1, 0))
    return filtered, total[0, :recordings]


def neighbour_shift(block, axis, distance):
    devices = range(lax.axis_size(axis))
    route = [(i - distance, i) for i in devices if i - distance in devices]
    return lax.ppermute(block, axis, route)


def halo_rows(patch_rows, halo):
    patches = patch_rows.shape[2]
    from_left = neighbour_shift(patch_rows[:, :, patches - halo :], "rec", 1)
    from_right = neighbour_shift(patch_rows[:, :, :halo], "rec", -1)
    return jnp.concatenate([from_left, patch_rows, from_right], axis=2)

def rolled_taps(rows, weight_of, taps):
    reach = taps // 2
    count = rows.shape[0]
    accumulated = None
    for offset in range(taps):
        product = jnp.dot(rows, weight_of(offset), preferred_element_type=jnp.float32)
        shift = (reach - offset) % count
        if shift:
            product = pltpu.roll(product, shift, 0)
        accumulated = product if accumulated is None else accumulated + product
    return accumulated


def merged(ref):
    shape = ref.shape
    return ref[0].reshape(shape[1] * shape[2], shape[3])


def first_kernel(rows_ref, taps_ref, keep_ref, out_ref):
    value = jax.nn.gelu(rolled_taps(merged(rows_ref), lambda k: taps_ref[0, k], taps_ref.shape[1]))
    value = jnp.where(keep_ref[...] > 0.5, value.astype(jnp.bfloat16), jnp.zeros((), jnp.bfloat16))
    out_ref[0] = value.reshape(out_ref.shape[1:])


def residual_layer(current, taps_ref):
    update = jax.nn.gelu(rolled_taps(current, lambda k: taps_ref[0, 0, k], taps_ref.shape[2]))
    return (current.astype(jnp.float32) + update).astype(jnp.bfloat16)


def hidden_kernel(rows_ref, taps_ref, keep_ref, out_ref):
    value = residual_layer(merged(rows_ref), taps_ref)
    value = jnp.where(keep_ref[...] > 0.5, value, jnp.zeros((), jnp.bfloat16))
    out_ref[0] = value.reshape(out_ref.shape[1:])


def last_kernel(rows_ref, taps_ref, mix_ref, out_ref):
    @pl.when(pl.program_id(0) == 0)
    def _():
        out_ref[...] = jnp.zeros_like(out_ref)

    span = rows_ref.shape[2]
    recordings, patches = out_ref.shape[:2]
    margin = (span - patches) // 2
    value = residual_layer(merged(rows_ref), taps_ref)
    mixed = jnp.dot(value, mix_ref[0], preferred_element_type=jnp.float32)
    for item in range(recordings):
        start = item * span + margin
        out_ref[item] += mixed[start : start + patches]


def edge_keep(span, margin, rec_index, patches, recordings):
    total = patches * lax.axis_size("rec")
    spot = rec_index * patches - margin + jnp.arange(span, dtype=jnp.int32)
    keep = ((spot >= 0) & (spot < total)).astype(jnp.float32)
    return jnp.tile(jnp.broadcast_to(keep[:, None], (span, EMB)), (recordings, 1))


def per_type_call(kernel, rows, taps, side, out_block, out_shape, out_map, flops, layer=None):
    types, recordings = rows.shape[:2]
    side_spec = (
        pl.BlockSpec((1,) + side.shape[1:], lambda m: (m, 0, 0))
        if kernel is last_kernel
        else pl.BlockSpec(side.shape, lambda m: (0, 0))
    )
    return pl.pallas_call(
        kernel,
        grid=(types,),
        in_specs=[
            pl.BlockSpec((1,) + rows.shape[1:], lambda m: (m, 0, 0, 0)),
            pl.BlockSpec((1,) + taps.shape[1:], lambda m: (m, 0, 0, 0))
            if layer is None
            else pl.BlockSpec((1, 1) + taps.shape[2:], lambda m: (layer, m, 0, 0, 0)),
            side_spec,
        ],
        out_specs=pl.BlockSpec(out_block, out_map),
        out_shape=out_shape,
        compiler_params=pltpu.CompilerParams(dimension_semantics=("arbitrary",)),
        cost_estimate=pl.CostEstimate(
            flops=flops, transcendentals=rows.shape[0] * rows.shape[1] * rows.shape[2] * EMB,
            bytes_accessed=rows.size * 2 + taps.size * 2 // (1 if layer is None else taps.shape[0]) + side.size * 2 + out_shape.size * 4,
        ),
    )(rows, taps, side)


def conv_mix(extended, first_taps, hidden_taps, mix, rec_index, patches):
    types, recordings, span, width = extended.shape
    taps = first_taps.shape[1]
    layers = hidden_taps.shape[0]
    margin = (span - patches) // 2
    keep = edge_keep(span, margin, rec_index, patches, recordings)
    block = (1, recordings, span, EMB)
    inner = jax.ShapeDtypeStruct((types, recordings, span, EMB), jnp.bfloat16)
    current = per_type_call(
        first_kernel, extended, first_taps, keep, block, inner,
        lambda m: (m, 0, 0, 0), 2 * types * recordings * span * width * EMB * taps,
    )
    for depth_index in range(layers - 1):
        current = per_type_call(
            hidden_kernel, current, hidden_taps, keep, block, inner,
            lambda m: (m, 0, 0, 0), 2 * types * recordings * span * EMB * EMB * taps, depth_index,
        )
    mix_width = mix.shape[-1]
    return per_type_call(
        last_kernel, current, hidden_taps, mix,
        (recordings, patches, mix_width), jax.ShapeDtypeStruct((recordings, patches, mix_width), jnp.float32),
        lambda m: (0, 0, 0), 2 * types * recordings * span * EMB * (EMB * taps + mix_width), layers - 1,
    )


def local(
    signal,
    montage,
    channels,
    lengths,
    boundary,
    conv_in,
    conv_hid,
    mix_weight,
    norm_gain,
    emit_weight,
    trans_within,
    trans_between,
    initial,
):
    groups = lax.axis_size("rec")
    chan_index = lax.axis_index("chan")
    rec_index = lax.axis_index("rec")
    recordings = signal.shape[0]
    patches = signal.shape[2] // SAMP
    slot_ids = chan_index * groups + jnp.arange(groups, dtype=jnp.int32)
    live_slots = slot_ids[None, :] < channels[:, None]
    places = jnp.arange(groups, dtype=jnp.int32)
    pick = (montage[:, 0, None, :] == places[None, :, None]) & live_slots[:, None, :]
    rows = jnp.einsum(
        "bms,bst->mbt", pick.astype(jnp.bfloat16), signal, preferred_element_type=jnp.float32
    ).astype(jnp.bfloat16)
    patch_rows = rows.reshape(groups, recordings, patches, SAMP)
    first_taps = lax.all_gather(conv_in[:, 0], "rec", tiled=True)
    hidden_taps = lax.all_gather(jnp.swapaxes(conv_hid[:, 0], 0, 1), "rec", axis=1, tiled=True)
    extended = halo_rows(patch_rows, HALO)
    partial_value = conv_mix(extended, first_taps, hidden_taps, mix_weight[:, 0], rec_index, patches)
    spread = lax.axis_size("chan")
    pieces = partial_value.reshape(recordings, spread, patches // spread, partial_value.shape[-1])
    pieces = lax.all_to_all(jnp.swapaxes(pieces, 0, 1), "chan", 0, 0, tiled=True)
    summed = jnp.sum(pieces, axis=0)
    average = jnp.mean(summed, axis=-1, keepdims=True)
    centred = summed - average
    variance = jnp.mean(centred * centred, axis=-1, keepdims=True)
    activated = jax.nn.gelu(centred * lax.rsqrt(variance + EPSILON) * norm_gain)
    emission = jnp.einsum("bpo,os->bps", activated, emit_weight, precision=lax.Precision.HIGHEST)
    shared = lax.all_to_all(jnp.broadcast_to(emission[None], (spread,) + emission.shape), "chan", 0, 0, tiled=True)
    emission = jnp.swapaxes(shared, 0, 1).reshape(recordings, patches, STATES)
    positions = rec_index * patches + jnp.arange(patches, dtype=jnp.int32)
    valid = positions[None, :] < lengths[:, None]
    cross = boundary == 1
    filtered, log_partition = crf_forward(
        emission, cross, valid, trans_within, trans_between, initial, rec_index
    )
    return (filtered, log_partition / lengths.astype(jnp.float32))


def solution(mesh):
    placed = (
        P(None, "chan", "rec"),
        P(None, "chan", None),
        P(),
        P(),
        P(None, "rec"),
        P("rec", "chan", None, None, None),
        P("rec", "chan", None, None, None, None),
        P(None, "chan", None, None),
        P(),
        P(),
        P(),
        P(),
        P(),
    )
    return jax.shard_map(
        local, mesh=mesh, in_specs=placed, out_specs=(P(None, None, "rec"), P()), check_vma=False
    )
```

```python
import functools

import jax
import jax.numpy as jnp
from jax import lax
from jax.experimental import pallas as pl
from jax.experimental.pallas import tpu as pltpu
from jax.sharding import PartitionSpec as P

SAMP = 200
EMB = 128
STATES = 5


EPSILON = 1e-05
NEGATIVE = -1e30
HALO = 8


def log_sum_exp(values, along):
    peak_value = jnp.max(values, axis=along, keepdims=True)
    return jnp.squeeze(peak_value, along) + jnp.log(
        jnp.sum(jnp.exp(values - peak_value), axis=along)
    )


LANES = 128


def forward_step(state, matrices, extra):
    terms = [state[i : i + 1, :] + matrices[i] for i in range(len(matrices))]
    peak = functools.reduce(jnp.maximum, terms)
    total = functools.reduce(lambda x, y: x + y, [jnp.exp(t - peak) for t in terms])
    moved = peak + jnp.log(total)
    if extra is not None:
        moved = moved + extra
    top = jnp.max(moved, axis=0, keepdims=True)
    level = top + jnp.log(jnp.sum(jnp.exp(moved - top), axis=0, keepdims=True))
    return moved - level, level


def prefix_kernel(within_ref, between_ref, start_ref, emit_ref, cross_ref, valid_ref, prefix_ref, offset_ref):
    patches = emit_ref.shape[0]
    within = [within_ref[i] for i in range(STATES)]
    between = [between_ref[i] for i in range(STATES)]

    def body(p, carry):
        state, offset = carry
        crossing = cross_ref[p] > 0.5
        counted = valid_ref[p] > 0.5
        matrices = [jnp.where(crossing, between[i], within[i]) for i in range(STATES)]
        moved, level = forward_step(state, matrices, emit_ref[p])
        state = jnp.where(counted, moved, state)
        offset = offset + jnp.where(counted, level, 0.0)
        prefix_ref[p] = state
        offset_ref[p] = offset
        return state, offset

    lax.fori_loop(0, patches, body, (start_ref[...], jnp.zeros((1, LANES), jnp.float32)))


def chain_kernel(prior_ref, mats_ref, incoming_ref, total_ref):
    count = mats_ref.shape[0]

    def body(k, carry):
        state, total = carry
        incoming_ref[k] = state
        matrices = [mats_ref[k, j] for j in range(STATES)]
        moved, level = forward_step(state, matrices, None)
        return moved, total + level

    _, total = lax.fori_loop(0, count, body, (prior_ref[...], jnp.zeros((1, LANES), jnp.float32)))
    total_ref[...] = total


def lanes_padded(values):
    pad = [(0, 0)] * (values.ndim - 1) + [(0, LANES - values.shape[-1])]
    return jnp.pad(values, pad)


def crf_forward(emission, cross, valid, trans_within, trans_between, initial, rec_index):
    recordings, patches, _ = emission.shape
    width = STATES * recordings
    emit_in = lanes_padded(jnp.tile(jnp.transpose(emission, (1, 2, 0)), (1, 1, STATES)))
    cross_in = lanes_padded(jnp.tile(cross.T.astype(jnp.float32), (1, STATES)))[:, None, :]
    valid_in = lanes_padded(jnp.tile(valid.T.astype(jnp.float32), (1, STATES)))[:, None, :]
    lane_start = jnp.arange(width, dtype=jnp.int32) // recordings
    basis = jnp.arange(STATES, dtype=jnp.int32)[:, None] == lane_start[None, :]
    start = lanes_padded(jnp.where(basis, 0.0, NEGATIVE).astype(jnp.float32))
    within_in = jnp.broadcast_to(trans_within[:, :, None], (STATES, STATES, LANES))
    between_in = jnp.broadcast_to(trans_between[:, :, None], (STATES, STATES, LANES))
    prefix, offset = pl.pallas_call(
        prefix_kernel,
        out_shape=(
            jax.ShapeDtypeStruct((patches, STATES, LANES), jnp.float32),
            jax.ShapeDtypeStruct((patches, 1, LANES), jnp.float32),
        ),
        cost_estimate=pl.CostEstimate(
            flops=patches * 80 * LANES * 8, transcendentals=patches * 8 * LANES * 8,
            bytes_accessed=patches * 14 * LANES * 4,
        ),
    )(within_in, between_in, start, emit_in, cross_in, valid_in)
    prefix_sj = prefix[:, :, :width].reshape(patches, STATES, STATES, recordings)
    offset_j = offset[:, 0, :width].reshape(patches, STATES, recordings)
    transfer = prefix_sj[patches - 1] + offset_j[patches - 1][None]
    transfer = jnp.transpose(transfer, (1, 0, 2))
    groups = lax.axis_size("rec")
    gathered = lax.all_to_all(jnp.broadcast_to(transfer[None], (groups,) + transfer.shape), "rec", 0, 0, tiled=True)
    mats = lanes_padded(gathered)
    prior = initial - log_sum_exp(initial, 0)
    prior_in = lanes_padded(jnp.broadcast_to(prior[:, None], (STATES, recordings)))
    incoming, total = pl.pallas_call(
        chain_kernel,
        out_shape=(
            jax.ShapeDtypeStruct((groups, STATES, LANES), jnp.float32),
            jax.ShapeDtypeStruct((1, LANES), jnp.float32),
        ),
    )(prior_in, mats)
    here = lax.dynamic_index_in_dim(incoming, rec_index, 0, keepdims=False)[:, :recordings]
    weights = here[None, None] + offset_j[:, None] + prefix_sj
    reached = log_sum_exp(weights, 2)
    totals = log_sum_exp(reached, 1)
    filtered = jnp.transpose(reached - totals[:, None], (2, 1, 0))
    return filtered, total[0, :recordings]


def neighbour_shift(block, axis, distance):
    devices = range(lax.axis_size(axis))
    route = [(i - distance, i) for i in devices if i - distance in devices]
    return lax.ppermute(block, axis, route)


def halo_rows(patch_rows, halo):
    patches = patch_rows.shape[2]
    from_left = neighbour_shift(patch_rows[:, :, patches - halo :], "rec", 1)
    from_right = neighbour_shift(patch_rows[:, :, :halo], "rec", -1)
    return jnp.concatenate([from_left, patch_rows, from_right], axis=2)

def rolled_taps(rows, weight_of, taps):
    reach = taps // 2
    count = rows.shape[0]
    accumulated = None
    for offset in range(taps):
        product = jnp.dot(rows, weight_of(offset), preferred_element_type=jnp.float32)
        shift = (reach - offset) % count
        if shift:
            product = pltpu.roll(product, shift, 0)
        accumulated = product if accumulated is None else accumulated + product
    return accumulated


def merged(ref):
    shape = ref.shape
    return ref[0].reshape(shape[1] * shape[2], shape[3])


def first_kernel(rows_ref, taps_ref, keep_ref, out_ref):
    value = jax.nn.gelu(rolled_taps(merged(rows_ref), lambda k: taps_ref[0, k], taps_ref.shape[1]))
    value = jnp.where(keep_ref[...] > 0.5, value.astype(jnp.bfloat16), jnp.zeros((), jnp.bfloat16))
    out_ref[0] = value.reshape(out_ref.shape[1:])


def residual_layer(current, taps_ref):
    update = jax.nn.gelu(rolled_taps(current, lambda k: taps_ref[0, 0, k], taps_ref.shape[2]))
    return (current.astype(jnp.float32) + update).astype(jnp.bfloat16)


def hidden_kernel(rows_ref, taps_ref, keep_ref, out_ref):
    value = residual_layer(merged(rows_ref), taps_ref)
    value = jnp.where(keep_ref[...] > 0.5, value, jnp.zeros((), jnp.bfloat16))
    out_ref[0] = value.reshape(out_ref.shape[1:])


def last_kernel(rows_ref, taps_ref, mix_ref, out_ref):
    @pl.when(pl.program_id(0) == 0)
    def _():
        out_ref[...] = jnp.zeros_like(out_ref)

    span = rows_ref.shape[2]
    recordings, patches = out_ref.shape[:2]
    margin = (span - patches) // 2
    value = residual_layer(merged(rows_ref), taps_ref)
    mixed = jnp.dot(value, mix_ref[0], preferred_element_type=jnp.float32)
    for item in range(recordings):
        start = item * span + margin
        out_ref[item] += mixed[start : start + patches]


def edge_keep(span, margin, rec_index, patches, recordings):
    total = patches * lax.axis_size("rec")
    spot = rec_index * patches - margin + jnp.arange(span, dtype=jnp.int32)
    keep = ((spot >= 0) & (spot < total)).astype(jnp.float32)
    return jnp.tile(jnp.broadcast_to(keep[:, None], (span, EMB)), (recordings, 1))


def per_type_call(kernel, rows, taps, side, out_block, out_shape, out_map, flops, layer=None):
    types, recordings = rows.shape[:2]
    side_spec = (
        pl.BlockSpec((1,) + side.shape[1:], lambda m: (m, 0, 0))
        if kernel is last_kernel
        else pl.BlockSpec(side.shape, lambda m: (0, 0))
    )
    return pl.pallas_call(
        kernel,
        grid=(types,),
        in_specs=[
            pl.BlockSpec((1,) + rows.shape[1:], lambda m: (m, 0, 0, 0)),
            pl.BlockSpec((1,) + taps.shape[1:], lambda m: (m, 0, 0, 0))
            if layer is None
            else pl.BlockSpec((1, 1) + taps.shape[2:], lambda m: (layer, m, 0, 0, 0)),
            side_spec,
        ],
        out_specs=pl.BlockSpec(out_block, out_map),
        out_shape=out_shape,
        compiler_params=pltpu.CompilerParams(dimension_semantics=("arbitrary",)),
        cost_estimate=pl.CostEstimate(
            flops=flops, transcendentals=rows.shape[0] * rows.shape[1] * rows.shape[2] * EMB,
            bytes_accessed=rows.size * 2 + taps.size * 2 // (1 if layer is None else taps.shape[0]) + side.size * 2 + out_shape.size * 4,
        ),
    )(rows, taps, side)


def conv_mix(extended, first_taps, hidden_taps, mix, rec_index, patches):
    types, recordings, span, width = extended.shape
    taps = first_taps.shape[1]
    layers = hidden_taps.shape[0]
    margin = (span - patches) // 2
    keep = edge_keep(span, margin, rec_index, patches, recordings)
    block = (1, recordings, span, EMB)
    inner = jax.ShapeDtypeStruct((types, recordings, span, EMB), jnp.bfloat16)
    current = per_type_call(
        first_kernel, extended, first_taps, keep, block, inner,
        lambda m: (m, 0, 0, 0), 2 * types * recordings * span * width * EMB * taps,
    )
    for depth_index in range(layers - 1):
        current = per_type_call(
            hidden_kernel, current, hidden_taps, keep, block, inner,
            lambda m: (m, 0, 0, 0), 2 * types * recordings * span * EMB * EMB * taps, depth_index,
        )
    mix_width = mix.shape[-1]
    return per_type_call(
        last_kernel, current, hidden_taps, mix,
        (recordings, patches, mix_width), jax.ShapeDtypeStruct((recordings, patches, mix_width), jnp.float32),
        lambda m: (0, 0, 0), 2 * types * recordings * span * EMB * (EMB * taps + mix_width), layers - 1,
    )


def local(
    signal,
    montage,
    channels,
    lengths,
    boundary,
    conv_in,
    conv_hid,
    mix_weight,
    norm_gain,
    emit_weight,
    trans_within,
    trans_between,
    initial,
):
    groups = lax.axis_size("rec")
    chan_index = lax.axis_index("chan")
    rec_index = lax.axis_index("rec")
    recordings = signal.shape[0]
    patches = signal.shape[2] // SAMP
    slot_ids = chan_index * groups + jnp.arange(groups, dtype=jnp.int32)
    live_slots = slot_ids[None, :] < channels[:, None]
    places = jnp.arange(groups, dtype=jnp.int32)
    pick = (montage[:, 0, None, :] == places[None, :, None]) & live_slots[:, None, :]
    rows = jnp.einsum(
        "bms,bst->mbt", pick.astype(jnp.bfloat16), signal, preferred_element_type=jnp.float32
    ).astype(jnp.bfloat16)
    patch_rows = rows.reshape(groups, recordings, patches, SAMP)
    first_taps = lax.all_gather(conv_in[:, 0], "rec", tiled=True)
    hidden_own = jnp.swapaxes(conv_hid[:, 0], 0, 1)
    hidden_taps = lax.all_to_all(
        jnp.broadcast_to(hidden_own, (hidden_own.shape[0], groups) + hidden_own.shape[2:]), "rec", 1, 1, tiled=True
    )
    extended = halo_rows(patch_rows, HALO)
    partial_value = conv_mix(extended, first_taps, hidden_taps, mix_weight[:, 0], rec_index, patches)
    spread = lax.axis_size("chan")
    pieces = partial_value.reshape(recordings, spread, patches // spread, partial_value.shape[-1])
    pieces = lax.all_to_all(jnp.swapaxes(pieces, 0, 1), "chan", 0, 0, tiled=True)
    summed = jnp.sum(pieces, axis=0)
    average = jnp.mean(summed, axis=-1, keepdims=True)
    centred = summed - average
    variance = jnp.mean(centred * centred, axis=-1, keepdims=True)
    activated = jax.nn.gelu(centred * lax.rsqrt(variance + EPSILON) * norm_gain)
    emission = jnp.einsum("bpo,os->bps", activated, emit_weight, precision=lax.Precision.HIGHEST)
    shared = lax.all_to_all(jnp.broadcast_to(emission[None], (spread,) + emission.shape), "chan", 0, 0, tiled=True)
    emission = jnp.swapaxes(shared, 0, 1).reshape(recordings, patches, STATES)
    positions = rec_index * patches + jnp.arange(patches, dtype=jnp.int32)
    valid = positions[None, :] < lengths[:, None]
    cross = boundary == 1
    filtered, log_partition = crf_forward(
        emission, cross, valid, trans_within, trans_between, initial, rec_index
    )
    return (filtered, log_partition / lengths.astype(jnp.float32))


def solution(mesh):
    placed = (
        P(None, "chan", "rec"),
        P(None, "chan", None),
        P(),
        P(),
        P(None, "rec"),
        P("rec", "chan", None, None, None),
        P("rec", "chan", None, None, None, None),
        P(None, "chan", None, None),
        P(),
        P(),
        P(),
        P(),
        P(),
    )
    return jax.shard_map(
        local, mesh=mesh, in_specs=placed, out_specs=(P(None, None, "rec"), P()), check_vma=False
    )
```

```python
import functools

import jax
import jax.numpy as jnp
from jax import lax
from jax.experimental import pallas as pl
from jax.experimental.pallas import tpu as pltpu
from jax.sharding import PartitionSpec as P

SAMP = 200
EMB = 128
STATES = 5


EPSILON = 1e-05
NEGATIVE = -1e30
MESH_SIDE = 4
HALO = 8


def log_sum_exp(values, along):
    peak_value = jnp.max(values, axis=along, keepdims=True)
    return jnp.squeeze(peak_value, along) + jnp.log(
        jnp.sum(jnp.exp(values - peak_value), axis=along)
    )


LANES = 128


def forward_step(state, matrices, extra):
    terms = [state[i : i + 1, :] + matrices[i] for i in range(len(matrices))]
    peak = functools.reduce(jnp.maximum, terms)
    total = functools.reduce(lambda x, y: x + y, [jnp.exp(t - peak) for t in terms])
    moved = peak + jnp.log(total)
    if extra is not None:
        moved = moved + extra
    top = jnp.max(moved, axis=0, keepdims=True)
    level = top + jnp.log(jnp.sum(jnp.exp(moved - top), axis=0, keepdims=True))
    return moved - level, level


def prefix_kernel(within_ref, between_ref, start_ref, emit_ref, cross_ref, valid_ref, prefix_ref, offset_ref):
    patches = emit_ref.shape[0]
    within = [within_ref[i] for i in range(STATES)]
    between = [between_ref[i] for i in range(STATES)]

    def body(p, carry):
        state, offset = carry
        crossing = cross_ref[p] > 0.5
        counted = valid_ref[p] > 0.5
        matrices = [jnp.where(crossing, between[i], within[i]) for i in range(STATES)]
        moved, level = forward_step(state, matrices, emit_ref[p])
        state = jnp.where(counted, moved, state)
        offset = offset + jnp.where(counted, level, 0.0)
        prefix_ref[p] = state
        offset_ref[p] = offset
        return state, offset

    lax.fori_loop(0, patches, body, (start_ref[...], jnp.zeros((1, LANES), jnp.float32)))


def chain_kernel(prior_ref, mats_ref, incoming_ref, total_ref):
    count = mats_ref.shape[0]

    def body(k, carry):
        state, total = carry
        incoming_ref[k] = state
        matrices = [mats_ref[k, j] for j in range(STATES)]
        moved, level = forward_step(state, matrices, None)
        return moved, total + level

    _, total = lax.fori_loop(0, count, body, (prior_ref[...], jnp.zeros((1, LANES), jnp.float32)))
    total_ref[...] = total


def lanes_padded(values):
    pad = [(0, 0)] * (values.ndim - 1) + [(0, LANES - values.shape[-1])]
    return jnp.pad(values, pad)


def crf_forward(emission, cross, valid, trans_within, trans_between, initial, rec_index):
    recordings, patches, _ = emission.shape
    width = STATES * recordings
    emit_in = lanes_padded(jnp.tile(jnp.transpose(emission, (1, 2, 0)), (1, 1, STATES)))
    cross_in = lanes_padded(jnp.tile(cross.T.astype(jnp.float32), (1, STATES)))[:, None, :]
    valid_in = lanes_padded(jnp.tile(valid.T.astype(jnp.float32), (1, STATES)))[:, None, :]
    lane_start = jnp.arange(width, dtype=jnp.int32) // recordings
    basis = jnp.arange(STATES, dtype=jnp.int32)[:, None] == lane_start[None, :]
    start = lanes_padded(jnp.where(basis, 0.0, NEGATIVE).astype(jnp.float32))
    within_in = jnp.broadcast_to(trans_within[:, :, None], (STATES, STATES, LANES))
    between_in = jnp.broadcast_to(trans_between[:, :, None], (STATES, STATES, LANES))
    prefix, offset = pl.pallas_call(
        prefix_kernel,
        out_shape=(
            jax.ShapeDtypeStruct((patches, STATES, LANES), jnp.float32),
            jax.ShapeDtypeStruct((patches, 1, LANES), jnp.float32),
        ),
        cost_estimate=pl.CostEstimate(
            flops=patches * 80 * LANES * 8, transcendentals=patches * 8 * LANES * 8,
            bytes_accessed=patches * 14 * LANES * 4,
        ),
    )(within_in, between_in, start, emit_in, cross_in, valid_in)
    prefix_sj = prefix[:, :, :width].reshape(patches, STATES, STATES, recordings)
    offset_j = offset[:, 0, :width].reshape(patches, STATES, recordings)
    transfer = prefix_sj[patches - 1] + offset_j[patches - 1][None]
    transfer = jnp.transpose(transfer, (1, 0, 2))
    gathered = torus_gather(transfer[None], rec_index, MESH_SIDE)
    mats = lanes_padded(gathered)
    prior = initial - log_sum_exp(initial, 0)
    prior_in = lanes_padded(jnp.broadcast_to(prior[:, None], (STATES, recordings)))
    groups = gathered.shape[0]
    incoming, total = pl.pallas_call(
        chain_kernel,
        out_shape=(
            jax.ShapeDtypeStruct((groups, STATES, LANES), jnp.float32),
            jax.ShapeDtypeStruct((1, LANES), jnp.float32),
        ),
    )(prior_in, mats)
    here = lax.dynamic_index_in_dim(incoming, rec_index, 0, keepdims=False)[:, :recordings]
    weights = here[None, None] + offset_j[:, None] + prefix_sj
    reached = log_sum_exp(weights, 2)
    totals = log_sum_exp(reached, 1)
    filtered = jnp.transpose(reached - totals[:, None], (2, 1, 0))
    return filtered, total[0, :recordings]


def neighbour_shift(block, axis, distance):
    devices = range(lax.axis_size(axis))
    route = [(i - distance, i) for i in devices if i - distance in devices]
    return lax.ppermute(block, axis, route)


def halo_rows(patch_rows, halo):
    patches = patch_rows.shape[2]
    from_left = neighbour_shift(patch_rows[:, :, patches - halo :], "rec", 1)
    from_right = neighbour_shift(patch_rows[:, :, :halo], "rec", -1)
    return jnp.concatenate([from_left, patch_rows, from_right], axis=2)

def rolled_taps(rows, weight_of, taps):
    reach = taps // 2
    count = rows.shape[0]
    accumulated = None
    for offset in range(taps):
        product = jnp.dot(rows, weight_of(offset), preferred_element_type=jnp.float32)
        shift = (reach - offset) % count
        if shift:
            product = pltpu.roll(product, shift, 0)
        accumulated = product if accumulated is None else accumulated + product
    return accumulated


def merged(ref):
    shape = ref.shape
    return ref[0].reshape(shape[1] * shape[2], shape[3])


def first_kernel(rows_ref, taps_ref, keep_ref, out_ref):
    value = jax.nn.gelu(rolled_taps(merged(rows_ref), lambda k: taps_ref[0, k], taps_ref.shape[1]))
    value = jnp.where(keep_ref[...] > 0.5, value.astype(jnp.bfloat16), jnp.zeros((), jnp.bfloat16))
    out_ref[0] = value.reshape(out_ref.shape[1:])


def residual_layer(current, taps_ref):
    update = jax.nn.gelu(rolled_taps(current, lambda k: taps_ref[0, 0, k], taps_ref.shape[2]))
    return (current.astype(jnp.float32) + update).astype(jnp.bfloat16)


def hidden_kernel(rows_ref, taps_ref, keep_ref, out_ref):
    value = residual_layer(merged(rows_ref), taps_ref)
    value = jnp.where(keep_ref[...] > 0.5, value, jnp.zeros((), jnp.bfloat16))
    out_ref[0] = value.reshape(out_ref.shape[1:])


def last_kernel(rows_ref, taps_ref, mix_ref, out_ref):
    @pl.when(pl.program_id(0) == 0)
    def _():
        out_ref[...] = jnp.zeros_like(out_ref)

    span = rows_ref.shape[2]
    recordings, patches = out_ref.shape[:2]
    margin = (span - patches) // 2
    value = residual_layer(merged(rows_ref), taps_ref)
    mixed = jnp.dot(value, mix_ref[0], preferred_element_type=jnp.float32)
    for item in range(recordings):
        start = item * span + margin
        out_ref[item] += mixed[start : start + patches]


def edge_keep(span, margin, rec_index, patches, recordings):
    total = patches * lax.axis_size("rec")
    spot = rec_index * patches - margin + jnp.arange(span, dtype=jnp.int32)
    keep = ((spot >= 0) & (spot < total)).astype(jnp.float32)
    return jnp.tile(jnp.broadcast_to(keep[:, None], (span, EMB)), (recordings, 1))


def per_type_call(kernel, rows, taps, side, out_block, out_shape, out_map, flops, layer=None):
    types, recordings = rows.shape[:2]
    side_spec = (
        pl.BlockSpec((1,) + side.shape[1:], lambda m: (m, 0, 0))
        if kernel is last_kernel
        else pl.BlockSpec(side.shape, lambda m: (0, 0))
    )
    return pl.pallas_call(
        kernel,
        grid=(types,),
        in_specs=[
            pl.BlockSpec((1,) + rows.shape[1:], lambda m: (m, 0, 0, 0)),
            pl.BlockSpec((1,) + taps.shape[1:], lambda m: (m, 0, 0, 0))
            if layer is None
            else pl.BlockSpec((1, 1) + taps.shape[2:], lambda m: (layer, m, 0, 0, 0)),
            side_spec,
        ],
        out_specs=pl.BlockSpec(out_block, out_map),
        out_shape=out_shape,
        compiler_params=pltpu.CompilerParams(dimension_semantics=("arbitrary",)),
        cost_estimate=pl.CostEstimate(
            flops=flops, transcendentals=rows.shape[0] * rows.shape[1] * rows.shape[2] * EMB,
            bytes_accessed=rows.size * 2 + taps.size * 2 // (1 if layer is None else taps.shape[0]) + side.size * 2 + out_shape.size * 4,
        ),
    )(rows, taps, side)


def conv_mix(extended, first_taps, hidden_taps, mix, rec_index, patches):
    types, recordings, span, width = extended.shape
    taps = first_taps.shape[1]
    layers = hidden_taps.shape[0]
    margin = (span - patches) // 2
    keep = edge_keep(span, margin, rec_index, patches, recordings)
    block = (1, recordings, span, EMB)
    inner = jax.ShapeDtypeStruct((types, recordings, span, EMB), jnp.bfloat16)
    current = per_type_call(
        first_kernel, extended, first_taps, keep, block, inner,
        lambda m: (m, 0, 0, 0), 2 * types * recordings * span * width * EMB * taps,
    )
    for depth_index in range(layers - 1):
        current = per_type_call(
            hidden_kernel, current, hidden_taps, keep, block, inner,
            lambda m: (m, 0, 0, 0), 2 * types * recordings * span * EMB * EMB * taps, depth_index,
        )
    mix_width = mix.shape[-1]
    return per_type_call(
        last_kernel, current, hidden_taps, mix,
        (recordings, patches, mix_width), jax.ShapeDtypeStruct((recordings, patches, mix_width), jnp.float32),
        lambda m: (0, 0, 0), 2 * types * recordings * span * EMB * (EMB * taps + mix_width), layers - 1,
    )


def torus_gather(block, rec_index, side):
    inner = rec_index % side
    outer = rec_index // side
    devices = side * side

    def shifted(values, step, stride):
        route = []
        for source in range(devices):
            row, col = source // side, source % side
            if stride == 1:
                target = row * side + (col + step) % side
            else:
                target = ((row + step) % side) * side + col
            route.append((source, target))
        return lax.ppermute(values, "rec", route)

    along = jnp.concatenate([block] + [shifted(block, step, 1) for step in range(1, side)], axis=0)
    whole = jnp.concatenate([along] + [shifted(along, step, side) for step in range(1, side)], axis=0)
    types = jnp.arange(devices, dtype=jnp.int32)
    position = ((outer - types // side) % side) * side + (inner - types % side) % side
    return jnp.take(whole, position, axis=0)


def local(
    signal,
    montage,
    channels,
    lengths,
    boundary,
    conv_in,
    conv_hid,
    mix_weight,
    norm_gain,
    emit_weight,
    trans_within,
    trans_between,
    initial,
):
    groups = lax.axis_size("rec")
    chan_index = lax.axis_index("chan")
    rec_index = lax.axis_index("rec")
    recordings = signal.shape[0]
    patches = signal.shape[2] // SAMP
    slot_ids = chan_index * groups + jnp.arange(groups, dtype=jnp.int32)
    live_slots = slot_ids[None, :] < channels[:, None]
    places = jnp.arange(groups, dtype=jnp.int32)
    pick = (montage[:, 0, None, :] == places[None, :, None]) & live_slots[:, None, :]
    rows = jnp.einsum(
        "bms,bst->mbt", pick.astype(jnp.bfloat16), signal, preferred_element_type=jnp.float32
    ).astype(jnp.bfloat16)
    patch_rows = rows.reshape(groups, recordings, patches, SAMP)
    first_taps = lax.all_gather(conv_in[:, 0], "rec", tiled=True)
    hidden_taps = lax.all_gather(jnp.swapaxes(conv_hid[:, 0], 0, 1), "rec", axis=1, tiled=True)
    extended = halo_rows(patch_rows, HALO)
    partial_value = conv_mix(extended, first_taps, hidden_taps, mix_weight[:, 0], rec_index, patches)
    spread = lax.axis_size("chan")
    pieces = partial_value.reshape(recordings, spread, patches // spread, partial_value.shape[-1])
    pieces = lax.all_to_all(jnp.swapaxes(pieces, 0, 1), "chan", 0, 0, tiled=True)
    summed = jnp.sum(pieces, axis=0)
    average = jnp.mean(summed, axis=-1, keepdims=True)
    centred = summed - average
    variance = jnp.mean(centred * centred, axis=-1, keepdims=True)
    activated = jax.nn.gelu(centred * lax.rsqrt(variance + EPSILON) * norm_gain)
    emission = jnp.einsum("bpo,os->bps", activated, emit_weight, precision=lax.Precision.HIGHEST)
    shared = lax.all_to_all(jnp.broadcast_to(emission[None], (spread,) + emission.shape), "chan", 0, 0, tiled=True)
    emission = jnp.swapaxes(shared, 0, 1).reshape(recordings, patches, STATES)
    positions = rec_index * patches + jnp.arange(patches, dtype=jnp.int32)
    valid = positions[None, :] < lengths[:, None]
    cross = boundary == 1
    filtered, log_partition = crf_forward(
        emission, cross, valid, trans_within, trans_between, initial, rec_index
    )
    return (filtered, log_partition / lengths.astype(jnp.float32))


def solution(mesh):
    placed = (
        P(None, "chan", "rec"),
        P(None, "chan", None),
        P(),
        P(),
        P(None, "rec"),
        P("rec", "chan", None, None, None),
        P("rec", "chan", None, None, None, None),
        P(None, "chan", None, None),
        P(),
        P(),
        P(),
        P(),
        P(),
    )
    return jax.shard_map(
        local, mesh=mesh, in_specs=placed, out_specs=(P(None, None, "rec"), P()), check_vma=False
    )
```

```python
import functools

import jax
import jax.numpy as jnp
from jax import lax
from jax.experimental import pallas as pl
from jax.experimental.pallas import tpu as pltpu
from jax.sharding import PartitionSpec as P

SAMP = 200
EMB = 128
STATES = 5


EPSILON = 1e-05
NEGATIVE = -1e30
MESH_SIDE = 4
HALO = 8


def log_sum_exp(values, along):
    peak_value = jnp.max(values, axis=along, keepdims=True)
    return jnp.squeeze(peak_value, along) + jnp.log(
        jnp.sum(jnp.exp(values - peak_value), axis=along)
    )


LANES = 128


def forward_step(state, matrices, extra):
    terms = [state[i : i + 1, :] + matrices[i] for i in range(len(matrices))]
    peak = functools.reduce(jnp.maximum, terms)
    total = functools.reduce(lambda x, y: x + y, [jnp.exp(t - peak) for t in terms])
    moved = peak + jnp.log(total)
    if extra is not None:
        moved = moved + extra
    top = jnp.max(moved, axis=0, keepdims=True)
    level = top + jnp.log(jnp.sum(jnp.exp(moved - top), axis=0, keepdims=True))
    return moved - level, level


def prefix_kernel(within_ref, between_ref, start_ref, emit_ref, cross_ref, valid_ref, prefix_ref, offset_ref):
    patches = emit_ref.shape[0]
    within = [within_ref[i] for i in range(STATES)]
    between = [between_ref[i] for i in range(STATES)]

    def body(p, carry):
        state, offset = carry
        crossing = cross_ref[p] > 0.5
        counted = valid_ref[p] > 0.5
        matrices = [jnp.where(crossing, between[i], within[i]) for i in range(STATES)]
        moved, level = forward_step(state, matrices, emit_ref[p])
        state = jnp.where(counted, moved, state)
        offset = offset + jnp.where(counted, level, 0.0)
        prefix_ref[p] = state
        offset_ref[p] = offset
        return state, offset

    lax.fori_loop(0, patches, body, (start_ref[...], jnp.zeros((1, LANES), jnp.float32)))


def chain_kernel(prior_ref, mats_ref, incoming_ref, total_ref):
    count = mats_ref.shape[0]

    def body(k, carry):
        state, total = carry
        incoming_ref[k] = state
        matrices = [mats_ref[k, j] for j in range(STATES)]
        moved, level = forward_step(state, matrices, None)
        return moved, total + level

    _, total = lax.fori_loop(0, count, body, (prior_ref[...], jnp.zeros((1, LANES), jnp.float32)))
    total_ref[...] = total


def lanes_padded(values):
    pad = [(0, 0)] * (values.ndim - 1) + [(0, LANES - values.shape[-1])]
    return jnp.pad(values, pad)


def crf_forward(emission, cross, valid, trans_within, trans_between, initial, rec_index):
    recordings, patches, _ = emission.shape
    width = STATES * recordings
    emit_in = lanes_padded(jnp.tile(jnp.transpose(emission, (1, 2, 0)), (1, 1, STATES)))
    cross_in = lanes_padded(jnp.tile(cross.T.astype(jnp.float32), (1, STATES)))[:, None, :]
    valid_in = lanes_padded(jnp.tile(valid.T.astype(jnp.float32), (1, STATES)))[:, None, :]
    lane_start = jnp.arange(width, dtype=jnp.int32) // recordings
    basis = jnp.arange(STATES, dtype=jnp.int32)[:, None] == lane_start[None, :]
    start = lanes_padded(jnp.where(basis, 0.0, NEGATIVE).astype(jnp.float32))
    within_in = jnp.broadcast_to(trans_within[:, :, None], (STATES, STATES, LANES))
    between_in = jnp.broadcast_to(trans_between[:, :, None], (STATES, STATES, LANES))
    prefix, offset = pl.pallas_call(
        prefix_kernel,
        out_shape=(
            jax.ShapeDtypeStruct((patches, STATES, LANES), jnp.float32),
            jax.ShapeDtypeStruct((patches, 1, LANES), jnp.float32),
        ),
        cost_estimate=pl.CostEstimate(
            flops=patches * 80 * LANES * 8, transcendentals=patches * 8 * LANES * 8,
            bytes_accessed=patches * 14 * LANES * 4,
        ),
    )(within_in, between_in, start, emit_in, cross_in, valid_in)
    prefix_sj = prefix[:, :, :width].reshape(patches, STATES, STATES, recordings)
    offset_j = offset[:, 0, :width].reshape(patches, STATES, recordings)
    transfer = prefix_sj[patches - 1] + offset_j[patches - 1][None]
    transfer = jnp.transpose(transfer, (1, 0, 2))
    gathered = torus_gather(transfer[None], rec_index, MESH_SIDE)
    mats = lanes_padded(gathered)
    prior = initial - log_sum_exp(initial, 0)
    prior_in = lanes_padded(jnp.broadcast_to(prior[:, None], (STATES, recordings)))
    groups = gathered.shape[0]
    incoming, total = pl.pallas_call(
        chain_kernel,
        out_shape=(
            jax.ShapeDtypeStruct((groups, STATES, LANES), jnp.float32),
            jax.ShapeDtypeStruct((1, LANES), jnp.float32),
        ),
    )(prior_in, mats)
    here = lax.dynamic_index_in_dim(incoming, rec_index, 0, keepdims=False)[:, :recordings]
    weights = here[None, None] + offset_j[:, None] + prefix_sj
    reached = log_sum_exp(weights, 2)
    totals = log_sum_exp(reached, 1)
    filtered = jnp.transpose(reached - totals[:, None], (2, 1, 0))
    return filtered, total[0, :recordings]


def neighbour_shift(block, axis, distance):
    devices = range(lax.axis_size(axis))
    route = [(i - distance, i) for i in devices if i - distance in devices]
    return lax.ppermute(block, axis, route)


def halo_rows(patch_rows, halo):
    patches = patch_rows.shape[2]
    from_left = neighbour_shift(patch_rows[:, :, patches - halo :], "rec", 1)
    from_right = neighbour_shift(patch_rows[:, :, :halo], "rec", -1)
    return jnp.concatenate([from_left, patch_rows, from_right], axis=2)

def rolled_taps(rows, weight_of, taps):
    reach = taps // 2
    count = rows.shape[0]
    accumulated = None
    for offset in range(taps):
        product = jnp.dot(rows, weight_of(offset), preferred_element_type=jnp.float32)
        shift = (reach - offset) % count
        if shift:
            product = pltpu.roll(product, shift, 0)
        accumulated = product if accumulated is None else accumulated + product
    return accumulated


def merged(ref):
    shape = ref.shape
    return ref[0].reshape(shape[1] * shape[2], shape[3])


def first_kernel(rows_ref, taps_ref, keep_ref, out_ref):
    value = jax.nn.gelu(rolled_taps(merged(rows_ref), lambda k: taps_ref[0, k], taps_ref.shape[1]))
    value = jnp.where(keep_ref[...] > 0.5, value.astype(jnp.bfloat16), jnp.zeros((), jnp.bfloat16))
    out_ref[0] = value.reshape(out_ref.shape[1:])


def residual_layer(current, taps_ref):
    update = jax.nn.gelu(rolled_taps(current, lambda k: taps_ref[0, 0, k], taps_ref.shape[2]))
    return (current.astype(jnp.float32) + update).astype(jnp.bfloat16)


def hidden_kernel(rows_ref, taps_ref, keep_ref, out_ref):
    value = residual_layer(merged(rows_ref), taps_ref)
    value = jnp.where(keep_ref[...] > 0.5, value, jnp.zeros((), jnp.bfloat16))
    out_ref[0] = value.reshape(out_ref.shape[1:])


def last_kernel(rows_ref, taps_ref, mix_ref, out_ref):
    @pl.when(pl.program_id(0) == 0)
    def _():
        out_ref[...] = jnp.zeros_like(out_ref)

    span = rows_ref.shape[2]
    recordings, patches = out_ref.shape[:2]
    margin = (span - patches) // 2
    value = residual_layer(merged(rows_ref), taps_ref)
    mixed = jnp.dot(value, mix_ref[0], preferred_element_type=jnp.float32)
    for item in range(recordings):
        start = item * span + margin
        out_ref[item] += mixed[start : start + patches]


def edge_keep(span, margin, rec_index, patches, recordings):
    total = patches * lax.axis_size("rec")
    spot = rec_index * patches - margin + jnp.arange(span, dtype=jnp.int32)
    keep = ((spot >= 0) & (spot < total)).astype(jnp.float32)
    return jnp.tile(jnp.broadcast_to(keep[:, None], (span, EMB)), (recordings, 1))


def per_type_call(kernel, rows, taps, side, out_block, out_shape, out_map, flops, layer=None, part=None):
    types, recordings = rows.shape[:2]
    rows_spec = pl.BlockSpec((1,) + rows.shape[1:], lambda m: (m, 0, 0, 0))
    if part is not None:
        count = out_block[0]
        rows_spec = pl.BlockSpec((1, count) + rows.shape[2:], lambda m: (m, part, 0, 0))
    side_spec = (
        pl.BlockSpec((1,) + side.shape[1:], lambda m: (m, 0, 0))
        if kernel is last_kernel
        else pl.BlockSpec(side.shape, lambda m: (0, 0))
    )
    return pl.pallas_call(
        kernel,
        grid=(types,),
        in_specs=[
            rows_spec,
            pl.BlockSpec((1,) + taps.shape[1:], lambda m: (m, 0, 0, 0))
            if layer is None
            else pl.BlockSpec((1, 1) + taps.shape[2:], lambda m: (layer, m, 0, 0, 0)),
            side_spec,
        ],
        out_specs=pl.BlockSpec(out_block, out_map),
        out_shape=out_shape,
        compiler_params=pltpu.CompilerParams(dimension_semantics=("arbitrary",)),
        cost_estimate=pl.CostEstimate(
            flops=flops, transcendentals=rows.shape[0] * rows.shape[1] * rows.shape[2] * EMB,
            bytes_accessed=rows.size * 2 + taps.size * 2 // (1 if layer is None else taps.shape[0]) + side.size * 2 + out_shape.size * 4,
        ),
    )(rows, taps, side)


def conv_mix(extended, first_taps, hidden_taps, mix, rec_index, patches):
    types, recordings, span, width = extended.shape
    taps = first_taps.shape[1]
    layers = hidden_taps.shape[0]
    margin = (span - patches) // 2
    keep = edge_keep(span, margin, rec_index, patches, recordings)
    block = (1, recordings, span, EMB)
    inner = jax.ShapeDtypeStruct((types, recordings, span, EMB), jnp.bfloat16)
    current = per_type_call(
        first_kernel, extended, first_taps, keep, block, inner,
        lambda m: (m, 0, 0, 0), 2 * types * recordings * span * width * EMB * taps,
    )
    for depth_index in range(layers - 1):
        current = per_type_call(
            hidden_kernel, current, hidden_taps, keep, block, inner,
            lambda m: (m, 0, 0, 0), 2 * types * recordings * span * EMB * EMB * taps, depth_index,
        )
    mix_width = mix.shape[-1]
    halves = 2
    count = recordings // halves
    return [
        per_type_call(
            last_kernel, current, hidden_taps, mix,
            (count, patches, mix_width), jax.ShapeDtypeStruct((count, patches, mix_width), jnp.float32),
            lambda m: (0, 0, 0), 2 * types * count * span * EMB * (EMB * taps + mix_width), layers - 1, half,
        )
        for half in range(halves)
    ]

def torus_gather(block, rec_index, side):
    inner = rec_index % side
    outer = rec_index // side
    devices = side * side

    def shifted(values, step, stride):
        route = []
        for source in range(devices):
            row, col = source // side, source % side
            if stride == 1:
                target = row * side + (col + step) % side
            else:
                target = ((row + step) % side) * side + col
            route.append((source, target))
        return lax.ppermute(values, "rec", route)

    along = jnp.concatenate([block] + [shifted(block, step, 1) for step in range(1, side)], axis=0)
    whole = jnp.concatenate([along] + [shifted(along, step, side) for step in range(1, side)], axis=0)
    types = jnp.arange(devices, dtype=jnp.int32)
    position = ((outer - types // side) % side) * side + (inner - types % side) % side
    return jnp.take(whole, position, axis=0)


def local(
    signal,
    montage,
    channels,
    lengths,
    boundary,
    conv_in,
    conv_hid,
    mix_weight,
    norm_gain,
    emit_weight,
    trans_within,
    trans_between,
    initial,
):
    groups = lax.axis_size("rec")
    chan_index = lax.axis_index("chan")
    rec_index = lax.axis_index("rec")
    recordings = signal.shape[0]
    patches = signal.shape[2] // SAMP
    slot_ids = chan_index * groups + jnp.arange(groups, dtype=jnp.int32)
    live_slots = slot_ids[None, :] < channels[:, None]
    places = jnp.arange(groups, dtype=jnp.int32)
    pick = (montage[:, 0, None, :] == places[None, :, None]) & live_slots[:, None, :]
    rows = jnp.einsum(
        "bms,bst->mbt", pick.astype(jnp.bfloat16), signal, preferred_element_type=jnp.float32
    ).astype(jnp.bfloat16)
    patch_rows = rows.reshape(groups, recordings, patches, SAMP)
    first_taps = lax.all_gather(conv_in[:, 0], "rec", tiled=True)
    hidden_taps = lax.all_gather(jnp.swapaxes(conv_hid[:, 0], 0, 1), "rec", axis=1, tiled=True)
    extended = halo_rows(patch_rows, HALO)
    partial_value = conv_mix(extended, first_taps, hidden_taps, mix_weight[:, 0], rec_index, patches)
    spread = lax.axis_size("chan")
    emissions = []
    for part_value in partial_value:
        count = part_value.shape[0]
        pieces = part_value.reshape(count, spread, patches // spread, part_value.shape[-1])
        pieces = lax.all_to_all(jnp.swapaxes(pieces, 0, 1), "chan", 0, 0, tiled=True)
        summed = jnp.sum(pieces, axis=0)
        average = jnp.mean(summed, axis=-1, keepdims=True)
        centred = summed - average
        variance = jnp.mean(centred * centred, axis=-1, keepdims=True)
        activated = jax.nn.gelu(centred * lax.rsqrt(variance + EPSILON) * norm_gain)
        emissions.append(jnp.einsum("bpo,os->bps", activated, emit_weight, precision=lax.Precision.HIGHEST))
    emission = jnp.concatenate(emissions, axis=0)
    shared = lax.all_to_all(jnp.broadcast_to(emission[None], (spread,) + emission.shape), "chan", 0, 0, tiled=True)
    emission = jnp.swapaxes(shared, 0, 1).reshape(recordings, patches, STATES)
    positions = rec_index * patches + jnp.arange(patches, dtype=jnp.int32)
    valid = positions[None, :] < lengths[:, None]
    cross = boundary == 1
    filtered, log_partition = crf_forward(
        emission, cross, valid, trans_within, trans_between, initial, rec_index
    )
    return (filtered, log_partition / lengths.astype(jnp.float32))


def solution(mesh):
    placed = (
        P(None, "chan", "rec"),
        P(None, "chan", None),
        P(),
        P(),
        P(None, "rec"),
        P("rec", "chan", None, None, None),
        P("rec", "chan", None, None, None, None),
        P(None, "chan", None, None),
        P(),
        P(),
        P(),
        P(),
        P(),
    )
    return jax.shard_map(
        local, mesh=mesh, in_specs=placed, out_specs=(P(None, None, "rec"), P()), check_vma=False
    )
```

```python
import functools

import jax
import jax.numpy as jnp
from jax import lax
from jax.experimental import pallas as pl
from jax.experimental.pallas import tpu as pltpu
from jax.sharding import PartitionSpec as P

SAMP = 200
EMB = 128
STATES = 5


EPSILON = 1e-05
NEGATIVE = -1e30
MESH_SIDE = 4
HALO = 8


def log_sum_exp(values, along):
    peak_value = jnp.max(values, axis=along, keepdims=True)
    return jnp.squeeze(peak_value, along) + jnp.log(
        jnp.sum(jnp.exp(values - peak_value), axis=along)
    )


LANES = 128


def forward_step(state, matrices, extra):
    terms = [state[i : i + 1, :] + matrices[i] for i in range(len(matrices))]
    peak = functools.reduce(jnp.maximum, terms)
    total = functools.reduce(lambda x, y: x + y, [jnp.exp(t - peak) for t in terms])
    moved = peak + jnp.log(total)
    if extra is not None:
        moved = moved + extra
    top = jnp.max(moved, axis=0, keepdims=True)
    level = top + jnp.log(jnp.sum(jnp.exp(moved - top), axis=0, keepdims=True))
    return moved - level, level


def prefix_kernel(within_ref, between_ref, start_ref, emit_ref, cross_ref, valid_ref, prefix_ref, offset_ref):
    patches = emit_ref.shape[0]
    within = [within_ref[i] for i in range(STATES)]
    between = [between_ref[i] for i in range(STATES)]

    def body(p, carry):
        state, offset = carry
        crossing = cross_ref[p] > 0.5
        counted = valid_ref[p] > 0.5
        matrices = [jnp.where(crossing, between[i], within[i]) for i in range(STATES)]
        moved, level = forward_step(state, matrices, emit_ref[p])
        state = jnp.where(counted, moved, state)
        offset = offset + jnp.where(counted, level, 0.0)
        prefix_ref[p] = state
        offset_ref[p] = offset
        return state, offset

    lax.fori_loop(0, patches, body, (start_ref[...], jnp.zeros((1, LANES), jnp.float32)), unroll=8)


def chain_kernel(prior_ref, mats_ref, incoming_ref, total_ref):
    count = mats_ref.shape[0]

    def body(k, carry):
        state, total = carry
        incoming_ref[k] = state
        matrices = [mats_ref[k, j] for j in range(STATES)]
        moved, level = forward_step(state, matrices, None)
        return moved, total + level

    _, total = lax.fori_loop(0, count, body, (prior_ref[...], jnp.zeros((1, LANES), jnp.float32)))
    total_ref[...] = total


def lanes_padded(values):
    pad = [(0, 0)] * (values.ndim - 1) + [(0, LANES - values.shape[-1])]
    return jnp.pad(values, pad)


def crf_forward(emission, cross, valid, trans_within, trans_between, initial, rec_index):
    recordings, patches, _ = emission.shape
    width = STATES * recordings
    emit_in = lanes_padded(jnp.tile(jnp.transpose(emission, (1, 2, 0)), (1, 1, STATES)))
    cross_in = lanes_padded(jnp.tile(cross.T.astype(jnp.float32), (1, STATES)))[:, None, :]
    valid_in = lanes_padded(jnp.tile(valid.T.astype(jnp.float32), (1, STATES)))[:, None, :]
    lane_start = jnp.arange(width, dtype=jnp.int32) // recordings
    basis = jnp.arange(STATES, dtype=jnp.int32)[:, None] == lane_start[None, :]
    start = lanes_padded(jnp.where(basis, 0.0, NEGATIVE).astype(jnp.float32))
    within_in = jnp.broadcast_to(trans_within[:, :, None], (STATES, STATES, LANES))
    between_in = jnp.broadcast_to(trans_between[:, :, None], (STATES, STATES, LANES))
    prefix, offset = pl.pallas_call(
        prefix_kernel,
        out_shape=(
            jax.ShapeDtypeStruct((patches, STATES, LANES), jnp.float32),
            jax.ShapeDtypeStruct((patches, 1, LANES), jnp.float32),
        ),
        cost_estimate=pl.CostEstimate(
            flops=patches * 80 * LANES * 8, transcendentals=patches * 8 * LANES * 8,
            bytes_accessed=patches * 14 * LANES * 4,
        ),
    )(within_in, between_in, start, emit_in, cross_in, valid_in)
    prefix_sj = prefix[:, :, :width].reshape(patches, STATES, STATES, recordings)
    offset_j = offset[:, 0, :width].reshape(patches, STATES, recordings)
    transfer = prefix_sj[patches - 1] + offset_j[patches - 1][None]
    transfer = jnp.transpose(transfer, (1, 0, 2))
    gathered = torus_gather(transfer[None], rec_index, MESH_SIDE)
    mats = lanes_padded(gathered)
    prior = initial - log_sum_exp(initial, 0)
    prior_in = lanes_padded(jnp.broadcast_to(prior[:, None], (STATES, recordings)))
    groups = gathered.shape[0]
    incoming, total = pl.pallas_call(
        chain_kernel,
        out_shape=(
            jax.ShapeDtypeStruct((groups, STATES, LANES), jnp.float32),
            jax.ShapeDtypeStruct((1, LANES), jnp.float32),
        ),
    )(prior_in, mats)
    here = lax.dynamic_index_in_dim(incoming, rec_index, 0, keepdims=False)[:, :recordings]
    weights = here[None, None] + offset_j[:, None] + prefix_sj
    reached = log_sum_exp(weights, 2)
    totals = log_sum_exp(reached, 1)
    filtered = jnp.transpose(reached - totals[:, None], (2, 1, 0))
    return filtered, total[0, :recordings]


def neighbour_shift(block, axis, distance):
    devices = range(lax.axis_size(axis))
    route = [(i - distance, i) for i in devices if i - distance in devices]
    return lax.ppermute(block, axis, route)


def halo_rows(patch_rows, halo):
    patches = patch_rows.shape[2]
    from_left = neighbour_shift(patch_rows[:, :, patches - halo :], "rec", 1)
    from_right = neighbour_shift(patch_rows[:, :, :halo], "rec", -1)
    return jnp.concatenate([from_left, patch_rows, from_right], axis=2)

def rolled_taps(rows, weight_of, taps):
    reach = taps // 2
    count = rows.shape[0]
    accumulated = None
    for offset in range(taps):
        product = jnp.dot(rows, weight_of(offset), preferred_element_type=jnp.float32)
        shift = (reach - offset) % count
        if shift:
            product = pltpu.roll(product, shift, 0)
        accumulated = product if accumulated is None else accumulated + product
    return accumulated


def merged(ref):
    shape = ref.shape
    return ref[0].reshape(shape[1] * shape[2], shape[3])


def first_kernel(rows_ref, taps_ref, keep_ref, out_ref):
    value = jax.nn.gelu(rolled_taps(merged(rows_ref), lambda k: taps_ref[0, k], taps_ref.shape[1]))
    value = jnp.where(keep_ref[...] > 0.5, value.astype(jnp.bfloat16), jnp.zeros((), jnp.bfloat16))
    out_ref[0] = value.reshape(out_ref.shape[1:])


def residual_layer(current, taps_ref):
    update = jax.nn.gelu(rolled_taps(current, lambda k: taps_ref[0, 0, k], taps_ref.shape[2]))
    return (current.astype(jnp.float32) + update).astype(jnp.bfloat16)


def hidden_kernel(rows_ref, taps_ref, keep_ref, out_ref):
    value = residual_layer(merged(rows_ref), taps_ref)
    value = jnp.where(keep_ref[...] > 0.5, value, jnp.zeros((), jnp.bfloat16))
    out_ref[0] = value.reshape(out_ref.shape[1:])


def last_kernel(rows_ref, taps_ref, mix_ref, out_ref):
    @pl.when(pl.program_id(0) == 0)
    def _():
        out_ref[...] = jnp.zeros_like(out_ref)

    span = rows_ref.shape[2]
    recordings, patches = out_ref.shape[:2]
    margin = (span - patches) // 2
    value = residual_layer(merged(rows_ref), taps_ref)
    mixed = jnp.dot(value, mix_ref[0], preferred_element_type=jnp.float32)
    for item in range(recordings):
        start = item * span + margin
        out_ref[item] += mixed[start : start + patches]


def edge_keep(span, margin, rec_index, patches, recordings):
    total = patches * lax.axis_size("rec")
    spot = rec_index * patches - margin + jnp.arange(span, dtype=jnp.int32)
    keep = ((spot >= 0) & (spot < total)).astype(jnp.float32)
    return jnp.tile(jnp.broadcast_to(keep[:, None], (span, EMB)), (recordings, 1))


def per_type_call(kernel, rows, taps, side, out_block, out_shape, out_map, flops, layer=None):
    types, recordings = rows.shape[:2]
    side_spec = (
        pl.BlockSpec((1,) + side.shape[1:], lambda m: (m, 0, 0))
        if kernel is last_kernel
        else pl.BlockSpec(side.shape, lambda m: (0, 0))
    )
    return pl.pallas_call(
        kernel,
        grid=(types,),
        in_specs=[
            pl.BlockSpec((1,) + rows.shape[1:], lambda m: (m, 0, 0, 0)),
            pl.BlockSpec((1,) + taps.shape[1:], lambda m: (m, 0, 0, 0))
            if layer is None
            else pl.BlockSpec((1, 1) + taps.shape[2:], lambda m: (layer, m, 0, 0, 0)),
            side_spec,
        ],
        out_specs=pl.BlockSpec(out_block, out_map),
        out_shape=out_shape,
        compiler_params=pltpu.CompilerParams(dimension_semantics=("arbitrary",)),
        cost_estimate=pl.CostEstimate(
            flops=flops, transcendentals=rows.shape[0] * rows.shape[1] * rows.shape[2] * EMB,
            bytes_accessed=rows.size * 2 + taps.size * 2 // (1 if layer is None else taps.shape[0]) + side.size * 2 + out_shape.size * 4,
        ),
    )(rows, taps, side)


def conv_mix(extended, first_taps, hidden_taps, mix, rec_index, patches):
    types, recordings, span, width = extended.shape
    taps = first_taps.shape[1]
    layers = hidden_taps.shape[0]
    margin = (span - patches) // 2
    keep = edge_keep(span, margin, rec_index, patches, recordings)
    block = (1, recordings, span, EMB)
    inner = jax.ShapeDtypeStruct((types, recordings, span, EMB), jnp.bfloat16)
    current = per_type_call(
        first_kernel, extended, first_taps, keep, block, inner,
        lambda m: (m, 0, 0, 0), 2 * types * recordings * span * width * EMB * taps,
    )
    for depth_index in range(layers - 1):
        current = per_type_call(
            hidden_kernel, current, hidden_taps, keep, block, inner,
            lambda m: (m, 0, 0, 0), 2 * types * recordings * span * EMB * EMB * taps, depth_index,
        )
    mix_width = mix.shape[-1]
    return per_type_call(
        last_kernel, current, hidden_taps, mix,
        (recordings, patches, mix_width), jax.ShapeDtypeStruct((recordings, patches, mix_width), jnp.float32),
        lambda m: (0, 0, 0), 2 * types * recordings * span * EMB * (EMB * taps + mix_width), layers - 1,
    )


def torus_gather(block, rec_index, side):
    inner = rec_index % side
    outer = rec_index // side
    devices = side * side

    def shifted(values, step, stride):
        route = []
        for source in range(devices):
            row, col = source // side, source % side
            if stride == 1:
                target = row * side + (col + step) % side
            else:
                target = ((row + step) % side) * side + col
            route.append((source, target))
        return lax.ppermute(values, "rec", route)

    along = jnp.concatenate([block] + [shifted(block, step, 1) for step in range(1, side)], axis=0)
    whole = jnp.concatenate([along] + [shifted(along, step, side) for step in range(1, side)], axis=0)
    types = jnp.arange(devices, dtype=jnp.int32)
    position = ((outer - types // side) % side) * side + (inner - types % side) % side
    return jnp.take(whole, position, axis=0)


def local(
    signal,
    montage,
    channels,
    lengths,
    boundary,
    conv_in,
    conv_hid,
    mix_weight,
    norm_gain,
    emit_weight,
    trans_within,
    trans_between,
    initial,
):
    groups = lax.axis_size("rec")
    chan_index = lax.axis_index("chan")
    rec_index = lax.axis_index("rec")
    recordings = signal.shape[0]
    patches = signal.shape[2] // SAMP
    slot_ids = chan_index * groups + jnp.arange(groups, dtype=jnp.int32)
    live_slots = slot_ids[None, :] < channels[:, None]
    places = jnp.arange(groups, dtype=jnp.int32)
    pick = (montage[:, 0, None, :] == places[None, :, None]) & live_slots[:, None, :]
    rows = jnp.einsum(
        "bms,bst->mbt", pick.astype(jnp.bfloat16), signal, preferred_element_type=jnp.float32
    ).astype(jnp.bfloat16)
    patch_rows = rows.reshape(groups, recordings, patches, SAMP)
    first_taps = lax.all_gather(conv_in[:, 0], "rec", tiled=True)
    hidden_taps = lax.all_gather(jnp.swapaxes(conv_hid[:, 0], 0, 1), "rec", axis=1, tiled=True)
    extended = halo_rows(patch_rows, HALO)
    partial_value = conv_mix(extended, first_taps, hidden_taps, mix_weight[:, 0], rec_index, patches)
    spread = lax.axis_size("chan")
    pieces = partial_value.reshape(recordings, spread, patches // spread, partial_value.shape[-1])
    pieces = lax.all_to_all(jnp.swapaxes(pieces, 0, 1), "chan", 0, 0, tiled=True)
    summed = jnp.sum(pieces, axis=0)
    average = jnp.mean(summed, axis=-1, keepdims=True)
    centred = summed - average
    variance = jnp.mean(centred * centred, axis=-1, keepdims=True)
    activated = jax.nn.gelu(centred * lax.rsqrt(variance + EPSILON) * norm_gain)
    emission = jnp.einsum("bpo,os->bps", activated, emit_weight, precision=lax.Precision.HIGHEST)
    shared = lax.all_to_all(jnp.broadcast_to(emission[None], (spread,) + emission.shape), "chan", 0, 0, tiled=True)
    emission = jnp.swapaxes(shared, 0, 1).reshape(recordings, patches, STATES)
    positions = rec_index * patches + jnp.arange(patches, dtype=jnp.int32)
    valid = positions[None, :] < lengths[:, None]
    cross = boundary == 1
    filtered, log_partition = crf_forward(
        emission, cross, valid, trans_within, trans_between, initial, rec_index
    )
    return (filtered, log_partition / lengths.astype(jnp.float32))


def solution(mesh):
    placed = (
        P(None, "chan", "rec"),
        P(None, "chan", None),
        P(),
        P(),
        P(None, "rec"),
        P("rec", "chan", None, None, None),
        P("rec", "chan", None, None, None, None),
        P(None, "chan", None, None),
        P(),
        P(),
        P(),
        P(),
        P(),
    )
    return jax.shard_map(
        local, mesh=mesh, in_specs=placed, out_specs=(P(None, None, "rec"), P()), check_vma=False
    )
```

```python
import functools

import jax
import jax.numpy as jnp
from jax import lax
from jax.experimental import pallas as pl
from jax.experimental.pallas import tpu as pltpu
from jax.sharding import PartitionSpec as P

SAMP = 200
EMB = 128
STATES = 5


EPSILON = 1e-05
NEGATIVE = -1e30
MESH_SIDE = 4
SUBSHARDS = 4
HALO = 8


def log_sum_exp(values, along):
    peak_value = jnp.max(values, axis=along, keepdims=True)
    return jnp.squeeze(peak_value, along) + jnp.log(
        jnp.sum(jnp.exp(values - peak_value), axis=along)
    )


LANES = 128


def forward_step(state, matrices, extra):
    terms = [state[i : i + 1, :] + matrices[i] for i in range(len(matrices))]
    peak = functools.reduce(jnp.maximum, terms)
    total = functools.reduce(lambda x, y: x + y, [jnp.exp(t - peak) for t in terms])
    moved = peak + jnp.log(total)
    if extra is not None:
        moved = moved + extra
    top = jnp.max(moved, axis=0, keepdims=True)
    level = top + jnp.log(jnp.sum(jnp.exp(moved - top), axis=0, keepdims=True))
    return moved - level, level


def prefix_kernel(within_ref, between_ref, start_ref, emit_ref, cross_ref, valid_ref, prefix_ref, offset_ref):
    patches = emit_ref.shape[0]
    within = [within_ref[i] for i in range(STATES)]
    between = [between_ref[i] for i in range(STATES)]

    def body(p, carry):
        state, offset = carry
        crossing = cross_ref[p] > 0.5
        counted = valid_ref[p] > 0.5
        matrices = [jnp.where(crossing, between[i], within[i]) for i in range(STATES)]
        moved, level = forward_step(state, matrices, emit_ref[p])
        state = jnp.where(counted, moved, state)
        offset = offset + jnp.where(counted, level, 0.0)
        prefix_ref[p] = state
        offset_ref[p] = offset
        return state, offset

    lax.fori_loop(0, patches, body, (start_ref[...], jnp.zeros((1, LANES), jnp.float32)), unroll=8)


def chain_kernel(prior_ref, mats_ref, incoming_ref, total_ref):
    count = mats_ref.shape[0]

    def body(k, carry):
        state, total = carry
        incoming_ref[k] = state
        matrices = [mats_ref[k, j] for j in range(STATES)]
        moved, level = forward_step(state, matrices, None)
        return moved, total + level

    _, total = lax.fori_loop(0, count, body, (prior_ref[...], jnp.zeros((1, LANES), jnp.float32)))
    total_ref[...] = total


def lanes_padded(values):
    pad = [(0, 0)] * (values.ndim - 1) + [(0, LANES - values.shape[-1])]
    return jnp.pad(values, pad)


def crf_forward(emission, cross, valid, trans_within, trans_between, initial, rec_index):
    recordings, patches, _ = emission.shape
    pieces = SUBSHARDS
    steps = patches // pieces
    block = STATES * recordings
    width = pieces * block

    def to_lanes(values):
        split = values.reshape((recordings, pieces, steps) + values.shape[2:])
        order = (2,) + tuple(range(3, split.ndim)) + (1, 0)
        moved = jnp.transpose(split, order)
        moved = jnp.broadcast_to(moved[..., None, :], moved.shape[:-1] + (STATES, recordings))
        return lanes_padded(moved.reshape(moved.shape[:-3] + (width,)))

    emit_in = to_lanes(emission)
    cross_in = to_lanes(cross.astype(jnp.float32))[:, None, :]
    valid_in = to_lanes(valid.astype(jnp.float32))[:, None, :]
    lane_start = (jnp.arange(width, dtype=jnp.int32) // recordings) % STATES
    basis = jnp.arange(STATES, dtype=jnp.int32)[:, None] == lane_start[None, :]
    start = lanes_padded(jnp.where(basis, 0.0, NEGATIVE).astype(jnp.float32))
    within_in = jnp.broadcast_to(trans_within[:, :, None], (STATES, STATES, LANES))
    between_in = jnp.broadcast_to(trans_between[:, :, None], (STATES, STATES, LANES))
    prefix, offset = pl.pallas_call(
        prefix_kernel,
        out_shape=(
            jax.ShapeDtypeStruct((steps, STATES, LANES), jnp.float32),
            jax.ShapeDtypeStruct((steps, 1, LANES), jnp.float32),
        ),
        cost_estimate=pl.CostEstimate(
            flops=steps * 80 * LANES * 8, transcendentals=steps * 8 * LANES * 8,
            bytes_accessed=steps * 14 * LANES * 4,
        ),
    )(within_in, between_in, start, emit_in, cross_in, valid_in)
    prefix_sj = prefix[:, :, :width].reshape(steps, STATES, pieces, STATES, recordings)
    offset_j = offset[:, 0, :width].reshape(steps, pieces, STATES, recordings)
    transfer = prefix_sj[steps - 1] + offset_j[steps - 1][None]
    transfer = jnp.transpose(transfer, (1, 2, 0, 3))
    gathered = torus_gather(transfer[None], rec_index, MESH_SIDE)
    gathered = gathered.reshape((-1,) + gathered.shape[2:])
    mats = lanes_padded(gathered)
    prior = initial - log_sum_exp(initial, 0)
    prior_in = lanes_padded(jnp.broadcast_to(prior[:, None], (STATES, recordings)))
    count = gathered.shape[0]
    incoming, total = pl.pallas_call(
        chain_kernel,
        out_shape=(
            jax.ShapeDtypeStruct((count, STATES, LANES), jnp.float32),
            jax.ShapeDtypeStruct((1, LANES), jnp.float32),
        ),
    )(prior_in, mats)
    here = lax.dynamic_slice_in_dim(incoming, rec_index * pieces, pieces, 0)[:, :, :recordings]
    weights = here[None, None] + offset_j[:, None] + prefix_sj
    reached = log_sum_exp(weights, 3)
    totals = log_sum_exp(reached, 1)
    normalized = reached - totals[:, None]
    filtered = jnp.transpose(normalized, (3, 1, 2, 0)).reshape(recordings, STATES, patches)
    return filtered, total[0, :recordings]

def neighbour_shift(block, axis, distance):
    devices = range(lax.axis_size(axis))
    route = [(i - distance, i) for i in devices if i - distance in devices]
    return lax.ppermute(block, axis, route)


def halo_rows(patch_rows, halo):
    patches = patch_rows.shape[2]
    from_left = neighbour_shift(patch_rows[:, :, patches - halo :], "rec", 1)
    from_right = neighbour_shift(patch_rows[:, :, :halo], "rec", -1)
    return jnp.concatenate([from_left, patch_rows, from_right], axis=2)

def rolled_taps(rows, weight_of, taps):
    reach = taps // 2
    count = rows.shape[0]
    accumulated = None
    for offset in range(taps):
        product = jnp.dot(rows, weight_of(offset), preferred_element_type=jnp.float32)
        shift = (reach - offset) % count
        if shift:
            product = pltpu.roll(product, shift, 0)
        accumulated = product if accumulated is None else accumulated + product
    return accumulated


def merged(ref):
    shape = ref.shape
    return ref[0].reshape(shape[1] * shape[2], shape[3])


def first_kernel(rows_ref, taps_ref, keep_ref, out_ref):
    value = jax.nn.gelu(rolled_taps(merged(rows_ref), lambda k: taps_ref[0, k], taps_ref.shape[1]))
    value = jnp.where(keep_ref[...] > 0.5, value.astype(jnp.bfloat16), jnp.zeros((), jnp.bfloat16))
    out_ref[0] = value.reshape(out_ref.shape[1:])


def residual_layer(current, taps_ref):
    update = jax.nn.gelu(rolled_taps(current, lambda k: taps_ref[0, 0, k], taps_ref.shape[2]))
    return (current.astype(jnp.float32) + update).astype(jnp.bfloat16)


def hidden_kernel(rows_ref, taps_ref, keep_ref, out_ref):
    value = residual_layer(merged(rows_ref), taps_ref)
    value = jnp.where(keep_ref[...] > 0.5, value, jnp.zeros((), jnp.bfloat16))
    out_ref[0] = value.reshape(out_ref.shape[1:])


def last_kernel(rows_ref, taps_ref, mix_ref, out_ref):
    @pl.when(pl.program_id(0) == 0)
    def _():
        out_ref[...] = jnp.zeros_like(out_ref)

    span = rows_ref.shape[2]
    recordings, patches = out_ref.shape[:2]
    margin = (span - patches) // 2
    value = residual_layer(merged(rows_ref), taps_ref)
    mixed = jnp.dot(value, mix_ref[0], preferred_element_type=jnp.float32)
    for item in range(recordings):
        start = item * span + margin
        out_ref[item] += mixed[start : start + patches]


def edge_keep(span, margin, rec_index, patches, recordings):
    total = patches * lax.axis_size("rec")
    spot = rec_index * patches - margin + jnp.arange(span, dtype=jnp.int32)
    keep = ((spot >= 0) & (spot < total)).astype(jnp.float32)
    return jnp.tile(jnp.broadcast_to(keep[:, None], (span, EMB)), (recordings, 1))


def per_type_call(kernel, rows, taps, side, out_block, out_shape, out_map, flops, layer=None):
    types, recordings = rows.shape[:2]
    side_spec = (
        pl.BlockSpec((1,) + side.shape[1:], lambda m: (m, 0, 0))
        if kernel is last_kernel
        else pl.BlockSpec(side.shape, lambda m: (0, 0))
    )
    return pl.pallas_call(
        kernel,
        grid=(types,),
        in_specs=[
            pl.BlockSpec((1,) + rows.shape[1:], lambda m: (m, 0, 0, 0)),
            pl.BlockSpec((1,) + taps.shape[1:], lambda m: (m, 0, 0, 0))
            if layer is None
            else pl.BlockSpec((1, 1) + taps.shape[2:], lambda m: (layer, m, 0, 0, 0)),
            side_spec,
        ],
        out_specs=pl.BlockSpec(out_block, out_map),
        out_shape=out_shape,
        compiler_params=pltpu.CompilerParams(dimension_semantics=("arbitrary",)),
        cost_estimate=pl.CostEstimate(
            flops=flops, transcendentals=rows.shape[0] * rows.shape[1] * rows.shape[2] * EMB,
            bytes_accessed=rows.size * 2 + taps.size * 2 // (1 if layer is None else taps.shape[0]) + side.size * 2 + out_shape.size * 4,
        ),
    )(rows, taps, side)


def conv_mix(extended, first_taps, hidden_taps, mix, rec_index, patches):
    types, recordings, span, width = extended.shape
    taps = first_taps.shape[1]
    layers = hidden_taps.shape[0]
    margin = (span - patches) // 2
    keep = edge_keep(span, margin, rec_index, patches, recordings)
    block = (1, recordings, span, EMB)
    inner = jax.ShapeDtypeStruct((types, recordings, span, EMB), jnp.bfloat16)
    current = per_type_call(
        first_kernel, extended, first_taps, keep, block, inner,
        lambda m: (m, 0, 0, 0), 2 * types * recordings * span * width * EMB * taps,
    )
    for depth_index in range(layers - 1):
        current = per_type_call(
            hidden_kernel, current, hidden_taps, keep, block, inner,
            lambda m: (m, 0, 0, 0), 2 * types * recordings * span * EMB * EMB * taps, depth_index,
        )
    mix_width = mix.shape[-1]
    return per_type_call(
        last_kernel, current, hidden_taps, mix,
        (recordings, patches, mix_width), jax.ShapeDtypeStruct((recordings, patches, mix_width), jnp.float32),
        lambda m: (0, 0, 0), 2 * types * recordings * span * EMB * (EMB * taps + mix_width), layers - 1,
    )


def torus_gather(block, rec_index, side):
    inner = rec_index % side
    outer = rec_index // side
    devices = side * side

    def shifted(values, step, stride):
        route = []
        for source in range(devices):
            row, col = source // side, source % side
            if stride == 1:
                target = row * side + (col + step) % side
            else:
                target = ((row + step) % side) * side + col
            route.append((source, target))
        return lax.ppermute(values, "rec", route)

    along = jnp.concatenate([block] + [shifted(block, step, 1) for step in range(1, side)], axis=0)
    whole = jnp.concatenate([along] + [shifted(along, step, side) for step in range(1, side)], axis=0)
    types = jnp.arange(devices, dtype=jnp.int32)
    position = ((outer - types // side) % side) * side + (inner - types % side) % side
    return jnp.take(whole, position, axis=0)


def local(
    signal,
    montage,
    channels,
    lengths,
    boundary,
    conv_in,
    conv_hid,
    mix_weight,
    norm_gain,
    emit_weight,
    trans_within,
    trans_between,
    initial,
):
    groups = lax.axis_size("rec")
    chan_index = lax.axis_index("chan")
    rec_index = lax.axis_index("rec")
    recordings = signal.shape[0]
    patches = signal.shape[2] // SAMP
    slot_ids = chan_index * groups + jnp.arange(groups, dtype=jnp.int32)
    live_slots = slot_ids[None, :] < channels[:, None]
    places = jnp.arange(groups, dtype=jnp.int32)
    pick = (montage[:, 0, None, :] == places[None, :, None]) & live_slots[:, None, :]
    rows = jnp.einsum(
        "bms,bst->mbt", pick.astype(jnp.bfloat16), signal, preferred_element_type=jnp.float32
    ).astype(jnp.bfloat16)
    patch_rows = rows.reshape(groups, recordings, patches, SAMP)
    first_taps = lax.all_gather(conv_in[:, 0], "rec", tiled=True)
    hidden_taps = lax.all_gather(jnp.swapaxes(conv_hid[:, 0], 0, 1), "rec", axis=1, tiled=True)
    extended = halo_rows(patch_rows, HALO)
    partial_value = conv_mix(extended, first_taps, hidden_taps, mix_weight[:, 0], rec_index, patches)
    spread = lax.axis_size("chan")
    pieces = partial_value.reshape(recordings, spread, patches // spread, partial_value.shape[-1])
    pieces = lax.all_to_all(jnp.swapaxes(pieces, 0, 1), "chan", 0, 0, tiled=True)
    summed = jnp.sum(pieces, axis=0)
    average = jnp.mean(summed, axis=-1, keepdims=True)
    centred = summed - average
    variance = jnp.mean(centred * centred, axis=-1, keepdims=True)
    activated = jax.nn.gelu(centred * lax.rsqrt(variance + EPSILON) * norm_gain)
    emission = jnp.einsum("bpo,os->bps", activated, emit_weight, precision=lax.Precision.HIGHEST)
    shared = lax.all_to_all(jnp.broadcast_to(emission[None], (spread,) + emission.shape), "chan", 0, 0, tiled=True)
    emission = jnp.swapaxes(shared, 0, 1).reshape(recordings, patches, STATES)
    positions = rec_index * patches + jnp.arange(patches, dtype=jnp.int32)
    valid = positions[None, :] < lengths[:, None]
    cross = boundary == 1
    filtered, log_partition = crf_forward(
        emission, cross, valid, trans_within, trans_between, initial, rec_index
    )
    return (filtered, log_partition / lengths.astype(jnp.float32))


def solution(mesh):
    placed = (
        P(None, "chan", "rec"),
        P(None, "chan", None),
        P(),
        P(),
        P(None, "rec"),
        P("rec", "chan", None, None, None),
        P("rec", "chan", None, None, None, None),
        P(None, "chan", None, None),
        P(),
        P(),
        P(),
        P(),
        P(),
    )
    return jax.shard_map(
        local, mesh=mesh, in_specs=placed, out_specs=(P(None, None, "rec"), P()), check_vma=False
    )
```

```python
import functools

import jax
import jax.numpy as jnp
from jax import lax
from jax.experimental import pallas as pl
from jax.experimental.pallas import tpu as pltpu
from jax.sharding import PartitionSpec as P

SAMP = 200
EMB = 128
STATES = 5


EPSILON = 1e-05
NEGATIVE = -1e30
MESH_SIDE = 4
SUBSHARDS = 4
HALO = 8


def log_sum_exp(values, along):
    peak_value = jnp.max(values, axis=along, keepdims=True)
    return jnp.squeeze(peak_value, along) + jnp.log(
        jnp.sum(jnp.exp(values - peak_value), axis=along)
    )


LANES = 128


def forward_step(state, matrices, extra):
    terms = [state[i : i + 1, :] + matrices[i] for i in range(len(matrices))]
    peak = functools.reduce(jnp.maximum, terms)
    total = functools.reduce(lambda x, y: x + y, [jnp.exp(t - peak) for t in terms])
    moved = peak + jnp.log(total)
    if extra is not None:
        moved = moved + extra
    top = jnp.max(moved, axis=0, keepdims=True)
    level = top + jnp.log(jnp.sum(jnp.exp(moved - top), axis=0, keepdims=True))
    return moved - level, level


def prefix_kernel(within_ref, between_ref, start_ref, emit_ref, cross_ref, valid_ref, prefix_ref, offset_ref):
    patches = emit_ref.shape[0]
    within = [within_ref[i] for i in range(STATES)]
    between = [between_ref[i] for i in range(STATES)]

    def body(p, carry):
        state, offset = carry
        crossing = cross_ref[p] > 0.5
        counted = valid_ref[p] > 0.5
        matrices = [jnp.where(crossing, between[i], within[i]) for i in range(STATES)]
        moved, level = forward_step(state, matrices, emit_ref[p])
        state = jnp.where(counted, moved, state)
        offset = offset + jnp.where(counted, level, 0.0)
        prefix_ref[p] = state
        offset_ref[p] = offset
        return state, offset

    lax.fori_loop(0, patches, body, (start_ref[...], jnp.zeros((1, LANES), jnp.float32)), unroll=8)


def chain_kernel(prior_ref, mats_ref, incoming_ref, total_ref):
    count = mats_ref.shape[0]

    def body(k, carry):
        state, total = carry
        incoming_ref[k] = state
        matrices = [mats_ref[k, j] for j in range(STATES)]
        moved, level = forward_step(state, matrices, None)
        return moved, total + level

    _, total = lax.fori_loop(0, count, body, (prior_ref[...], jnp.zeros((1, LANES), jnp.float32)))
    total_ref[...] = total


def lanes_padded(values):
    pad = [(0, 0)] * (values.ndim - 1) + [(0, LANES - values.shape[-1])]
    return jnp.pad(values, pad)


def crf_forward(emission, cross, valid, trans_within, trans_between, initial, rec_index):
    recordings, patches, _ = emission.shape
    pieces = SUBSHARDS
    steps = patches // pieces
    block = STATES * recordings
    width = pieces * block

    def to_lanes(values):
        split = values.reshape((recordings, pieces, steps) + values.shape[2:])
        order = (2,) + tuple(range(3, split.ndim)) + (1, 0)
        moved = jnp.transpose(split, order)
        moved = jnp.broadcast_to(moved[..., None, :], moved.shape[:-1] + (STATES, recordings))
        return lanes_padded(moved.reshape(moved.shape[:-3] + (width,)))

    emit_in = to_lanes(emission)
    cross_in = to_lanes(cross.astype(jnp.float32))[:, None, :]
    valid_in = to_lanes(valid.astype(jnp.float32))[:, None, :]
    lane_start = (jnp.arange(width, dtype=jnp.int32) // recordings) % STATES
    basis = jnp.arange(STATES, dtype=jnp.int32)[:, None] == lane_start[None, :]
    start = lanes_padded(jnp.where(basis, 0.0, NEGATIVE).astype(jnp.float32))
    within_in = jnp.broadcast_to(trans_within[:, :, None], (STATES, STATES, LANES))
    between_in = jnp.broadcast_to(trans_between[:, :, None], (STATES, STATES, LANES))
    prefix, offset = pl.pallas_call(
        prefix_kernel,
        out_shape=(
            jax.ShapeDtypeStruct((steps, STATES, LANES), jnp.float32),
            jax.ShapeDtypeStruct((steps, 1, LANES), jnp.float32),
        ),
        cost_estimate=pl.CostEstimate(
            flops=steps * 80 * LANES * 8, transcendentals=steps * 8 * LANES * 8,
            bytes_accessed=steps * 14 * LANES * 4,
        ),
    )(within_in, between_in, start, emit_in, cross_in, valid_in)
    prefix_sj = prefix[:, :, :width].reshape(steps, STATES, pieces, STATES, recordings)
    offset_j = offset[:, 0, :width].reshape(steps, pieces, STATES, recordings)
    transfer = prefix_sj[steps - 1] + offset_j[steps - 1][None]
    transfer = jnp.transpose(transfer, (1, 2, 0, 3))
    gathered = ring_gather(transfer[None], rec_index)
    gathered = gathered.reshape((-1,) + gathered.shape[2:])
    mats = lanes_padded(gathered)
    prior = initial - log_sum_exp(initial, 0)
    prior_in = lanes_padded(jnp.broadcast_to(prior[:, None], (STATES, recordings)))
    count = gathered.shape[0]
    incoming, total = pl.pallas_call(
        chain_kernel,
        out_shape=(
            jax.ShapeDtypeStruct((count, STATES, LANES), jnp.float32),
            jax.ShapeDtypeStruct((1, LANES), jnp.float32),
        ),
    )(prior_in, mats)
    here = lax.dynamic_slice_in_dim(incoming, rec_index * pieces, pieces, 0)[:, :, :recordings]
    weights = here[None, None] + offset_j[:, None] + prefix_sj
    reached = log_sum_exp(weights, 3)
    totals = log_sum_exp(reached, 1)
    normalized = reached - totals[:, None]
    filtered = jnp.transpose(normalized, (3, 1, 2, 0)).reshape(recordings, STATES, patches)
    return filtered, total[0, :recordings]

def neighbour_shift(block, axis, distance):
    devices = range(lax.axis_size(axis))
    route = [(i - distance, i) for i in devices if i - distance in devices]
    return lax.ppermute(block, axis, route)


def halo_rows(patch_rows, halo):
    patches = patch_rows.shape[2]
    from_left = neighbour_shift(patch_rows[:, :, patches - halo :], "rec", 1)
    from_right = neighbour_shift(patch_rows[:, :, :halo], "rec", -1)
    return jnp.concatenate([from_left, patch_rows, from_right], axis=2)

def rolled_taps(rows, weight_of, taps):
    reach = taps // 2
    count = rows.shape[0]
    accumulated = None
    for offset in range(taps):
        product = jnp.dot(rows, weight_of(offset), preferred_element_type=jnp.float32)
        shift = (reach - offset) % count
        if shift:
            product = pltpu.roll(product, shift, 0)
        accumulated = product if accumulated is None else accumulated + product
    return accumulated


def merged(ref):
    shape = ref.shape
    return ref[0].reshape(shape[1] * shape[2], shape[3])


def first_kernel(rows_ref, taps_ref, keep_ref, out_ref):
    value = jax.nn.gelu(rolled_taps(merged(rows_ref), lambda k: taps_ref[0, k], taps_ref.shape[1]))
    value = jnp.where(keep_ref[...] > 0.5, value.astype(jnp.bfloat16), jnp.zeros((), jnp.bfloat16))
    out_ref[0] = value.reshape(out_ref.shape[1:])


def residual_layer(current, taps_ref):
    update = jax.nn.gelu(rolled_taps(current, lambda k: taps_ref[0, 0, k], taps_ref.shape[2]))
    return (current.astype(jnp.float32) + update).astype(jnp.bfloat16)


def hidden_kernel(rows_ref, taps_ref, keep_ref, out_ref):
    value = residual_layer(merged(rows_ref), taps_ref)
    value = jnp.where(keep_ref[...] > 0.5, value, jnp.zeros((), jnp.bfloat16))
    out_ref[0] = value.reshape(out_ref.shape[1:])


def last_kernel(rows_ref, taps_ref, mix_ref, out_ref):
    @pl.when(pl.program_id(0) == 0)
    def _():
        out_ref[...] = jnp.zeros_like(out_ref)

    span = rows_ref.shape[2]
    recordings, patches = out_ref.shape[:2]
    margin = (span - patches) // 2
    value = residual_layer(merged(rows_ref), taps_ref)
    mixed = jnp.dot(value, mix_ref[0], preferred_element_type=jnp.float32)
    for item in range(recordings):
        start = item * span + margin
        out_ref[item] += mixed[start : start + patches]


def edge_keep(span, margin, rec_index, patches, recordings):
    total = patches * lax.axis_size("rec")
    spot = rec_index * patches - margin + jnp.arange(span, dtype=jnp.int32)
    keep = ((spot >= 0) & (spot < total)).astype(jnp.float32)
    return jnp.tile(jnp.broadcast_to(keep[:, None], (span, EMB)), (recordings, 1))


def per_type_call(kernel, rows, taps, side, out_block, out_shape, out_map, flops, layer=None):
    types, recordings = rows.shape[:2]
    side_spec = (
        pl.BlockSpec((1,) + side.shape[1:], lambda m: (m, 0, 0))
        if kernel is last_kernel
        else pl.BlockSpec(side.shape, lambda m: (0, 0))
    )
    return pl.pallas_call(
        kernel,
        grid=(types,),
        in_specs=[
            pl.BlockSpec((1,) + rows.shape[1:], lambda m: (m, 0, 0, 0)),
            pl.BlockSpec((1,) + taps.shape[1:], lambda m: (m, 0, 0, 0))
            if layer is None
            else pl.BlockSpec((1, 1) + taps.shape[2:], lambda m: (layer, m, 0, 0, 0)),
            side_spec,
        ],
        out_specs=pl.BlockSpec(out_block, out_map),
        out_shape=out_shape,
        compiler_params=pltpu.CompilerParams(dimension_semantics=("arbitrary",)),
        cost_estimate=pl.CostEstimate(
            flops=flops, transcendentals=rows.shape[0] * rows.shape[1] * rows.shape[2] * EMB,
            bytes_accessed=rows.size * 2 + taps.size * 2 // (1 if layer is None else taps.shape[0]) + side.size * 2 + out_shape.size * 4,
        ),
    )(rows, taps, side)


def conv_mix(extended, first_taps, hidden_taps, mix, rec_index, patches):
    types, recordings, span, width = extended.shape
    taps = first_taps.shape[1]
    layers = hidden_taps.shape[0]
    margin = (span - patches) // 2
    keep = edge_keep(span, margin, rec_index, patches, recordings)
    block = (1, recordings, span, EMB)
    inner = jax.ShapeDtypeStruct((types, recordings, span, EMB), jnp.bfloat16)
    current = per_type_call(
        first_kernel, extended, first_taps, keep, block, inner,
        lambda m: (m, 0, 0, 0), 2 * types * recordings * span * width * EMB * taps,
    )
    for depth_index in range(layers - 1):
        current = per_type_call(
            hidden_kernel, current, hidden_taps, keep, block, inner,
            lambda m: (m, 0, 0, 0), 2 * types * recordings * span * EMB * EMB * taps, depth_index,
        )
    mix_width = mix.shape[-1]
    return per_type_call(
        last_kernel, current, hidden_taps, mix,
        (recordings, patches, mix_width), jax.ShapeDtypeStruct((recordings, patches, mix_width), jnp.float32),
        lambda m: (0, 0, 0), 2 * types * recordings * span * EMB * (EMB * taps + mix_width), layers - 1,
    )


def ring_gather(block, rec_index):
    devices = lax.axis_size("rec")
    parts = [block]
    for step in range(1, devices):
        route = [(source, (source + step) % devices) for source in range(devices)]
        parts.append(lax.ppermute(block, "rec", route))
    whole = jnp.concatenate(parts, axis=0)
    position = (rec_index - jnp.arange(devices, dtype=jnp.int32)) % devices
    return jnp.take(whole, position, axis=0)


def torus_gather(block, rec_index, side):
    inner = rec_index % side
    outer = rec_index // side
    devices = side * side

    def shifted(values, step, stride):
        route = []
        for source in range(devices):
            row, col = source // side, source % side
            if stride == 1:
                target = row * side + (col + step) % side
            else:
                target = ((row + step) % side) * side + col
            route.append((source, target))
        return lax.ppermute(values, "rec", route)

    along = jnp.concatenate([block] + [shifted(block, step, 1) for step in range(1, side)], axis=0)
    whole = jnp.concatenate([along] + [shifted(along, step, side) for step in range(1, side)], axis=0)
    types = jnp.arange(devices, dtype=jnp.int32)
    position = ((outer - types // side) % side) * side + (inner - types % side) % side
    return jnp.take(whole, position, axis=0)


def local(
    signal,
    montage,
    channels,
    lengths,
    boundary,
    conv_in,
    conv_hid,
    mix_weight,
    norm_gain,
    emit_weight,
    trans_within,
    trans_between,
    initial,
):
    groups = lax.axis_size("rec")
    chan_index = lax.axis_index("chan")
    rec_index = lax.axis_index("rec")
    recordings = signal.shape[0]
    patches = signal.shape[2] // SAMP
    slot_ids = chan_index * groups + jnp.arange(groups, dtype=jnp.int32)
    live_slots = slot_ids[None, :] < channels[:, None]
    places = jnp.arange(groups, dtype=jnp.int32)
    pick = (montage[:, 0, None, :] == places[None, :, None]) & live_slots[:, None, :]
    rows = jnp.einsum(
        "bms,bst->mbt", pick.astype(jnp.bfloat16), signal, preferred_element_type=jnp.float32
    ).astype(jnp.bfloat16)
    patch_rows = rows.reshape(groups, recordings, patches, SAMP)
    first_taps = lax.all_gather(conv_in[:, 0], "rec", tiled=True)
    hidden_taps = lax.all_gather(jnp.swapaxes(conv_hid[:, 0], 0, 1), "rec", axis=1, tiled=True)
    extended = halo_rows(patch_rows, HALO)
    partial_value = conv_mix(extended, first_taps, hidden_taps, mix_weight[:, 0], rec_index, patches)
    spread = lax.axis_size("chan")
    pieces = partial_value.reshape(recordings, spread, patches // spread, partial_value.shape[-1])
    pieces = lax.all_to_all(jnp.swapaxes(pieces, 0, 1), "chan", 0, 0, tiled=True)
    summed = jnp.sum(pieces, axis=0)
    average = jnp.mean(summed, axis=-1, keepdims=True)
    centred = summed - average
    variance = jnp.mean(centred * centred, axis=-1, keepdims=True)
    activated = jax.nn.gelu(centred * lax.rsqrt(variance + EPSILON) * norm_gain)
    emission = jnp.einsum("bpo,os->bps", activated, emit_weight, precision=lax.Precision.HIGHEST)
    shared = lax.all_to_all(jnp.broadcast_to(emission[None], (spread,) + emission.shape), "chan", 0, 0, tiled=True)
    emission = jnp.swapaxes(shared, 0, 1).reshape(recordings, patches, STATES)
    positions = rec_index * patches + jnp.arange(patches, dtype=jnp.int32)
    valid = positions[None, :] < lengths[:, None]
    cross = boundary == 1
    filtered, log_partition = crf_forward(
        emission, cross, valid, trans_within, trans_between, initial, rec_index
    )
    return (filtered, log_partition / lengths.astype(jnp.float32))


def solution(mesh):
    placed = (
        P(None, "chan", "rec"),
        P(None, "chan", None),
        P(),
        P(),
        P(None, "rec"),
        P("rec", "chan", None, None, None),
        P("rec", "chan", None, None, None, None),
        P(None, "chan", None, None),
        P(),
        P(),
        P(),
        P(),
        P(),
    )
    return jax.shard_map(
        local, mesh=mesh, in_specs=placed, out_specs=(P(None, None, "rec"), P()), check_vma=False
    )
```

```python
import functools

import jax
import jax.numpy as jnp
from jax import lax
from jax.experimental import pallas as pl
from jax.experimental.pallas import tpu as pltpu
from jax.sharding import PartitionSpec as P

SAMP = 200
EMB = 128
STATES = 5


EPSILON = 1e-05
NEGATIVE = -1e30
MESH_SIDE = 4
SUBSHARDS = 4
HALO = 8


def log_sum_exp(values, along):
    peak_value = jnp.max(values, axis=along, keepdims=True)
    return jnp.squeeze(peak_value, along) + jnp.log(
        jnp.sum(jnp.exp(values - peak_value), axis=along)
    )


LANES = 128


def forward_step(state, matrices, extra):
    terms = [state[i : i + 1, :] + matrices[i] for i in range(len(matrices))]
    peak = functools.reduce(jnp.maximum, terms)
    total = functools.reduce(lambda x, y: x + y, [jnp.exp(t - peak) for t in terms])
    moved = peak + jnp.log(total)
    if extra is not None:
        moved = moved + extra
    top = jnp.max(moved, axis=0, keepdims=True)
    level = top + jnp.log(jnp.sum(jnp.exp(moved - top), axis=0, keepdims=True))
    return moved - level, level


def prefix_kernel(within_ref, between_ref, start_ref, emit_ref, cross_ref, valid_ref, prefix_ref, offset_ref):
    patches = emit_ref.shape[0]
    within = [within_ref[i] for i in range(STATES)]
    between = [between_ref[i] for i in range(STATES)]

    def body(p, carry):
        state, offset = carry
        crossing = cross_ref[p] > 0.5
        counted = valid_ref[p] > 0.5
        matrices = [jnp.where(crossing, between[i], within[i]) for i in range(STATES)]
        moved, level = forward_step(state, matrices, emit_ref[p])
        state = jnp.where(counted, moved, state)
        offset = offset + jnp.where(counted, level, 0.0)
        prefix_ref[p] = state
        offset_ref[p] = offset
        return state, offset

    lax.fori_loop(0, patches, body, (start_ref[...], jnp.zeros((1, LANES), jnp.float32)), unroll=8)


def chain_kernel(prior_ref, mats_ref, incoming_ref, total_ref):
    count = mats_ref.shape[0]

    def body(k, carry):
        state, total = carry
        incoming_ref[k] = state
        matrices = [mats_ref[k, j] for j in range(STATES)]
        moved, level = forward_step(state, matrices, None)
        return moved, total + level

    _, total = lax.fori_loop(0, count, body, (prior_ref[...], jnp.zeros((1, prior_ref.shape[1]), jnp.float32)))
    total_ref[...] = total


def lanes_padded(values):
    pad = [(0, 0)] * (values.ndim - 1) + [(0, LANES - values.shape[-1])]
    return jnp.pad(values, pad)


def crf_forward(emission, cross, valid, trans_within, trans_between, initial, rec_index):
    recordings, patches, _ = emission.shape
    pieces = SUBSHARDS
    steps = patches // pieces
    block = STATES * recordings
    width = pieces * block

    def to_lanes(values):
        split = values.reshape((recordings, pieces, steps) + values.shape[2:])
        order = (2,) + tuple(range(3, split.ndim)) + (1, 0)
        moved = jnp.transpose(split, order)
        moved = jnp.broadcast_to(moved[..., None, :], moved.shape[:-1] + (STATES, recordings))
        return lanes_padded(moved.reshape(moved.shape[:-3] + (width,)))

    emit_in = to_lanes(emission)
    cross_in = to_lanes(cross.astype(jnp.float32))[:, None, :]
    valid_in = to_lanes(valid.astype(jnp.float32))[:, None, :]
    lane_start = (jnp.arange(width, dtype=jnp.int32) // recordings) % STATES
    basis = jnp.arange(STATES, dtype=jnp.int32)[:, None] == lane_start[None, :]
    start = lanes_padded(jnp.where(basis, 0.0, NEGATIVE).astype(jnp.float32))
    within_in = jnp.broadcast_to(trans_within[:, :, None], (STATES, STATES, LANES))
    between_in = jnp.broadcast_to(trans_between[:, :, None], (STATES, STATES, LANES))
    prefix, offset = pl.pallas_call(
        prefix_kernel,
        out_shape=(
            jax.ShapeDtypeStruct((steps, STATES, LANES), jnp.float32),
            jax.ShapeDtypeStruct((steps, 1, LANES), jnp.float32),
        ),
        cost_estimate=pl.CostEstimate(
            flops=steps * 80 * LANES * 8, transcendentals=steps * 8 * LANES * 8,
            bytes_accessed=steps * 14 * LANES * 4,
        ),
    )(within_in, between_in, start, emit_in, cross_in, valid_in)
    prefix_sj = prefix[:, :, :width].reshape(steps, STATES, pieces, STATES, recordings)
    offset_j = offset[:, 0, :width].reshape(steps, pieces, STATES, recordings)
    transfer = prefix_sj[steps - 1] + offset_j[steps - 1][None]
    transfer = jnp.transpose(transfer, (1, 2, 0, 3))
    gathered = torus_gather(transfer[None], rec_index, MESH_SIDE)
    gathered = gathered.reshape((-1,) + gathered.shape[2:])
    mats = gathered
    prior = initial - log_sum_exp(initial, 0)
    prior_in = jnp.broadcast_to(prior[:, None], (STATES, recordings))
    count = gathered.shape[0]
    incoming, total = pl.pallas_call(
        chain_kernel,
        out_shape=(
            jax.ShapeDtypeStruct((count, STATES, recordings), jnp.float32),
            jax.ShapeDtypeStruct((1, recordings), jnp.float32),
        ),
    )(prior_in, mats)
    here = lax.dynamic_slice_in_dim(incoming, rec_index * pieces, pieces, 0)[:, :, :recordings]
    weights = here[None, None] + offset_j[:, None] + prefix_sj
    reached = log_sum_exp(weights, 3)
    totals = log_sum_exp(reached, 1)
    normalized = reached - totals[:, None]
    filtered = jnp.transpose(normalized, (3, 1, 2, 0)).reshape(recordings, STATES, patches)
    return filtered, total[0, :recordings]

def neighbour_shift(block, axis, distance):
    devices = range(lax.axis_size(axis))
    route = [(i - distance, i) for i in devices if i - distance in devices]
    return lax.ppermute(block, axis, route)


def halo_rows(patch_rows, halo):
    patches = patch_rows.shape[2]
    from_left = neighbour_shift(patch_rows[:, :, patches - halo :], "rec", 1)
    from_right = neighbour_shift(patch_rows[:, :, :halo], "rec", -1)
    return jnp.concatenate([from_left, patch_rows, from_right], axis=2)

def rolled_taps(rows, weight_of, taps):
    reach = taps // 2
    count = rows.shape[0]
    accumulated = None
    for offset in range(taps):
        product = jnp.dot(rows, weight_of(offset), preferred_element_type=jnp.float32)
        shift = (reach - offset) % count
        if shift:
            product = pltpu.roll(product, shift, 0)
        accumulated = product if accumulated is None else accumulated + product
    return accumulated


def merged(ref):
    shape = ref.shape
    return ref[0].reshape(shape[1] * shape[2], shape[3])


def first_kernel(rows_ref, taps_ref, keep_ref, out_ref):
    value = jax.nn.gelu(rolled_taps(merged(rows_ref), lambda k: taps_ref[0, k], taps_ref.shape[1]))
    value = jnp.where(keep_ref[...] > 0.5, value.astype(jnp.bfloat16), jnp.zeros((), jnp.bfloat16))
    out_ref[0] = value.reshape(out_ref.shape[1:])


def residual_layer(current, taps_ref):
    update = jax.nn.gelu(rolled_taps(current, lambda k: taps_ref[0, 0, k], taps_ref.shape[2]))
    return (current.astype(jnp.float32) + update).astype(jnp.bfloat16)


def hidden_kernel(rows_ref, taps_ref, keep_ref, out_ref):
    value = residual_layer(merged(rows_ref), taps_ref)
    value = jnp.where(keep_ref[...] > 0.5, value, jnp.zeros((), jnp.bfloat16))
    out_ref[0] = value.reshape(out_ref.shape[1:])


def last_kernel(rows_ref, taps_ref, mix_ref, out_ref):
    @pl.when(pl.program_id(0) == 0)
    def _():
        out_ref[...] = jnp.zeros_like(out_ref)

    span = rows_ref.shape[2]
    recordings, patches = out_ref.shape[:2]
    margin = (span - patches) // 2
    value = residual_layer(merged(rows_ref), taps_ref)
    mixed = jnp.dot(value, mix_ref[0], preferred_element_type=jnp.float32)
    for item in range(recordings):
        start = item * span + margin
        out_ref[item] += mixed[start : start + patches]


def edge_keep(span, margin, rec_index, patches, recordings):
    total = patches * lax.axis_size("rec")
    spot = rec_index * patches - margin + jnp.arange(span, dtype=jnp.int32)
    keep = ((spot >= 0) & (spot < total)).astype(jnp.float32)
    return jnp.tile(jnp.broadcast_to(keep[:, None], (span, EMB)), (recordings, 1))


def per_type_call(kernel, rows, taps, side, out_block, out_shape, out_map, flops, layer=None):
    types, recordings = rows.shape[:2]
    side_spec = (
        pl.BlockSpec((1,) + side.shape[1:], lambda m: (m, 0, 0))
        if kernel is last_kernel
        else pl.BlockSpec(side.shape, lambda m: (0, 0))
    )
    return pl.pallas_call(
        kernel,
        grid=(types,),
        in_specs=[
            pl.BlockSpec((1,) + rows.shape[1:], lambda m: (m, 0, 0, 0)),
            pl.BlockSpec((1,) + taps.shape[1:], lambda m: (m, 0, 0, 0))
            if layer is None
            else pl.BlockSpec((1, 1) + taps.shape[2:], lambda m: (layer, m, 0, 0, 0)),
            side_spec,
        ],
        out_specs=pl.BlockSpec(out_block, out_map),
        out_shape=out_shape,
        compiler_params=pltpu.CompilerParams(dimension_semantics=("arbitrary",)),
        cost_estimate=pl.CostEstimate(
            flops=flops, transcendentals=rows.shape[0] * rows.shape[1] * rows.shape[2] * EMB,
            bytes_accessed=rows.size * 2 + taps.size * 2 // (1 if layer is None else taps.shape[0]) + side.size * 2 + out_shape.size * 4,
        ),
    )(rows, taps, side)


def conv_mix(extended, first_taps, hidden_taps, mix, rec_index, patches):
    types, recordings, span, width = extended.shape
    taps = first_taps.shape[1]
    layers = hidden_taps.shape[0]
    margin = (span - patches) // 2
    keep = edge_keep(span, margin, rec_index, patches, recordings)
    block = (1, recordings, span, EMB)
    inner = jax.ShapeDtypeStruct((types, recordings, span, EMB), jnp.bfloat16)
    current = per_type_call(
        first_kernel, extended, first_taps, keep, block, inner,
        lambda m: (m, 0, 0, 0), 2 * types * recordings * span * width * EMB * taps,
    )
    for depth_index in range(layers - 1):
        current = per_type_call(
            hidden_kernel, current, hidden_taps, keep, block, inner,
            lambda m: (m, 0, 0, 0), 2 * types * recordings * span * EMB * EMB * taps, depth_index,
        )
    mix_width = mix.shape[-1]
    return per_type_call(
        last_kernel, current, hidden_taps, mix,
        (recordings, patches, mix_width), jax.ShapeDtypeStruct((recordings, patches, mix_width), jnp.float32),
        lambda m: (0, 0, 0), 2 * types * recordings * span * EMB * (EMB * taps + mix_width), layers - 1,
    )


def torus_gather(block, rec_index, side):
    inner = rec_index % side
    outer = rec_index // side
    devices = side * side

    def shifted(values, step, stride):
        route = []
        for source in range(devices):
            row, col = source // side, source % side
            if stride == 1:
                target = row * side + (col + step) % side
            else:
                target = ((row + step) % side) * side + col
            route.append((source, target))
        return lax.ppermute(values, "rec", route)

    along = jnp.concatenate([block] + [shifted(block, step, 1) for step in range(1, side)], axis=0)
    whole = jnp.concatenate([along] + [shifted(along, step, side) for step in range(1, side)], axis=0)
    types = jnp.arange(devices, dtype=jnp.int32)
    position = ((outer - types // side) % side) * side + (inner - types % side) % side
    return jnp.take(whole, position, axis=0)


def local(
    signal,
    montage,
    channels,
    lengths,
    boundary,
    conv_in,
    conv_hid,
    mix_weight,
    norm_gain,
    emit_weight,
    trans_within,
    trans_between,
    initial,
):
    groups = lax.axis_size("rec")
    chan_index = lax.axis_index("chan")
    rec_index = lax.axis_index("rec")
    recordings = signal.shape[0]
    patches = signal.shape[2] // SAMP
    slot_ids = chan_index * groups + jnp.arange(groups, dtype=jnp.int32)
    live_slots = slot_ids[None, :] < channels[:, None]
    places = jnp.arange(groups, dtype=jnp.int32)
    pick = (montage[:, 0, None, :] == places[None, :, None]) & live_slots[:, None, :]
    rows = jnp.einsum(
        "bms,bst->mbt", pick.astype(jnp.bfloat16), signal, preferred_element_type=jnp.float32
    ).astype(jnp.bfloat16)
    patch_rows = rows.reshape(groups, recordings, patches, SAMP)
    first_taps = lax.all_gather(conv_in[:, 0], "rec", tiled=True)
    hidden_taps = lax.all_gather(jnp.swapaxes(conv_hid[:, 0], 0, 1), "rec", axis=1, tiled=True)
    extended = halo_rows(patch_rows, HALO)
    partial_value = conv_mix(extended, first_taps, hidden_taps, mix_weight[:, 0], rec_index, patches)
    spread = lax.axis_size("chan")
    pieces = partial_value.reshape(recordings, spread, patches // spread, partial_value.shape[-1])
    pieces = lax.all_to_all(jnp.swapaxes(pieces, 0, 1), "chan", 0, 0, tiled=True)
    summed = jnp.sum(pieces, axis=0)
    average = jnp.mean(summed, axis=-1, keepdims=True)
    centred = summed - average
    variance = jnp.mean(centred * centred, axis=-1, keepdims=True)
    activated = jax.nn.gelu(centred * lax.rsqrt(variance + EPSILON) * norm_gain)
    emission = jnp.einsum("bpo,os->bps", activated, emit_weight, precision=lax.Precision.HIGHEST)
    shared = lax.all_to_all(jnp.broadcast_to(emission[None], (spread,) + emission.shape), "chan", 0, 0, tiled=True)
    emission = jnp.swapaxes(shared, 0, 1).reshape(recordings, patches, STATES)
    positions = rec_index * patches + jnp.arange(patches, dtype=jnp.int32)
    valid = positions[None, :] < lengths[:, None]
    cross = boundary == 1
    filtered, log_partition = crf_forward(
        emission, cross, valid, trans_within, trans_between, initial, rec_index
    )
    return (filtered, log_partition / lengths.astype(jnp.float32))


def solution(mesh):
    placed = (
        P(None, "chan", "rec"),
        P(None, "chan", None),
        P(),
        P(),
        P(None, "rec"),
        P("rec", "chan", None, None, None),
        P("rec", "chan", None, None, None, None),
        P(None, "chan", None, None),
        P(),
        P(),
        P(),
        P(),
        P(),
    )
    return jax.shard_map(
        local, mesh=mesh, in_specs=placed, out_specs=(P(None, None, "rec"), P()), check_vma=False
    )
```

```python
import functools

import jax
import jax.numpy as jnp
from jax import lax
from jax.experimental import pallas as pl
from jax.experimental.pallas import tpu as pltpu
from jax.sharding import PartitionSpec as P

SAMP = 200
EMB = 128
STATES = 5


EPSILON = 1e-05
NEGATIVE = -1e30
MESH_SIDE = 4
SUBSHARDS = 4
HALO = 8


def log_sum_exp(values, along):
    peak_value = jnp.max(values, axis=along, keepdims=True)
    return jnp.squeeze(peak_value, along) + jnp.log(
        jnp.sum(jnp.exp(values - peak_value), axis=along)
    )


LANES = 128


def forward_step(state, matrices, extra):
    terms = [state[i : i + 1, :] + matrices[i] for i in range(len(matrices))]
    peak = functools.reduce(jnp.maximum, terms)
    total = functools.reduce(lambda x, y: x + y, [jnp.exp(t - peak) for t in terms])
    moved = peak + jnp.log(total)
    if extra is not None:
        moved = moved + extra
    top = jnp.max(moved, axis=0, keepdims=True)
    level = top + jnp.log(jnp.sum(jnp.exp(moved - top), axis=0, keepdims=True))
    return moved - level, level


def prefix_kernel(within_ref, between_ref, start_ref, emit_ref, cross_ref, valid_ref, prefix_ref, offset_ref):
    patches = emit_ref.shape[0]
    lanes = start_ref.shape[1]
    within = [jnp.broadcast_to(within_ref[i], (STATES, lanes)) for i in range(STATES)]
    between = [jnp.broadcast_to(between_ref[i], (STATES, lanes)) for i in range(STATES)]

    def body(p, carry):
        state, offset = carry
        crossing = cross_ref[p] > 0.5
        counted = valid_ref[p] > 0.5
        matrices = [jnp.where(crossing, between[i], within[i]) for i in range(STATES)]
        moved, level = forward_step(state, matrices, emit_ref[p])
        state = jnp.where(counted, moved, state)
        offset = offset + jnp.where(counted, level, 0.0)
        prefix_ref[p] = state
        offset_ref[p] = offset
        return state, offset

    lax.fori_loop(0, patches, body, (start_ref[...], jnp.zeros((1, LANES), jnp.float32)), unroll=8)


def chain_kernel(prior_ref, mats_ref, incoming_ref, total_ref):
    count = mats_ref.shape[0]

    def body(k, carry):
        state, total = carry
        incoming_ref[k] = state
        matrices = [mats_ref[k, j] for j in range(STATES)]
        moved, level = forward_step(state, matrices, None)
        return moved, total + level

    _, total = lax.fori_loop(0, count, body, (prior_ref[...], jnp.zeros((1, prior_ref.shape[1]), jnp.float32)))
    total_ref[...] = total


def lanes_padded(values):
    pad = [(0, 0)] * (values.ndim - 1) + [(0, LANES - values.shape[-1])]
    return jnp.pad(values, pad)


def crf_forward(emission, cross, valid, trans_within, trans_between, initial, rec_index):
    recordings, patches, _ = emission.shape
    pieces = SUBSHARDS
    steps = patches // pieces
    block = STATES * recordings
    width = pieces * block

    def to_lanes(values):
        split = values.reshape((recordings, pieces, steps) + values.shape[2:])
        order = (2,) + tuple(range(3, split.ndim)) + (1, 0)
        moved = jnp.transpose(split, order)
        moved = jnp.broadcast_to(moved[..., None, :], moved.shape[:-1] + (STATES, recordings))
        return lanes_padded(moved.reshape(moved.shape[:-3] + (width,)))

    emit_in = to_lanes(emission)
    cross_in = to_lanes(cross.astype(jnp.float32))[:, None, :]
    valid_in = to_lanes(valid.astype(jnp.float32))[:, None, :]
    lane_start = (jnp.arange(width, dtype=jnp.int32) // recordings) % STATES
    basis = jnp.arange(STATES, dtype=jnp.int32)[:, None] == lane_start[None, :]
    start = lanes_padded(jnp.where(basis, 0.0, NEGATIVE).astype(jnp.float32))
    within_in = trans_within[:, :, None]
    between_in = trans_between[:, :, None]
    prefix, offset = pl.pallas_call(
        prefix_kernel,
        out_shape=(
            jax.ShapeDtypeStruct((steps, STATES, LANES), jnp.float32),
            jax.ShapeDtypeStruct((steps, 1, LANES), jnp.float32),
        ),
        cost_estimate=pl.CostEstimate(
            flops=steps * 80 * LANES * 8, transcendentals=steps * 8 * LANES * 8,
            bytes_accessed=steps * 14 * LANES * 4,
        ),
    )(within_in, between_in, start, emit_in, cross_in, valid_in)
    prefix_sj = prefix[:, :, :width].reshape(steps, STATES, pieces, STATES, recordings)
    offset_j = offset[:, 0, :width].reshape(steps, pieces, STATES, recordings)
    transfer = prefix_sj[steps - 1] + offset_j[steps - 1][None]
    transfer = jnp.transpose(transfer, (1, 2, 0, 3))
    gathered = torus_gather(transfer[None], rec_index, MESH_SIDE)
    gathered = gathered.reshape((-1,) + gathered.shape[2:])
    mats = gathered
    prior = initial - log_sum_exp(initial, 0)
    prior_in = jnp.broadcast_to(prior[:, None], (STATES, recordings))
    count = gathered.shape[0]
    incoming, total = pl.pallas_call(
        chain_kernel,
        out_shape=(
            jax.ShapeDtypeStruct((count, STATES, recordings), jnp.float32),
            jax.ShapeDtypeStruct((1, recordings), jnp.float32),
        ),
    )(prior_in, mats)
    here = lax.dynamic_slice_in_dim(incoming, rec_index * pieces, pieces, 0)[:, :, :recordings]
    weights = here[None, None] + offset_j[:, None] + prefix_sj
    reached = log_sum_exp(weights, 3)
    totals = log_sum_exp(reached, 1)
    normalized = reached - totals[:, None]
    filtered = jnp.transpose(normalized, (3, 1, 2, 0)).reshape(recordings, STATES, patches)
    return filtered, total[0, :recordings]

def neighbour_shift(block, axis, distance):
    devices = range(lax.axis_size(axis))
    route = [(i - distance, i) for i in devices if i - distance in devices]
    return lax.ppermute(block, axis, route)


def halo_rows(patch_rows, halo):
    patches = patch_rows.shape[2]
    from_left = neighbour_shift(patch_rows[:, :, patches - halo :], "rec", 1)
    from_right = neighbour_shift(patch_rows[:, :, :halo], "rec", -1)
    return jnp.concatenate([from_left, patch_rows, from_right], axis=2)

def rolled_taps(rows, weight_of, taps):
    reach = taps // 2
    count = rows.shape[0]
    accumulated = None
    for offset in range(taps):
        product = jnp.dot(rows, weight_of(offset), preferred_element_type=jnp.float32)
        shift = (reach - offset) % count
        if shift:
            product = pltpu.roll(product, shift, 0)
        accumulated = product if accumulated is None else accumulated + product
    return accumulated


def merged(ref):
    shape = ref.shape
    return ref[0].reshape(shape[1] * shape[2], shape[3])


def first_kernel(rows_ref, taps_ref, keep_ref, out_ref):
    value = jax.nn.gelu(rolled_taps(merged(rows_ref), lambda k: taps_ref[0, k], taps_ref.shape[1]))
    value = jnp.where(keep_ref[...] > 0.5, value.astype(jnp.bfloat16), jnp.zeros((), jnp.bfloat16))
    out_ref[0] = value.reshape(out_ref.shape[1:])


def residual_layer(current, taps_ref):
    update = jax.nn.gelu(rolled_taps(current, lambda k: taps_ref[0, 0, k], taps_ref.shape[2]))
    return (current.astype(jnp.float32) + update).astype(jnp.bfloat16)


def hidden_kernel(rows_ref, taps_ref, keep_ref, out_ref):
    value = residual_layer(merged(rows_ref), taps_ref)
    value = jnp.where(keep_ref[...] > 0.5, value, jnp.zeros((), jnp.bfloat16))
    out_ref[0] = value.reshape(out_ref.shape[1:])


def last_kernel(rows_ref, taps_ref, mix_ref, out_ref):
    @pl.when(pl.program_id(0) == 0)
    def _():
        out_ref[...] = jnp.zeros_like(out_ref)

    span = rows_ref.shape[2]
    recordings, patches = out_ref.shape[:2]
    margin = (span - patches) // 2
    value = residual_layer(merged(rows_ref), taps_ref)
    mixed = jnp.dot(value, mix_ref[0], preferred_element_type=jnp.float32)
    for item in range(recordings):
        start = item * span + margin
        out_ref[item] += mixed[start : start + patches]


def edge_keep(span, margin, rec_index, patches, recordings):
    total = patches * lax.axis_size("rec")
    spot = rec_index * patches - margin + jnp.arange(span, dtype=jnp.int32)
    keep = ((spot >= 0) & (spot < total)).astype(jnp.float32)
    return jnp.tile(jnp.broadcast_to(keep[:, None], (span, EMB)), (recordings, 1))


def per_type_call(kernel, rows, taps, side, out_block, out_shape, out_map, flops, layer=None):
    types, recordings = rows.shape[:2]
    side_spec = (
        pl.BlockSpec((1,) + side.shape[1:], lambda m: (m, 0, 0))
        if kernel is last_kernel
        else pl.BlockSpec(side.shape, lambda m: (0, 0))
    )
    return pl.pallas_call(
        kernel,
        grid=(types,),
        in_specs=[
            pl.BlockSpec((1,) + rows.shape[1:], lambda m: (m, 0, 0, 0)),
            pl.BlockSpec((1,) + taps.shape[1:], lambda m: (m, 0, 0, 0))
            if layer is None
            else pl.BlockSpec((1, 1) + taps.shape[2:], lambda m: (layer, m, 0, 0, 0)),
            side_spec,
        ],
        out_specs=pl.BlockSpec(out_block, out_map),
        out_shape=out_shape,
        compiler_params=pltpu.CompilerParams(dimension_semantics=("arbitrary",)),
        cost_estimate=pl.CostEstimate(
            flops=flops, transcendentals=rows.shape[0] * rows.shape[1] * rows.shape[2] * EMB,
            bytes_accessed=rows.size * 2 + taps.size * 2 // (1 if layer is None else taps.shape[0]) + side.size * 2 + out_shape.size * 4,
        ),
    )(rows, taps, side)


def conv_mix(extended, first_taps, hidden_taps, mix, rec_index, patches):
    types, recordings, span, width = extended.shape
    taps = first_taps.shape[1]
    layers = hidden_taps.shape[0]
    margin = (span - patches) // 2
    keep = edge_keep(span, margin, rec_index, patches, recordings)
    block = (1, recordings, span, EMB)
    inner = jax.ShapeDtypeStruct((types, recordings, span, EMB), jnp.bfloat16)
    current = per_type_call(
        first_kernel, extended, first_taps, keep, block, inner,
        lambda m: (m, 0, 0, 0), 2 * types * recordings * span * width * EMB * taps,
    )
    for depth_index in range(layers - 1):
        current = per_type_call(
            hidden_kernel, current, hidden_taps, keep, block, inner,
            lambda m: (m, 0, 0, 0), 2 * types * recordings * span * EMB * EMB * taps, depth_index,
        )
    mix_width = mix.shape[-1]
    return per_type_call(
        last_kernel, current, hidden_taps, mix,
        (recordings, patches, mix_width), jax.ShapeDtypeStruct((recordings, patches, mix_width), jnp.float32),
        lambda m: (0, 0, 0), 2 * types * recordings * span * EMB * (EMB * taps + mix_width), layers - 1,
    )


def torus_gather(block, rec_index, side):
    inner = rec_index % side
    outer = rec_index // side
    devices = side * side

    def shifted(values, step, stride):
        route = []
        for source in range(devices):
            row, col = source // side, source % side
            if stride == 1:
                target = row * side + (col + step) % side
            else:
                target = ((row + step) % side) * side + col
            route.append((source, target))
        return lax.ppermute(values, "rec", route)

    along = jnp.concatenate([block] + [shifted(block, step, 1) for step in range(1, side)], axis=0)
    whole = jnp.concatenate([along] + [shifted(along, step, side) for step in range(1, side)], axis=0)
    types = jnp.arange(devices, dtype=jnp.int32)
    position = ((outer - types // side) % side) * side + (inner - types % side) % side
    return jnp.take(whole, position, axis=0)


def local(
    signal,
    montage,
    channels,
    lengths,
    boundary,
    conv_in,
    conv_hid,
    mix_weight,
    norm_gain,
    emit_weight,
    trans_within,
    trans_between,
    initial,
):
    groups = lax.axis_size("rec")
    chan_index = lax.axis_index("chan")
    rec_index = lax.axis_index("rec")
    recordings = signal.shape[0]
    patches = signal.shape[2] // SAMP
    slot_ids = chan_index * groups + jnp.arange(groups, dtype=jnp.int32)
    live_slots = slot_ids[None, :] < channels[:, None]
    places = jnp.arange(groups, dtype=jnp.int32)
    pick = (montage[:, 0, None, :] == places[None, :, None]) & live_slots[:, None, :]
    rows = jnp.einsum(
        "bms,bst->mbt", pick.astype(jnp.bfloat16), signal, preferred_element_type=jnp.float32
    ).astype(jnp.bfloat16)
    patch_rows = rows.reshape(groups, recordings, patches, SAMP)
    first_taps = lax.all_gather(conv_in[:, 0], "rec", tiled=True)
    hidden_taps = lax.all_gather(jnp.swapaxes(conv_hid[:, 0], 0, 1), "rec", axis=1, tiled=True)
    extended = halo_rows(patch_rows, HALO)
    partial_value = conv_mix(extended, first_taps, hidden_taps, mix_weight[:, 0], rec_index, patches)
    spread = lax.axis_size("chan")
    pieces = partial_value.reshape(recordings, spread, patches // spread, partial_value.shape[-1])
    pieces = lax.all_to_all(jnp.swapaxes(pieces, 0, 1), "chan", 0, 0, tiled=True)
    summed = jnp.sum(pieces, axis=0)
    average = jnp.mean(summed, axis=-1, keepdims=True)
    centred = summed - average
    variance = jnp.mean(centred * centred, axis=-1, keepdims=True)
    activated = jax.nn.gelu(centred * lax.rsqrt(variance + EPSILON) * norm_gain)
    emission = jnp.einsum("bpo,os->bps", activated, emit_weight, precision=lax.Precision.HIGHEST)
    shared = lax.all_to_all(jnp.broadcast_to(emission[None], (spread,) + emission.shape), "chan", 0, 0, tiled=True)
    emission = jnp.swapaxes(shared, 0, 1).reshape(recordings, patches, STATES)
    positions = rec_index * patches + jnp.arange(patches, dtype=jnp.int32)
    valid = positions[None, :] < lengths[:, None]
    cross = boundary == 1
    filtered, log_partition = crf_forward(
        emission, cross, valid, trans_within, trans_between, initial, rec_index
    )
    return (filtered, log_partition / lengths.astype(jnp.float32))


def solution(mesh):
    placed = (
        P(None, "chan", "rec"),
        P(None, "chan", None),
        P(),
        P(),
        P(None, "rec"),
        P("rec", "chan", None, None, None),
        P("rec", "chan", None, None, None, None),
        P(None, "chan", None, None),
        P(),
        P(),
        P(),
        P(),
        P(),
    )
    return jax.shard_map(
        local, mesh=mesh, in_specs=placed, out_specs=(P(None, None, "rec"), P()), check_vma=False
    )
```

```python
import functools

import jax
import jax.numpy as jnp
from jax import lax
from jax.experimental import pallas as pl
from jax.experimental.pallas import tpu as pltpu
from jax.sharding import PartitionSpec as P

SAMP = 200
EMB = 128
STATES = 5


EPSILON = 1e-05
NEGATIVE = -1e30
MESH_SIDE = 4
SUBSHARDS = 4
HALO = 8


def log_sum_exp(values, along):
    peak_value = jnp.max(values, axis=along, keepdims=True)
    return jnp.squeeze(peak_value, along) + jnp.log(
        jnp.sum(jnp.exp(values - peak_value), axis=along)
    )


LANES = 128


def forward_step(state, matrices, extra):
    terms = [state[i : i + 1, :] + matrices[i] for i in range(len(matrices))]
    peak = functools.reduce(jnp.maximum, terms)
    total = functools.reduce(lambda x, y: x + y, [jnp.exp(t - peak) for t in terms])
    moved = peak + jnp.log(total)
    if extra is not None:
        moved = moved + extra
    top = jnp.max(moved, axis=0, keepdims=True)
    level = top + jnp.log(jnp.sum(jnp.exp(moved - top), axis=0, keepdims=True))
    return moved - level, level


def prefix_kernel(within_ref, between_ref, start_ref, emit_ref, cross_ref, valid_ref, prefix_ref, offset_ref):
    patches = emit_ref.shape[0]
    lanes = start_ref.shape[1]
    within = [jnp.broadcast_to(within_ref[i], (STATES, lanes)) for i in range(STATES)]
    between = [jnp.broadcast_to(between_ref[i], (STATES, lanes)) for i in range(STATES)]

    def body(p, carry):
        state, offset = carry
        crossing = cross_ref[p] > 0.5
        counted = valid_ref[p] > 0.5
        matrices = [jnp.where(crossing, between[i], within[i]) for i in range(STATES)]
        moved, level = forward_step(state, matrices, emit_ref[p])
        state = jnp.where(counted, moved, state)
        offset = offset + jnp.where(counted, level, 0.0)
        prefix_ref[p] = state
        offset_ref[p] = offset
        return state, offset

    lax.fori_loop(0, patches, body, (start_ref[...], jnp.zeros((1, LANES), jnp.float32)), unroll=8)


def chain_kernel(prior_ref, mats_ref, incoming_ref, total_ref):
    count = mats_ref.shape[0]

    def body(k, carry):
        state, total = carry
        incoming_ref[k] = state
        matrices = [mats_ref[k, j] for j in range(STATES)]
        moved, level = forward_step(state, matrices, None)
        return moved, total + level

    _, total = lax.fori_loop(0, count, body, (prior_ref[...], jnp.zeros((1, prior_ref.shape[1]), jnp.float32)))
    total_ref[...] = total


def lanes_padded(values):
    pad = [(0, 0)] * (values.ndim - 1) + [(0, LANES - values.shape[-1])]
    return jnp.pad(values, pad)


def crf_forward(emission, cross, valid, trans_within, trans_between, initial, rec_index):
    recordings, patches, _ = emission.shape
    pieces = SUBSHARDS
    steps = patches // pieces
    block = STATES * recordings
    width = pieces * block

    def to_lanes(values):
        split = values.reshape((recordings, pieces, steps) + values.shape[2:])
        order = (2,) + tuple(range(3, split.ndim)) + (1, 0)
        moved = jnp.transpose(split, order)
        moved = jnp.broadcast_to(moved[..., None, :], moved.shape[:-1] + (STATES, recordings))
        return lanes_padded(moved.reshape(moved.shape[:-3] + (width,)))

    emit_in = to_lanes(emission)
    cross_in = to_lanes(cross.astype(jnp.float32))[:, None, :]
    valid_in = to_lanes(valid.astype(jnp.float32))[:, None, :]
    lane_start = (jnp.arange(width, dtype=jnp.int32) // recordings) % STATES
    basis = jnp.arange(STATES, dtype=jnp.int32)[:, None] == lane_start[None, :]
    start = lanes_padded(jnp.where(basis, 0.0, NEGATIVE).astype(jnp.float32))
    within_in = trans_within[:, :, None]
    between_in = trans_between[:, :, None]
    prefix, offset = pl.pallas_call(
        prefix_kernel,
        out_shape=(
            jax.ShapeDtypeStruct((steps, STATES, LANES), jnp.float32),
            jax.ShapeDtypeStruct((steps, 1, LANES), jnp.float32),
        ),
        cost_estimate=pl.CostEstimate(
            flops=steps * 80 * LANES * 8, transcendentals=steps * 8 * LANES * 8,
            bytes_accessed=steps * 14 * LANES * 4,
        ),
    )(within_in, between_in, start, emit_in, cross_in, valid_in)
    prefix_sj = prefix[:, :, :width].reshape(steps, STATES, pieces, STATES, recordings)
    offset_j = offset[:, 0, :width].reshape(steps, pieces, STATES, recordings)
    transfer = prefix_sj[steps - 1] + offset_j[steps - 1][None]
    transfer = jnp.transpose(transfer, (1, 2, 0, 3))
    gathered = torus_gather(transfer[None], rec_index, MESH_SIDE)
    gathered = gathered.reshape((-1,) + gathered.shape[2:])
    mats = gathered
    prior = initial - log_sum_exp(initial, 0)
    prior_in = jnp.broadcast_to(prior[:, None], (STATES, recordings))
    count = gathered.shape[0]
    incoming, total = pl.pallas_call(
        chain_kernel,
        out_shape=(
            jax.ShapeDtypeStruct((count, STATES, recordings), jnp.float32),
            jax.ShapeDtypeStruct((1, recordings), jnp.float32),
        ),
    )(prior_in, mats)
    here = lax.dynamic_slice_in_dim(incoming, rec_index * pieces, pieces, 0)[:, :, :recordings]
    weights = here[None, None] + offset_j[:, None] + prefix_sj
    reached = log_sum_exp(weights, 3)
    totals = log_sum_exp(reached, 1)
    normalized = reached - totals[:, None]
    filtered = jnp.transpose(normalized, (3, 1, 2, 0)).reshape(recordings, STATES, patches)
    return filtered, total[0, :recordings]

def neighbour_shift(block, axis, distance):
    devices = range(lax.axis_size(axis))
    route = [(i - distance, i) for i in devices if i - distance in devices]
    return lax.ppermute(block, axis, route)


def halo_rows(patch_rows, halo):
    patches = patch_rows.shape[2]
    from_left = neighbour_shift(patch_rows[:, :, patches - halo :], "rec", 1)
    from_right = neighbour_shift(patch_rows[:, :, :halo], "rec", -1)
    return jnp.concatenate([from_left, patch_rows, from_right], axis=2)

def rolled_taps(rows, weight_of, taps):
    reach = taps // 2
    count = rows.shape[0]
    accumulated = None
    for offset in range(taps):
        product = jnp.dot(rows, weight_of(offset), preferred_element_type=jnp.float32)
        shift = (reach - offset) % count
        if shift:
            product = pltpu.roll(product, shift, 0)
        accumulated = product if accumulated is None else accumulated + product
    return accumulated


def merged(ref):
    shape = ref.shape
    return ref[0].reshape(shape[1] * shape[2], shape[3])


def first_kernel(rows_ref, taps_ref, keep_ref, out_ref):
    value = jax.nn.gelu(rolled_taps(merged(rows_ref), lambda k: taps_ref[0, k], taps_ref.shape[1]))
    value = jnp.where(keep_ref[...] > 0.5, value.astype(jnp.bfloat16), jnp.zeros((), jnp.bfloat16))
    out_ref[0] = value.reshape(out_ref.shape[1:])


def residual_layer(current, taps_ref):
    update = jax.nn.gelu(rolled_taps(current, lambda k: taps_ref[0, 0, k], taps_ref.shape[2]))
    return (current.astype(jnp.float32) + update).astype(jnp.bfloat16)


def hidden_kernel(rows_ref, taps_ref, keep_ref, out_ref):
    value = residual_layer(merged(rows_ref), taps_ref)
    value = jnp.where(keep_ref[...] > 0.5, value, jnp.zeros((), jnp.bfloat16))
    out_ref[0] = value.reshape(out_ref.shape[1:])


def last_kernel(rows_ref, taps_ref, keep_ref, mix_ref, out_ref):
    @pl.when(pl.program_id(0) == 0)
    def _():
        out_ref[...] = jnp.zeros_like(out_ref)

    span = rows_ref.shape[2]
    recordings, patches = out_ref.shape[:2]
    margin = (span - patches) // 2
    value = merged(rows_ref)
    layers = taps_ref.shape[0]
    for depth_index in range(layers):
        value = residual_layer(value, taps_ref.at[depth_index : depth_index + 1])
        if depth_index + 1 < layers:
            value = jnp.where(keep_ref[...] > 0.5, value, jnp.zeros((), jnp.bfloat16))
    mixed = jnp.dot(value, mix_ref[0], preferred_element_type=jnp.float32)
    for item in range(recordings):
        start = item * span + margin
        out_ref[item] += mixed[start : start + patches]


def edge_keep(span, margin, rec_index, patches, recordings):
    total = patches * lax.axis_size("rec")
    spot = rec_index * patches - margin + jnp.arange(span, dtype=jnp.int32)
    keep = ((spot >= 0) & (spot < total)).astype(jnp.float32)
    return jnp.tile(jnp.broadcast_to(keep[:, None], (span, EMB)), (recordings, 1))


def per_type_call(kernel, rows, taps, side, out_block, out_shape, out_map, flops, layer=None):
    types, recordings = rows.shape[:2]
    side_spec = (
        pl.BlockSpec((1,) + side.shape[1:], lambda m: (m, 0, 0))
        if kernel is last_kernel
        else pl.BlockSpec(side.shape, lambda m: (0, 0))
    )
    return pl.pallas_call(
        kernel,
        grid=(types,),
        in_specs=[
            pl.BlockSpec((1,) + rows.shape[1:], lambda m: (m, 0, 0, 0)),
            pl.BlockSpec((1,) + taps.shape[1:], lambda m: (m, 0, 0, 0))
            if layer is None
            else pl.BlockSpec((1, 1) + taps.shape[2:], lambda m: (layer, m, 0, 0, 0)),
            side_spec,
        ],
        out_specs=pl.BlockSpec(out_block, out_map),
        out_shape=out_shape,
        compiler_params=pltpu.CompilerParams(dimension_semantics=("arbitrary",)),
        cost_estimate=pl.CostEstimate(
            flops=flops, transcendentals=rows.shape[0] * rows.shape[1] * rows.shape[2] * EMB,
            bytes_accessed=rows.size * 2 + taps.size * 2 // (1 if layer is None else taps.shape[0]) + side.size * 2 + out_shape.size * 4,
        ),
    )(rows, taps, side)


def conv_mix(extended, first_taps, hidden_taps, mix, rec_index, patches):
    types, recordings, span, width = extended.shape
    taps = first_taps.shape[1]
    layers = hidden_taps.shape[0]
    margin = (span - patches) // 2
    keep = edge_keep(span, margin, rec_index, patches, recordings)
    block = (1, recordings, span, EMB)
    inner = jax.ShapeDtypeStruct((types, recordings, span, EMB), jnp.bfloat16)
    current = per_type_call(
        first_kernel, extended, first_taps, keep, block, inner,
        lambda m: (m, 0, 0, 0), 2 * types * recordings * span * width * EMB * taps,
    )
    mix_width = mix.shape[-1]
    return pl.pallas_call(
        last_kernel,
        grid=(types,),
        in_specs=[
            pl.BlockSpec((1,) + current.shape[1:], lambda m: (m, 0, 0, 0)),
            pl.BlockSpec((layers, 1) + hidden_taps.shape[2:], lambda m: (0, m, 0, 0, 0)),
            pl.BlockSpec(keep.shape, lambda m: (0, 0)),
            pl.BlockSpec((1,) + mix.shape[1:], lambda m: (m, 0, 0)),
        ],
        out_specs=pl.BlockSpec((recordings, patches, mix_width), lambda m: (0, 0, 0)),
        out_shape=jax.ShapeDtypeStruct((recordings, patches, mix_width), jnp.float32),
        compiler_params=pltpu.CompilerParams(dimension_semantics=("arbitrary",)),
        cost_estimate=pl.CostEstimate(
            flops=2 * types * recordings * span * EMB * (layers * EMB * taps + mix_width),
            transcendentals=layers * types * recordings * span * EMB,
            bytes_accessed=current.size * 2 + hidden_taps.size * 2 + mix.size * 2 + recordings * patches * mix_width * 4,
        ),
    )(current, hidden_taps, keep, mix)

def torus_gather(block, rec_index, side):
    inner = rec_index % side
    outer = rec_index // side
    devices = side * side

    def shifted(values, step, stride):
        route = []
        for source in range(devices):
            row, col = source // side, source % side
            if stride == 1:
                target = row * side + (col + step) % side
            else:
                target = ((row + step) % side) * side + col
            route.append((source, target))
        return lax.ppermute(values, "rec", route)

    along = jnp.concatenate([block] + [shifted(block, step, 1) for step in range(1, side)], axis=0)
    whole = jnp.concatenate([along] + [shifted(along, step, side) for step in range(1, side)], axis=0)
    types = jnp.arange(devices, dtype=jnp.int32)
    position = ((outer - types // side) % side) * side + (inner - types % side) % side
    return jnp.take(whole, position, axis=0)


def local(
    signal,
    montage,
    channels,
    lengths,
    boundary,
    conv_in,
    conv_hid,
    mix_weight,
    norm_gain,
    emit_weight,
    trans_within,
    trans_between,
    initial,
):
    groups = lax.axis_size("rec")
    chan_index = lax.axis_index("chan")
    rec_index = lax.axis_index("rec")
    recordings = signal.shape[0]
    patches = signal.shape[2] // SAMP
    slot_ids = chan_index * groups + jnp.arange(groups, dtype=jnp.int32)
    live_slots = slot_ids[None, :] < channels[:, None]
    places = jnp.arange(groups, dtype=jnp.int32)
    pick = (montage[:, 0, None, :] == places[None, :, None]) & live_slots[:, None, :]
    rows = jnp.einsum(
        "bms,bst->mbt", pick.astype(jnp.bfloat16), signal, preferred_element_type=jnp.float32
    ).astype(jnp.bfloat16)
    patch_rows = rows.reshape(groups, recordings, patches, SAMP)
    first_taps = lax.all_gather(conv_in[:, 0], "rec", tiled=True)
    hidden_taps = lax.all_gather(jnp.swapaxes(conv_hid[:, 0], 0, 1), "rec", axis=1, tiled=True)
    extended = halo_rows(patch_rows, HALO)
    partial_value = conv_mix(extended, first_taps, hidden_taps, mix_weight[:, 0], rec_index, patches)
    spread = lax.axis_size("chan")
    pieces = partial_value.reshape(recordings, spread, patches // spread, partial_value.shape[-1])
    pieces = lax.all_to_all(jnp.swapaxes(pieces, 0, 1), "chan", 0, 0, tiled=True)
    summed = jnp.sum(pieces, axis=0)
    average = jnp.mean(summed, axis=-1, keepdims=True)
    centred = summed - average
    variance = jnp.mean(centred * centred, axis=-1, keepdims=True)
    activated = jax.nn.gelu(centred * lax.rsqrt(variance + EPSILON) * norm_gain)
    emission = jnp.einsum("bpo,os->bps", activated, emit_weight, precision=lax.Precision.HIGHEST)
    shared = lax.all_to_all(jnp.broadcast_to(emission[None], (spread,) + emission.shape), "chan", 0, 0, tiled=True)
    emission = jnp.swapaxes(shared, 0, 1).reshape(recordings, patches, STATES)
    positions = rec_index * patches + jnp.arange(patches, dtype=jnp.int32)
    valid = positions[None, :] < lengths[:, None]
    cross = boundary == 1
    filtered, log_partition = crf_forward(
        emission, cross, valid, trans_within, trans_between, initial, rec_index
    )
    return (filtered, log_partition / lengths.astype(jnp.float32))


def solution(mesh):
    placed = (
        P(None, "chan", "rec"),
        P(None, "chan", None),
        P(),
        P(),
        P(None, "rec"),
        P("rec", "chan", None, None, None),
        P("rec", "chan", None, None, None, None),
        P(None, "chan", None, None),
        P(),
        P(),
        P(),
        P(),
        P(),
    )
    return jax.shard_map(
        local, mesh=mesh, in_specs=placed, out_specs=(P(None, None, "rec"), P()), check_vma=False
    )
```

```python
import functools

import jax
import jax.numpy as jnp
from jax import lax
from jax.experimental import pallas as pl
from jax.experimental.pallas import tpu as pltpu
from jax.sharding import PartitionSpec as P

SAMP = 200
EMB = 128
STATES = 5


EPSILON = 1e-05
NEGATIVE = -1e30
MESH_SIDE = 4
SUBSHARDS = 4
HALO = 8


def log_sum_exp(values, along):
    peak_value = jnp.max(values, axis=along, keepdims=True)
    return jnp.squeeze(peak_value, along) + jnp.log(
        jnp.sum(jnp.exp(values - peak_value), axis=along)
    )


LANES = 128


def forward_step(state, matrices, extra):
    terms = [state[i : i + 1, :] + matrices[i] for i in range(len(matrices))]
    peak = functools.reduce(jnp.maximum, terms)
    total = functools.reduce(lambda x, y: x + y, [jnp.exp(t - peak) for t in terms])
    moved = peak + jnp.log(total)
    if extra is not None:
        moved = moved + extra
    top = jnp.max(moved, axis=0, keepdims=True)
    level = top + jnp.log(jnp.sum(jnp.exp(moved - top), axis=0, keepdims=True))
    return moved - level, level


def prefix_kernel(within_ref, between_ref, start_ref, emit_ref, cross_ref, valid_ref, prefix_ref, offset_ref):
    patches = emit_ref.shape[0]
    lanes = start_ref.shape[1]
    within = [jnp.broadcast_to(within_ref[i], (STATES, lanes)) for i in range(STATES)]
    between = [jnp.broadcast_to(between_ref[i], (STATES, lanes)) for i in range(STATES)]

    def body(p, carry):
        state, offset = carry
        crossing = cross_ref[p] > 0.5
        counted = valid_ref[p] > 0.5
        matrices = [jnp.where(crossing, between[i], within[i]) for i in range(STATES)]
        moved, level = forward_step(state, matrices, emit_ref[p])
        state = jnp.where(counted, moved, state)
        offset = offset + jnp.where(counted, level, 0.0)
        prefix_ref[p] = state
        offset_ref[p] = offset
        return state, offset

    lax.fori_loop(0, patches, body, (start_ref[...], jnp.zeros((1, LANES), jnp.float32)), unroll=8)


def chain_kernel(prior_ref, mats_ref, incoming_ref, total_ref):
    count = mats_ref.shape[0]

    def body(k, carry):
        state, total = carry
        incoming_ref[k] = state
        matrices = [mats_ref[k, j] for j in range(STATES)]
        moved, level = forward_step(state, matrices, None)
        return moved, total + level

    _, total = lax.fori_loop(0, count, body, (prior_ref[...], jnp.zeros((1, prior_ref.shape[1]), jnp.float32)))
    total_ref[...] = total


def lanes_padded(values):
    pad = [(0, 0)] * (values.ndim - 1) + [(0, LANES - values.shape[-1])]
    return jnp.pad(values, pad)


def crf_forward(emission, cross, valid, trans_within, trans_between, initial, rec_index):
    recordings, patches, _ = emission.shape
    pieces = SUBSHARDS
    steps = patches // pieces
    block = STATES * recordings
    width = pieces * block

    def to_lanes(values):
        split = values.reshape((recordings, pieces, steps) + values.shape[2:])
        order = (2,) + tuple(range(3, split.ndim)) + (1, 0)
        moved = jnp.transpose(split, order)
        moved = jnp.broadcast_to(moved[..., None, :], moved.shape[:-1] + (STATES, recordings))
        return lanes_padded(moved.reshape(moved.shape[:-3] + (width,)))

    emit_in = to_lanes(emission)
    cross_in = to_lanes(cross.astype(jnp.float32))[:, None, :]
    valid_in = to_lanes(valid.astype(jnp.float32))[:, None, :]
    lane_start = (jnp.arange(width, dtype=jnp.int32) // recordings) % STATES
    basis = jnp.arange(STATES, dtype=jnp.int32)[:, None] == lane_start[None, :]
    start = lanes_padded(jnp.where(basis, 0.0, NEGATIVE).astype(jnp.float32))
    within_in = trans_within[:, :, None]
    between_in = trans_between[:, :, None]
    prefix, offset = pl.pallas_call(
        prefix_kernel,
        out_shape=(
            jax.ShapeDtypeStruct((steps, STATES, LANES), jnp.float32),
            jax.ShapeDtypeStruct((steps, 1, LANES), jnp.float32),
        ),
        cost_estimate=pl.CostEstimate(
            flops=steps * 80 * LANES * 8, transcendentals=steps * 8 * LANES * 8,
            bytes_accessed=steps * 14 * LANES * 4,
        ),
    )(within_in, between_in, start, emit_in, cross_in, valid_in)
    prefix_sj = prefix[:, :, :width].reshape(steps, STATES, pieces, STATES, recordings)
    offset_j = offset[:, 0, :width].reshape(steps, pieces, STATES, recordings)
    transfer = prefix_sj[steps - 1] + offset_j[steps - 1][None]
    transfer = jnp.transpose(transfer, (1, 2, 0, 3))
    gathered = torus_gather(transfer[None], rec_index, MESH_SIDE)
    gathered = gathered.reshape((-1,) + gathered.shape[2:])
    mats = gathered
    prior = initial - log_sum_exp(initial, 0)
    prior_in = jnp.broadcast_to(prior[:, None], (STATES, recordings))
    count = gathered.shape[0]
    incoming, total = pl.pallas_call(
        chain_kernel,
        out_shape=(
            jax.ShapeDtypeStruct((count, STATES, recordings), jnp.float32),
            jax.ShapeDtypeStruct((1, recordings), jnp.float32),
        ),
    )(prior_in, mats)
    here = lax.dynamic_slice_in_dim(incoming, rec_index * pieces, pieces, 0)[:, :, :recordings]
    weights = here[None, None] + offset_j[:, None] + prefix_sj
    reached = log_sum_exp(weights, 3)
    totals = log_sum_exp(reached, 1)
    normalized = reached - totals[:, None]
    filtered = jnp.transpose(normalized, (3, 1, 2, 0)).reshape(recordings, STATES, patches)
    return filtered, total[0, :recordings]

def neighbour_shift(block, axis, distance):
    devices = range(lax.axis_size(axis))
    route = [(i - distance, i) for i in devices if i - distance in devices]
    return lax.ppermute(block, axis, route)


def halo_rows(patch_rows, halo):
    patches = patch_rows.shape[2]
    from_left = neighbour_shift(patch_rows[:, :, patches - halo :], "rec", 1)
    from_right = neighbour_shift(patch_rows[:, :, :halo], "rec", -1)
    return jnp.concatenate([from_left, patch_rows, from_right], axis=2)

def rolled_taps(rows, weight_of, taps):
    reach = taps // 2
    count = rows.shape[0]
    accumulated = None
    for offset in range(taps):
        product = jnp.dot(rows, weight_of(offset), preferred_element_type=jnp.float32)
        shift = (reach - offset) % count
        if shift:
            product = pltpu.roll(product, shift, 0)
        accumulated = product if accumulated is None else accumulated + product
    return accumulated


def merged(ref):
    shape = ref.shape
    return ref[0].reshape(shape[1] * shape[2], shape[3])


def first_kernel(rows_ref, taps_ref, keep_ref, out_ref):
    value = jax.nn.gelu(rolled_taps(merged(rows_ref), lambda k: taps_ref[0, k], taps_ref.shape[1]))
    value = jnp.where(keep_ref[...] > 0.5, value.astype(jnp.bfloat16), jnp.zeros((), jnp.bfloat16))
    out_ref[0] = value.reshape(out_ref.shape[1:])


def residual_layer(current, taps_ref):
    update = jax.nn.gelu(rolled_taps(current, lambda k: taps_ref[0, 0, k], taps_ref.shape[2]))
    return (current.astype(jnp.float32) + update).astype(jnp.bfloat16)


def hidden_kernel(rows_ref, taps_ref, keep_ref, out_ref):
    value = residual_layer(merged(rows_ref), taps_ref)
    value = jnp.where(keep_ref[...] > 0.5, value, jnp.zeros((), jnp.bfloat16))
    out_ref[0] = value.reshape(out_ref.shape[1:])


def last_kernel(rows_ref, taps_ref, keep_ref, mix_ref, out_ref):
    @pl.when(pl.program_id(0) == 0)
    def _():
        out_ref[...] = jnp.zeros_like(out_ref)

    span = rows_ref.shape[2]
    chunks, recordings, piece = out_ref.shape[:3]
    patches = chunks * piece
    margin = (span - patches) // 2
    value = merged(rows_ref)
    layers = taps_ref.shape[0]
    for depth_index in range(layers):
        value = residual_layer(value, taps_ref.at[depth_index : depth_index + 1])
        if depth_index + 1 < layers:
            value = jnp.where(keep_ref[...] > 0.5, value, jnp.zeros((), jnp.bfloat16))
    mixed = jnp.dot(value, mix_ref[0], preferred_element_type=jnp.float32)
    for item in range(recordings):
        for chunk in range(chunks):
            start = item * span + margin + chunk * piece
            out_ref[chunk, item] += mixed[start : start + piece]


def edge_keep(span, margin, rec_index, patches, recordings):
    total = patches * lax.axis_size("rec")
    spot = rec_index * patches - margin + jnp.arange(span, dtype=jnp.int32)
    keep = ((spot >= 0) & (spot < total)).astype(jnp.float32)
    return jnp.tile(jnp.broadcast_to(keep[:, None], (span, EMB)), (recordings, 1))


def per_type_call(kernel, rows, taps, side, out_block, out_shape, out_map, flops, layer=None):
    types, recordings = rows.shape[:2]
    side_spec = (
        pl.BlockSpec((1,) + side.shape[1:], lambda m: (m, 0, 0))
        if kernel is last_kernel
        else pl.BlockSpec(side.shape, lambda m: (0, 0))
    )
    return pl.pallas_call(
        kernel,
        grid=(types,),
        in_specs=[
            pl.BlockSpec((1,) + rows.shape[1:], lambda m: (m, 0, 0, 0)),
            pl.BlockSpec((1,) + taps.shape[1:], lambda m: (m, 0, 0, 0))
            if layer is None
            else pl.BlockSpec((1, 1) + taps.shape[2:], lambda m: (layer, m, 0, 0, 0)),
            side_spec,
        ],
        out_specs=pl.BlockSpec(out_block, out_map),
        out_shape=out_shape,
        compiler_params=pltpu.CompilerParams(dimension_semantics=("arbitrary",)),
        cost_estimate=pl.CostEstimate(
            flops=flops, transcendentals=rows.shape[0] * rows.shape[1] * rows.shape[2] * EMB,
            bytes_accessed=rows.size * 2 + taps.size * 2 // (1 if layer is None else taps.shape[0]) + side.size * 2 + out_shape.size * 4,
        ),
    )(rows, taps, side)


def conv_mix(extended, first_taps, hidden_taps, mix, rec_index, patches):
    types, recordings, span, width = extended.shape
    taps = first_taps.shape[1]
    layers = hidden_taps.shape[0]
    margin = (span - patches) // 2
    keep = edge_keep(span, margin, rec_index, patches, recordings)
    block = (1, recordings, span, EMB)
    inner = jax.ShapeDtypeStruct((types, recordings, span, EMB), jnp.bfloat16)
    current = per_type_call(
        first_kernel, extended, first_taps, keep, block, inner,
        lambda m: (m, 0, 0, 0), 2 * types * recordings * span * width * EMB * taps,
    )
    mix_width = mix.shape[-1]
    spread = lax.axis_size("chan")
    return pl.pallas_call(
        last_kernel,
        grid=(types,),
        in_specs=[
            pl.BlockSpec((1,) + current.shape[1:], lambda m: (m, 0, 0, 0)),
            pl.BlockSpec((layers, 1) + hidden_taps.shape[2:], lambda m: (0, m, 0, 0, 0)),
            pl.BlockSpec(keep.shape, lambda m: (0, 0)),
            pl.BlockSpec((1,) + mix.shape[1:], lambda m: (m, 0, 0)),
        ],
        out_specs=pl.BlockSpec((spread, recordings, patches // spread, mix_width), lambda m: (0, 0, 0, 0)),
        out_shape=jax.ShapeDtypeStruct((spread, recordings, patches // spread, mix_width), jnp.float32),
        compiler_params=pltpu.CompilerParams(dimension_semantics=("arbitrary",)),
        cost_estimate=pl.CostEstimate(
            flops=2 * types * recordings * span * EMB * (layers * EMB * taps + mix_width),
            transcendentals=layers * types * recordings * span * EMB,
            bytes_accessed=current.size * 2 + hidden_taps.size * 2 + mix.size * 2 + recordings * patches * mix_width * 4,
        ),
    )(current, hidden_taps, keep, mix)

def torus_gather(block, rec_index, side):
    inner = rec_index % side
    outer = rec_index // side
    devices = side * side

    def shifted(values, step, stride):
        route = []
        for source in range(devices):
            row, col = source // side, source % side
            if stride == 1:
                target = row * side + (col + step) % side
            else:
                target = ((row + step) % side) * side + col
            route.append((source, target))
        return lax.ppermute(values, "rec", route)

    along = jnp.concatenate([block] + [shifted(block, step, 1) for step in range(1, side)], axis=0)
    whole = jnp.concatenate([along] + [shifted(along, step, side) for step in range(1, side)], axis=0)
    types = jnp.arange(devices, dtype=jnp.int32)
    position = ((outer - types // side) % side) * side + (inner - types % side) % side
    return jnp.take(whole, position, axis=0)


def local(
    signal,
    montage,
    channels,
    lengths,
    boundary,
    conv_in,
    conv_hid,
    mix_weight,
    norm_gain,
    emit_weight,
    trans_within,
    trans_between,
    initial,
):
    groups = lax.axis_size("rec")
    chan_index = lax.axis_index("chan")
    rec_index = lax.axis_index("rec")
    recordings = signal.shape[0]
    patches = signal.shape[2] // SAMP
    slot_ids = chan_index * groups + jnp.arange(groups, dtype=jnp.int32)
    live_slots = slot_ids[None, :] < channels[:, None]
    places = jnp.arange(groups, dtype=jnp.int32)
    pick = (montage[:, 0, None, :] == places[None, :, None]) & live_slots[:, None, :]
    rows = jnp.einsum(
        "bms,bst->mbt", pick.astype(jnp.bfloat16), signal, preferred_element_type=jnp.float32
    ).astype(jnp.bfloat16)
    patch_rows = rows.reshape(groups, recordings, patches, SAMP)
    first_taps = lax.all_gather(conv_in[:, 0], "rec", tiled=True)
    hidden_taps = lax.all_gather(jnp.swapaxes(conv_hid[:, 0], 0, 1), "rec", axis=1, tiled=True)
    extended = halo_rows(patch_rows, HALO)
    partial_value = conv_mix(extended, first_taps, hidden_taps, mix_weight[:, 0], rec_index, patches)
    spread = lax.axis_size("chan")
    pieces = lax.all_to_all(partial_value, "chan", 0, 0, tiled=True)
    summed = jnp.sum(pieces, axis=0)
    average = jnp.mean(summed, axis=-1, keepdims=True)
    centred = summed - average
    variance = jnp.mean(centred * centred, axis=-1, keepdims=True)
    activated = jax.nn.gelu(centred * lax.rsqrt(variance + EPSILON) * norm_gain)
    emission = jnp.einsum("bpo,os->bps", activated, emit_weight, precision=lax.Precision.HIGHEST)
    shared = lax.all_to_all(jnp.broadcast_to(emission[None], (spread,) + emission.shape), "chan", 0, 0, tiled=True)
    emission = jnp.swapaxes(shared, 0, 1).reshape(recordings, patches, STATES)
    positions = rec_index * patches + jnp.arange(patches, dtype=jnp.int32)
    valid = positions[None, :] < lengths[:, None]
    cross = boundary == 1
    filtered, log_partition = crf_forward(
        emission, cross, valid, trans_within, trans_between, initial, rec_index
    )
    return (filtered, log_partition / lengths.astype(jnp.float32))


def solution(mesh):
    placed = (
        P(None, "chan", "rec"),
        P(None, "chan", None),
        P(),
        P(),
        P(None, "rec"),
        P("rec", "chan", None, None, None),
        P("rec", "chan", None, None, None, None),
        P(None, "chan", None, None),
        P(),
        P(),
        P(),
        P(),
        P(),
    )
    return jax.shard_map(
        local, mesh=mesh, in_specs=placed, out_specs=(P(None, None, "rec"), P()), check_vma=False
    )
```

```python
import functools

import jax
import jax.numpy as jnp
from jax import lax
from jax.experimental import pallas as pl
from jax.experimental.pallas import tpu as pltpu
from jax.sharding import PartitionSpec as P

SAMP = 200
EMB = 128
STATES = 5


EPSILON = 1e-05
NEGATIVE = -1e30
MESH_SIDE = 4
SUBSHARDS = 4
HALO = 8


def log_sum_exp(values, along):
    peak_value = jnp.max(values, axis=along, keepdims=True)
    return jnp.squeeze(peak_value, along) + jnp.log(
        jnp.sum(jnp.exp(values - peak_value), axis=along)
    )


LANES = 128


def forward_step(state, matrices, extra):
    terms = [state[i : i + 1, :] + matrices[i] for i in range(len(matrices))]
    peak = functools.reduce(jnp.maximum, terms)
    total = functools.reduce(lambda x, y: x + y, [jnp.exp(t - peak) for t in terms])
    moved = peak + jnp.log(total)
    if extra is not None:
        moved = moved + extra
    top = jnp.max(moved, axis=0, keepdims=True)
    level = top + jnp.log(jnp.sum(jnp.exp(moved - top), axis=0, keepdims=True))
    return moved - level, level


def prefix_kernel(within_ref, between_ref, start_ref, emit_ref, cross_ref, valid_ref, prefix_ref, offset_ref):
    patches = emit_ref.shape[0]
    lanes = start_ref.shape[1]
    within = [jnp.broadcast_to(within_ref[i], (STATES, lanes)) for i in range(STATES)]
    between = [jnp.broadcast_to(between_ref[i], (STATES, lanes)) for i in range(STATES)]

    def body(p, carry):
        state, offset = carry
        crossing = cross_ref[p] > 0.5
        counted = valid_ref[p] > 0.5
        matrices = [jnp.where(crossing, between[i], within[i]) for i in range(STATES)]
        moved, level = forward_step(state, matrices, emit_ref[p])
        state = jnp.where(counted, moved, state)
        offset = offset + jnp.where(counted, level, 0.0)
        prefix_ref[p] = state
        offset_ref[p] = offset
        return state, offset

    lax.fori_loop(0, patches, body, (start_ref[...], jnp.zeros((1, LANES), jnp.float32)), unroll=8)


def chain_kernel(prior_ref, mats_ref, incoming_ref, total_ref):
    count = mats_ref.shape[0]

    def body(k, carry):
        state, total = carry
        incoming_ref[k] = state
        matrices = [mats_ref[k, j] for j in range(STATES)]
        moved, level = forward_step(state, matrices, None)
        return moved, total + level

    _, total = lax.fori_loop(0, count, body, (prior_ref[...], jnp.zeros((1, prior_ref.shape[1]), jnp.float32)), unroll=8)
    total_ref[...] = total


def lanes_padded(values):
    pad = [(0, 0)] * (values.ndim - 1) + [(0, LANES - values.shape[-1])]
    return jnp.pad(values, pad)


def crf_forward(emission, cross, valid, trans_within, trans_between, initial, rec_index):
    recordings, patches, _ = emission.shape
    pieces = SUBSHARDS
    steps = patches // pieces
    block = STATES * recordings
    width = pieces * block

    def to_lanes(values):
        split = values.reshape((recordings, pieces, steps) + values.shape[2:])
        order = (2,) + tuple(range(3, split.ndim)) + (1, 0)
        moved = jnp.transpose(split, order)
        moved = jnp.broadcast_to(moved[..., None, :], moved.shape[:-1] + (STATES, recordings))
        return lanes_padded(moved.reshape(moved.shape[:-3] + (width,)))

    emit_in = to_lanes(emission)
    cross_in = to_lanes(cross.astype(jnp.float32))[:, None, :]
    valid_in = to_lanes(valid.astype(jnp.float32))[:, None, :]
    lane_start = (jnp.arange(width, dtype=jnp.int32) // recordings) % STATES
    basis = jnp.arange(STATES, dtype=jnp.int32)[:, None] == lane_start[None, :]
    start = lanes_padded(jnp.where(basis, 0.0, NEGATIVE).astype(jnp.float32))
    within_in = trans_within[:, :, None]
    between_in = trans_between[:, :, None]
    prefix, offset = pl.pallas_call(
        prefix_kernel,
        out_shape=(
            jax.ShapeDtypeStruct((steps, STATES, LANES), jnp.float32),
            jax.ShapeDtypeStruct((steps, 1, LANES), jnp.float32),
        ),
        cost_estimate=pl.CostEstimate(
            flops=steps * 80 * LANES * 8, transcendentals=steps * 8 * LANES * 8,
            bytes_accessed=steps * 14 * LANES * 4,
        ),
    )(within_in, between_in, start, emit_in, cross_in, valid_in)
    prefix_sj = prefix[:, :, :width].reshape(steps, STATES, pieces, STATES, recordings)
    offset_j = offset[:, 0, :width].reshape(steps, pieces, STATES, recordings)
    transfer = prefix_sj[steps - 1] + offset_j[steps - 1][None]
    transfer = jnp.transpose(transfer, (1, 2, 0, 3))
    gathered = torus_gather(transfer[None], rec_index, MESH_SIDE)
    gathered = gathered.reshape((-1,) + gathered.shape[2:])
    mats = gathered
    prior = initial - log_sum_exp(initial, 0)
    prior_in = jnp.broadcast_to(prior[:, None], (STATES, recordings))
    count = gathered.shape[0]
    incoming, total = pl.pallas_call(
        chain_kernel,
        out_shape=(
            jax.ShapeDtypeStruct((count, STATES, recordings), jnp.float32),
            jax.ShapeDtypeStruct((1, recordings), jnp.float32),
        ),
    )(prior_in, mats)
    here = lax.dynamic_slice_in_dim(incoming, rec_index * pieces, pieces, 0)[:, :, :recordings]
    weights = here[None, None] + offset_j[:, None] + prefix_sj
    reached = log_sum_exp(weights, 3)
    totals = log_sum_exp(reached, 1)
    normalized = reached - totals[:, None]
    filtered = jnp.transpose(normalized, (3, 1, 2, 0)).reshape(recordings, STATES, patches)
    return filtered, total[0, :recordings]

def neighbour_shift(block, axis, distance):
    devices = range(lax.axis_size(axis))
    route = [(i - distance, i) for i in devices if i - distance in devices]
    return lax.ppermute(block, axis, route)


def halo_rows(patch_rows, halo):
    patches = patch_rows.shape[2]
    from_left = neighbour_shift(patch_rows[:, :, patches - halo :], "rec", 1)
    from_right = neighbour_shift(patch_rows[:, :, :halo], "rec", -1)
    return jnp.concatenate([from_left, patch_rows, from_right], axis=2)

def rolled_taps(rows, weight_of, taps):
    reach = taps // 2
    count = rows.shape[0]
    accumulated = None
    for offset in range(taps):
        product = jnp.dot(rows, weight_of(offset), preferred_element_type=jnp.float32)
        shift = (reach - offset) % count
        if shift:
            product = pltpu.roll(product, shift, 0)
        accumulated = product if accumulated is None else accumulated + product
    return accumulated


def merged(ref):
    shape = ref.shape
    return ref[0].reshape(shape[1] * shape[2], shape[3])


def first_kernel(rows_ref, taps_ref, keep_ref, out_ref):
    value = jax.nn.gelu(rolled_taps(merged(rows_ref), lambda k: taps_ref[0, k], taps_ref.shape[1]))
    value = jnp.where(keep_ref[...] > 0.5, value.astype(jnp.bfloat16), jnp.zeros((), jnp.bfloat16))
    out_ref[0] = value.reshape(out_ref.shape[1:])


def residual_layer(current, taps_ref):
    update = jax.nn.gelu(rolled_taps(current, lambda k: taps_ref[0, 0, k], taps_ref.shape[2]))
    return (current.astype(jnp.float32) + update).astype(jnp.bfloat16)


def hidden_kernel(rows_ref, taps_ref, keep_ref, out_ref):
    value = residual_layer(merged(rows_ref), taps_ref)
    value = jnp.where(keep_ref[...] > 0.5, value, jnp.zeros((), jnp.bfloat16))
    out_ref[0] = value.reshape(out_ref.shape[1:])


def last_kernel(rows_ref, taps_ref, keep_ref, mix_ref, out_ref):
    @pl.when(pl.program_id(0) == 0)
    def _():
        out_ref[...] = jnp.zeros_like(out_ref)

    span = rows_ref.shape[2]
    chunks, recordings, piece = out_ref.shape[:3]
    patches = chunks * piece
    margin = (span - patches) // 2
    value = merged(rows_ref)
    layers = taps_ref.shape[0]
    for depth_index in range(layers):
        value = residual_layer(value, taps_ref.at[depth_index : depth_index + 1])
        if depth_index + 1 < layers:
            value = jnp.where(keep_ref[...] > 0.5, value, jnp.zeros((), jnp.bfloat16))
    mixed = jnp.dot(value, mix_ref[0], preferred_element_type=jnp.float32)
    for item in range(recordings):
        for chunk in range(chunks):
            start = item * span + margin + chunk * piece
            out_ref[chunk, item] += mixed[start : start + piece]


def edge_keep(span, margin, rec_index, patches, recordings):
    total = patches * lax.axis_size("rec")
    spot = rec_index * patches - margin + jnp.arange(span, dtype=jnp.int32)
    keep = ((spot >= 0) & (spot < total)).astype(jnp.float32)
    return jnp.tile(jnp.broadcast_to(keep[:, None], (span, EMB)), (recordings, 1))


def per_type_call(kernel, rows, taps, side, out_block, out_shape, out_map, flops, layer=None):
    types, recordings = rows.shape[:2]
    side_spec = (
        pl.BlockSpec((1,) + side.shape[1:], lambda m: (m, 0, 0))
        if kernel is last_kernel
        else pl.BlockSpec(side.shape, lambda m: (0, 0))
    )
    return pl.pallas_call(
        kernel,
        grid=(types,),
        in_specs=[
            pl.BlockSpec((1,) + rows.shape[1:], lambda m: (m, 0, 0, 0)),
            pl.BlockSpec((1,) + taps.shape[1:], lambda m: (m, 0, 0, 0))
            if layer is None
            else pl.BlockSpec((1, 1) + taps.shape[2:], lambda m: (layer, m, 0, 0, 0)),
            side_spec,
        ],
        out_specs=pl.BlockSpec(out_block, out_map),
        out_shape=out_shape,
        compiler_params=pltpu.CompilerParams(dimension_semantics=("arbitrary",)),
        cost_estimate=pl.CostEstimate(
            flops=flops, transcendentals=rows.shape[0] * rows.shape[1] * rows.shape[2] * EMB,
            bytes_accessed=rows.size * 2 + taps.size * 2 // (1 if layer is None else taps.shape[0]) + side.size * 2 + out_shape.size * 4,
        ),
    )(rows, taps, side)


def conv_mix(extended, first_taps, hidden_taps, mix, rec_index, patches):
    types, recordings, span, width = extended.shape
    taps = first_taps.shape[1]
    layers = hidden_taps.shape[0]
    margin = (span - patches) // 2
    keep = edge_keep(span, margin, rec_index, patches, recordings)
    block = (1, recordings, span, EMB)
    inner = jax.ShapeDtypeStruct((types, recordings, span, EMB), jnp.bfloat16)
    current = per_type_call(
        first_kernel, extended, first_taps, keep, block, inner,
        lambda m: (m, 0, 0, 0), 2 * types * recordings * span * width * EMB * taps,
    )
    mix_width = mix.shape[-1]
    spread = lax.axis_size("chan")
    return pl.pallas_call(
        last_kernel,
        grid=(types,),
        in_specs=[
            pl.BlockSpec((1,) + current.shape[1:], lambda m: (m, 0, 0, 0)),
            pl.BlockSpec((layers, 1) + hidden_taps.shape[2:], lambda m: (0, m, 0, 0, 0)),
            pl.BlockSpec(keep.shape, lambda m: (0, 0)),
            pl.BlockSpec((1,) + mix.shape[1:], lambda m: (m, 0, 0)),
        ],
        out_specs=pl.BlockSpec((spread, recordings, patches // spread, mix_width), lambda m: (0, 0, 0, 0)),
        out_shape=jax.ShapeDtypeStruct((spread, recordings, patches // spread, mix_width), jnp.float32),
        compiler_params=pltpu.CompilerParams(dimension_semantics=("arbitrary",)),
        cost_estimate=pl.CostEstimate(
            flops=2 * types * recordings * span * EMB * (layers * EMB * taps + mix_width),
            transcendentals=layers * types * recordings * span * EMB,
            bytes_accessed=current.size * 2 + hidden_taps.size * 2 + mix.size * 2 + recordings * patches * mix_width * 4,
        ),
    )(current, hidden_taps, keep, mix)

def torus_gather(block, rec_index, side):
    inner = rec_index % side
    outer = rec_index // side
    devices = side * side

    def shifted(values, step, stride):
        route = []
        for source in range(devices):
            row, col = source // side, source % side
            if stride == 1:
                target = row * side + (col + step) % side
            else:
                target = ((row + step) % side) * side + col
            route.append((source, target))
        return lax.ppermute(values, "rec", route)

    along = jnp.concatenate([block] + [shifted(block, step, 1) for step in range(1, side)], axis=0)
    whole = jnp.concatenate([along] + [shifted(along, step, side) for step in range(1, side)], axis=0)
    types = jnp.arange(devices, dtype=jnp.int32)
    position = ((outer - types // side) % side) * side + (inner - types % side) % side
    return jnp.take(whole, position, axis=0)


def local(
    signal,
    montage,
    channels,
    lengths,
    boundary,
    conv_in,
    conv_hid,
    mix_weight,
    norm_gain,
    emit_weight,
    trans_within,
    trans_between,
    initial,
):
    groups = lax.axis_size("rec")
    chan_index = lax.axis_index("chan")
    rec_index = lax.axis_index("rec")
    recordings = signal.shape[0]
    patches = signal.shape[2] // SAMP
    slot_ids = chan_index * groups + jnp.arange(groups, dtype=jnp.int32)
    live_slots = slot_ids[None, :] < channels[:, None]
    places = jnp.arange(groups, dtype=jnp.int32)
    pick = (montage[:, 0, None, :] == places[None, :, None]) & live_slots[:, None, :]
    rows = jnp.einsum(
        "bms,bst->mbt", pick.astype(jnp.bfloat16), signal, preferred_element_type=jnp.float32
    ).astype(jnp.bfloat16)
    patch_rows = rows.reshape(groups, recordings, patches, SAMP)
    first_taps = lax.all_gather(conv_in[:, 0], "rec", tiled=True)
    hidden_taps = lax.all_gather(jnp.swapaxes(conv_hid[:, 0], 0, 1), "rec", axis=1, tiled=True)
    extended = halo_rows(patch_rows, HALO)
    partial_value = conv_mix(extended, first_taps, hidden_taps, mix_weight[:, 0], rec_index, patches)
    spread = lax.axis_size("chan")
    pieces = lax.all_to_all(partial_value, "chan", 0, 0, tiled=True)
    summed = jnp.sum(pieces, axis=0)
    average = jnp.mean(summed, axis=-1, keepdims=True)
    centred = summed - average
    variance = jnp.mean(centred * centred, axis=-1, keepdims=True)
    activated = jax.nn.gelu(centred * lax.rsqrt(variance + EPSILON) * norm_gain)
    emission = jnp.einsum("bpo,os->bps", activated, emit_weight, precision=lax.Precision.HIGHEST)
    shared = lax.all_to_all(jnp.broadcast_to(emission[None], (spread,) + emission.shape), "chan", 0, 0, tiled=True)
    emission = jnp.swapaxes(shared, 0, 1).reshape(recordings, patches, STATES)
    positions = rec_index * patches + jnp.arange(patches, dtype=jnp.int32)
    valid = positions[None, :] < lengths[:, None]
    cross = boundary == 1
    filtered, log_partition = crf_forward(
        emission, cross, valid, trans_within, trans_between, initial, rec_index
    )
    return (filtered, log_partition / lengths.astype(jnp.float32))


def solution(mesh):
    placed = (
        P(None, "chan", "rec"),
        P(None, "chan", None),
        P(),
        P(),
        P(None, "rec"),
        P("rec", "chan", None, None, None),
        P("rec", "chan", None, None, None, None),
        P(None, "chan", None, None),
        P(),
        P(),
        P(),
        P(),
        P(),
    )
    return jax.shard_map(
        local, mesh=mesh, in_specs=placed, out_specs=(P(None, None, "rec"), P()), check_vma=False
    )
```

```python
import functools

import jax
import jax.numpy as jnp
from jax import lax
from jax.experimental import pallas as pl
from jax.experimental.pallas import tpu as pltpu
from jax.sharding import PartitionSpec as P

SAMP = 200
EMB = 128
STATES = 5


EPSILON = 1e-05
NEGATIVE = -1e30
MESH_SIDE = 4
SUBSHARDS = 4
HALO = 8


def log_sum_exp(values, along):
    peak_value = jnp.max(values, axis=along, keepdims=True)
    return jnp.squeeze(peak_value, along) + jnp.log(
        jnp.sum(jnp.exp(values - peak_value), axis=along)
    )


LANES = 128


def forward_step(state, matrices, extra):
    terms = [state[i : i + 1, :] + matrices[i] for i in range(len(matrices))]
    peak = functools.reduce(jnp.maximum, terms)
    total = functools.reduce(lambda x, y: x + y, [jnp.exp(t - peak) for t in terms])
    moved = peak + jnp.log(total)
    if extra is not None:
        moved = moved + extra
    top = jnp.max(moved, axis=0, keepdims=True)
    level = top + jnp.log(jnp.sum(jnp.exp(moved - top), axis=0, keepdims=True))
    return moved - level, level


def prefix_kernel(within_ref, between_ref, start_ref, emit_ref, cross_ref, valid_ref, prefix_ref, offset_ref):
    patches = emit_ref.shape[0]
    lanes = start_ref.shape[1]
    within = [jnp.broadcast_to(within_ref[i], (STATES, lanes)) for i in range(STATES)]
    between = [jnp.broadcast_to(between_ref[i], (STATES, lanes)) for i in range(STATES)]

    def body(p, carry):
        state, offset = carry
        crossing = cross_ref[p] > 0.5
        counted = valid_ref[p] > 0.5
        matrices = [jnp.where(crossing, between[i], within[i]) for i in range(STATES)]
        moved, level = forward_step(state, matrices, emit_ref[p])
        state = jnp.where(counted, moved, state)
        offset = offset + jnp.where(counted, level, 0.0)
        prefix_ref[p] = state
        offset_ref[p] = offset
        return state, offset

    lax.fori_loop(0, patches, body, (start_ref[...], jnp.zeros((1, LANES), jnp.float32)), unroll=True)


def chain_kernel(prior_ref, mats_ref, incoming_ref, total_ref):
    count = mats_ref.shape[0]

    def body(k, carry):
        state, total = carry
        incoming_ref[k] = state
        matrices = [mats_ref[k, j] for j in range(STATES)]
        moved, level = forward_step(state, matrices, None)
        return moved, total + level

    _, total = lax.fori_loop(0, count, body, (prior_ref[...], jnp.zeros((1, prior_ref.shape[1]), jnp.float32)), unroll=8)
    total_ref[...] = total


def lanes_padded(values):
    pad = [(0, 0)] * (values.ndim - 1) + [(0, LANES - values.shape[-1])]
    return jnp.pad(values, pad)


def crf_forward(emission, cross, valid, trans_within, trans_between, initial, rec_index):
    recordings, patches, _ = emission.shape
    pieces = SUBSHARDS
    steps = patches // pieces
    block = STATES * recordings
    width = pieces * block

    def to_lanes(values):
        split = values.reshape((recordings, pieces, steps) + values.shape[2:])
        order = (2,) + tuple(range(3, split.ndim)) + (1, 0)
        moved = jnp.transpose(split, order)
        moved = jnp.broadcast_to(moved[..., None, :], moved.shape[:-1] + (STATES, recordings))
        return lanes_padded(moved.reshape(moved.shape[:-3] + (width,)))

    emit_in = to_lanes(emission)
    cross_in = to_lanes(cross.astype(jnp.float32))[:, None, :]
    valid_in = to_lanes(valid.astype(jnp.float32))[:, None, :]
    lane_start = (jnp.arange(width, dtype=jnp.int32) // recordings) % STATES
    basis = jnp.arange(STATES, dtype=jnp.int32)[:, None] == lane_start[None, :]
    start = lanes_padded(jnp.where(basis, 0.0, NEGATIVE).astype(jnp.float32))
    within_in = trans_within[:, :, None]
    between_in = trans_between[:, :, None]
    prefix, offset = pl.pallas_call(
        prefix_kernel,
        out_shape=(
            jax.ShapeDtypeStruct((steps, STATES, LANES), jnp.float32),
            jax.ShapeDtypeStruct((steps, 1, LANES), jnp.float32),
        ),
        cost_estimate=pl.CostEstimate(
            flops=steps * 80 * LANES * 8, transcendentals=steps * 8 * LANES * 8,
            bytes_accessed=steps * 14 * LANES * 4,
        ),
    )(within_in, between_in, start, emit_in, cross_in, valid_in)
    prefix_sj = prefix[:, :, :width].reshape(steps, STATES, pieces, STATES, recordings)
    offset_j = offset[:, 0, :width].reshape(steps, pieces, STATES, recordings)
    transfer = prefix_sj[steps - 1] + offset_j[steps - 1][None]
    transfer = jnp.transpose(transfer, (1, 2, 0, 3))
    gathered = torus_gather(transfer[None], rec_index, MESH_SIDE)
    gathered = gathered.reshape((-1,) + gathered.shape[2:])
    mats = gathered
    prior = initial - log_sum_exp(initial, 0)
    prior_in = jnp.broadcast_to(prior[:, None], (STATES, recordings))
    count = gathered.shape[0]
    incoming, total = pl.pallas_call(
        chain_kernel,
        out_shape=(
            jax.ShapeDtypeStruct((count, STATES, recordings), jnp.float32),
            jax.ShapeDtypeStruct((1, recordings), jnp.float32),
        ),
    )(prior_in, mats)
    here = lax.dynamic_slice_in_dim(incoming, rec_index * pieces, pieces, 0)[:, :, :recordings]
    weights = here[None, None] + offset_j[:, None] + prefix_sj
    reached = log_sum_exp(weights, 3)
    totals = log_sum_exp(reached, 1)
    normalized = reached - totals[:, None]
    filtered = jnp.transpose(normalized, (3, 1, 2, 0)).reshape(recordings, STATES, patches)
    return filtered, total[0, :recordings]

def neighbour_shift(block, axis, distance):
    devices = range(lax.axis_size(axis))
    route = [(i - distance, i) for i in devices if i - distance in devices]
    return lax.ppermute(block, axis, route)


def halo_rows(patch_rows, halo):
    patches = patch_rows.shape[2]
    from_left = neighbour_shift(patch_rows[:, :, patches - halo :], "rec", 1)
    from_right = neighbour_shift(patch_rows[:, :, :halo], "rec", -1)
    return jnp.concatenate([from_left, patch_rows, from_right], axis=2)

def rolled_taps(rows, weight_of, taps):
    reach = taps // 2
    count = rows.shape[0]
    accumulated = None
    for offset in range(taps):
        product = jnp.dot(rows, weight_of(offset), preferred_element_type=jnp.float32)
        shift = (reach - offset) % count
        if shift:
            product = pltpu.roll(product, shift, 0)
        accumulated = product if accumulated is None else accumulated + product
    return accumulated


def merged(ref):
    shape = ref.shape
    return ref[0].reshape(shape[1] * shape[2], shape[3])


def first_kernel(rows_ref, taps_ref, keep_ref, out_ref):
    value = jax.nn.gelu(rolled_taps(merged(rows_ref), lambda k: taps_ref[0, k], taps_ref.shape[1]))
    value = jnp.where(keep_ref[...] > 0.5, value.astype(jnp.bfloat16), jnp.zeros((), jnp.bfloat16))
    out_ref[0] = value.reshape(out_ref.shape[1:])


def residual_layer(current, taps_ref):
    update = jax.nn.gelu(rolled_taps(current, lambda k: taps_ref[0, 0, k], taps_ref.shape[2]))
    return (current.astype(jnp.float32) + update).astype(jnp.bfloat16)


def hidden_kernel(rows_ref, taps_ref, keep_ref, out_ref):
    value = residual_layer(merged(rows_ref), taps_ref)
    value = jnp.where(keep_ref[...] > 0.5, value, jnp.zeros((), jnp.bfloat16))
    out_ref[0] = value.reshape(out_ref.shape[1:])


def last_kernel(rows_ref, taps_ref, keep_ref, mix_ref, out_ref):
    @pl.when(pl.program_id(0) == 0)
    def _():
        out_ref[...] = jnp.zeros_like(out_ref)

    span = rows_ref.shape[2]
    chunks, recordings, piece = out_ref.shape[:3]
    patches = chunks * piece
    margin = (span - patches) // 2
    value = merged(rows_ref)
    layers = taps_ref.shape[0]
    for depth_index in range(layers):
        value = residual_layer(value, taps_ref.at[depth_index : depth_index + 1])
        if depth_index + 1 < layers:
            value = jnp.where(keep_ref[...] > 0.5, value, jnp.zeros((), jnp.bfloat16))
    mixed = jnp.dot(value, mix_ref[0], preferred_element_type=jnp.float32)
    for item in range(recordings):
        for chunk in range(chunks):
            start = item * span + margin + chunk * piece
            out_ref[chunk, item] += mixed[start : start + piece]


def edge_keep(span, margin, rec_index, patches, recordings):
    total = patches * lax.axis_size("rec")
    spot = rec_index * patches - margin + jnp.arange(span, dtype=jnp.int32)
    keep = ((spot >= 0) & (spot < total)).astype(jnp.float32)
    return jnp.tile(jnp.broadcast_to(keep[:, None], (span, EMB)), (recordings, 1))


def per_type_call(kernel, rows, taps, side, out_block, out_shape, out_map, flops, layer=None):
    types, recordings = rows.shape[:2]
    side_spec = (
        pl.BlockSpec((1,) + side.shape[1:], lambda m: (m, 0, 0))
        if kernel is last_kernel
        else pl.BlockSpec(side.shape, lambda m: (0, 0))
    )
    return pl.pallas_call(
        kernel,
        grid=(types,),
        in_specs=[
            pl.BlockSpec((1,) + rows.shape[1:], lambda m: (m, 0, 0, 0)),
            pl.BlockSpec((1,) + taps.shape[1:], lambda m: (m, 0, 0, 0))
            if layer is None
            else pl.BlockSpec((1, 1) + taps.shape[2:], lambda m: (layer, m, 0, 0, 0)),
            side_spec,
        ],
        out_specs=pl.BlockSpec(out_block, out_map),
        out_shape=out_shape,
        compiler_params=pltpu.CompilerParams(dimension_semantics=("arbitrary",)),
        cost_estimate=pl.CostEstimate(
            flops=flops, transcendentals=rows.shape[0] * rows.shape[1] * rows.shape[2] * EMB,
            bytes_accessed=rows.size * 2 + taps.size * 2 // (1 if layer is None else taps.shape[0]) + side.size * 2 + out_shape.size * 4,
        ),
    )(rows, taps, side)


def conv_mix(extended, first_taps, hidden_taps, mix, rec_index, patches):
    types, recordings, span, width = extended.shape
    taps = first_taps.shape[1]
    layers = hidden_taps.shape[0]
    margin = (span - patches) // 2
    keep = edge_keep(span, margin, rec_index, patches, recordings)
    block = (1, recordings, span, EMB)
    inner = jax.ShapeDtypeStruct((types, recordings, span, EMB), jnp.bfloat16)
    current = per_type_call(
        first_kernel, extended, first_taps, keep, block, inner,
        lambda m: (m, 0, 0, 0), 2 * types * recordings * span * width * EMB * taps,
    )
    mix_width = mix.shape[-1]
    spread = lax.axis_size("chan")
    return pl.pallas_call(
        last_kernel,
        grid=(types,),
        in_specs=[
            pl.BlockSpec((1,) + current.shape[1:], lambda m: (m, 0, 0, 0)),
            pl.BlockSpec((layers, 1) + hidden_taps.shape[2:], lambda m: (0, m, 0, 0, 0)),
            pl.BlockSpec(keep.shape, lambda m: (0, 0)),
            pl.BlockSpec((1,) + mix.shape[1:], lambda m: (m, 0, 0)),
        ],
        out_specs=pl.BlockSpec((spread, recordings, patches // spread, mix_width), lambda m: (0, 0, 0, 0)),
        out_shape=jax.ShapeDtypeStruct((spread, recordings, patches // spread, mix_width), jnp.float32),
        compiler_params=pltpu.CompilerParams(dimension_semantics=("arbitrary",)),
        cost_estimate=pl.CostEstimate(
            flops=2 * types * recordings * span * EMB * (layers * EMB * taps + mix_width),
            transcendentals=layers * types * recordings * span * EMB,
            bytes_accessed=current.size * 2 + hidden_taps.size * 2 + mix.size * 2 + recordings * patches * mix_width * 4,
        ),
    )(current, hidden_taps, keep, mix)

def torus_gather(block, rec_index, side):
    inner = rec_index % side
    outer = rec_index // side
    devices = side * side

    def shifted(values, step, stride):
        route = []
        for source in range(devices):
            row, col = source // side, source % side
            if stride == 1:
                target = row * side + (col + step) % side
            else:
                target = ((row + step) % side) * side + col
            route.append((source, target))
        return lax.ppermute(values, "rec", route)

    along = jnp.concatenate([block] + [shifted(block, step, 1) for step in range(1, side)], axis=0)
    whole = jnp.concatenate([along] + [shifted(along, step, side) for step in range(1, side)], axis=0)
    types = jnp.arange(devices, dtype=jnp.int32)
    position = ((outer - types // side) % side) * side + (inner - types % side) % side
    return jnp.take(whole, position, axis=0)


def local(
    signal,
    montage,
    channels,
    lengths,
    boundary,
    conv_in,
    conv_hid,
    mix_weight,
    norm_gain,
    emit_weight,
    trans_within,
    trans_between,
    initial,
):
    groups = lax.axis_size("rec")
    chan_index = lax.axis_index("chan")
    rec_index = lax.axis_index("rec")
    recordings = signal.shape[0]
    patches = signal.shape[2] // SAMP
    slot_ids = chan_index * groups + jnp.arange(groups, dtype=jnp.int32)
    live_slots = slot_ids[None, :] < channels[:, None]
    places = jnp.arange(groups, dtype=jnp.int32)
    pick = (montage[:, 0, None, :] == places[None, :, None]) & live_slots[:, None, :]
    rows = jnp.einsum(
        "bms,bst->mbt", pick.astype(jnp.bfloat16), signal, preferred_element_type=jnp.float32
    ).astype(jnp.bfloat16)
    patch_rows = rows.reshape(groups, recordings, patches, SAMP)
    first_taps = lax.all_gather(conv_in[:, 0], "rec", tiled=True)
    hidden_taps = lax.all_gather(jnp.swapaxes(conv_hid[:, 0], 0, 1), "rec", axis=1, tiled=True)
    extended = halo_rows(patch_rows, HALO)
    partial_value = conv_mix(extended, first_taps, hidden_taps, mix_weight[:, 0], rec_index, patches)
    spread = lax.axis_size("chan")
    pieces = lax.all_to_all(partial_value, "chan", 0, 0, tiled=True)
    summed = jnp.sum(pieces, axis=0)
    average = jnp.mean(summed, axis=-1, keepdims=True)
    centred = summed - average
    variance = jnp.mean(centred * centred, axis=-1, keepdims=True)
    activated = jax.nn.gelu(centred * lax.rsqrt(variance + EPSILON) * norm_gain)
    emission = jnp.einsum("bpo,os->bps", activated, emit_weight, precision=lax.Precision.HIGHEST)
    shared = lax.all_to_all(jnp.broadcast_to(emission[None], (spread,) + emission.shape), "chan", 0, 0, tiled=True)
    emission = jnp.swapaxes(shared, 0, 1).reshape(recordings, patches, STATES)
    positions = rec_index * patches + jnp.arange(patches, dtype=jnp.int32)
    valid = positions[None, :] < lengths[:, None]
    cross = boundary == 1
    filtered, log_partition = crf_forward(
        emission, cross, valid, trans_within, trans_between, initial, rec_index
    )
    return (filtered, log_partition / lengths.astype(jnp.float32))


def solution(mesh):
    placed = (
        P(None, "chan", "rec"),
        P(None, "chan", None),
        P(),
        P(),
        P(None, "rec"),
        P("rec", "chan", None, None, None),
        P("rec", "chan", None, None, None, None),
        P(None, "chan", None, None),
        P(),
        P(),
        P(),
        P(),
        P(),
    )
    return jax.shard_map(
        local, mesh=mesh, in_specs=placed, out_specs=(P(None, None, "rec"), P()), check_vma=False
    )
```

```python
import functools

import jax
import jax.numpy as jnp
from jax import lax
from jax.experimental import pallas as pl
from jax.experimental.pallas import tpu as pltpu
from jax.sharding import PartitionSpec as P

SAMP = 200
EMB = 128
STATES = 5


EPSILON = 1e-05
NEGATIVE = -1e30
MESH_SIDE = 4
SUBSHARDS = 4
HALO = 8


def log_sum_exp(values, along):
    peak_value = jnp.max(values, axis=along, keepdims=True)
    return jnp.squeeze(peak_value, along) + jnp.log(
        jnp.sum(jnp.exp(values - peak_value), axis=along)
    )


LANES = 128


def forward_step(state, matrices, extra):
    terms = [state[i : i + 1, :] + matrices[i] for i in range(len(matrices))]
    peak = functools.reduce(jnp.maximum, terms)
    total = functools.reduce(lambda x, y: x + y, [jnp.exp(t - peak) for t in terms])
    moved = peak + jnp.log(total)
    if extra is not None:
        moved = moved + extra
    top = jnp.max(moved, axis=0, keepdims=True)
    level = top + jnp.log(jnp.sum(jnp.exp(moved - top), axis=0, keepdims=True))
    return moved - level, level


def prefix_kernel(within_ref, between_ref, start_ref, emit_ref, cross_ref, valid_ref, prefix_ref, offset_ref):
    patches = emit_ref.shape[0]
    lanes = start_ref.shape[1]
    within = [jnp.broadcast_to(within_ref[i], (STATES, lanes)) for i in range(STATES)]
    between = [jnp.broadcast_to(between_ref[i], (STATES, lanes)) for i in range(STATES)]

    def body(p, carry):
        state, offset = carry
        crossing = cross_ref[p] > 0.5
        counted = valid_ref[p] > 0.5
        matrices = [jnp.where(crossing, between[i], within[i]) for i in range(STATES)]
        moved, level = forward_step(state, matrices, emit_ref[p])
        state = jnp.where(counted, moved, state)
        offset = offset + jnp.where(counted, level, 0.0)
        prefix_ref[p] = state
        offset_ref[p] = offset
        return state, offset

    lax.fori_loop(0, patches, body, (start_ref[...], jnp.zeros((1, LANES), jnp.float32)), unroll=True)


def chain_kernel(prior_ref, mats_ref, incoming_ref, total_ref):
    count = mats_ref.shape[0]

    def body(k, carry):
        state, total = carry
        incoming_ref[k] = state
        matrices = [mats_ref[k, j] for j in range(STATES)]
        moved, level = forward_step(state, matrices, None)
        return moved, total + level

    _, total = lax.fori_loop(0, count, body, (prior_ref[...], jnp.zeros((1, prior_ref.shape[1]), jnp.float32)), unroll=True)
    total_ref[...] = total


def lanes_padded(values):
    pad = [(0, 0)] * (values.ndim - 1) + [(0, LANES - values.shape[-1])]
    return jnp.pad(values, pad)


def crf_forward(emission, cross, valid, trans_within, trans_between, initial, rec_index):
    recordings, patches, _ = emission.shape
    pieces = SUBSHARDS
    steps = patches // pieces
    block = STATES * recordings
    width = pieces * block

    def to_lanes(values):
        split = values.reshape((recordings, pieces, steps) + values.shape[2:])
        order = (2,) + tuple(range(3, split.ndim)) + (1, 0)
        moved = jnp.transpose(split, order)
        moved = jnp.broadcast_to(moved[..., None, :], moved.shape[:-1] + (STATES, recordings))
        return lanes_padded(moved.reshape(moved.shape[:-3] + (width,)))

    emit_in = to_lanes(emission)
    cross_in = to_lanes(cross.astype(jnp.float32))[:, None, :]
    valid_in = to_lanes(valid.astype(jnp.float32))[:, None, :]
    lane_start = (jnp.arange(width, dtype=jnp.int32) // recordings) % STATES
    basis = jnp.arange(STATES, dtype=jnp.int32)[:, None] == lane_start[None, :]
    start = lanes_padded(jnp.where(basis, 0.0, NEGATIVE).astype(jnp.float32))
    within_in = trans_within[:, :, None]
    between_in = trans_between[:, :, None]
    prefix, offset = pl.pallas_call(
        prefix_kernel,
        out_shape=(
            jax.ShapeDtypeStruct((steps, STATES, LANES), jnp.float32),
            jax.ShapeDtypeStruct((steps, 1, LANES), jnp.float32),
        ),
        cost_estimate=pl.CostEstimate(
            flops=steps * 80 * LANES * 8, transcendentals=steps * 8 * LANES * 8,
            bytes_accessed=steps * 14 * LANES * 4,
        ),
    )(within_in, between_in, start, emit_in, cross_in, valid_in)
    prefix_sj = prefix[:, :, :width].reshape(steps, STATES, pieces, STATES, recordings)
    offset_j = offset[:, 0, :width].reshape(steps, pieces, STATES, recordings)
    transfer = prefix_sj[steps - 1] + offset_j[steps - 1][None]
    transfer = jnp.transpose(transfer, (1, 2, 0, 3))
    gathered = torus_gather(transfer[None], rec_index, MESH_SIDE)
    gathered = gathered.reshape((-1,) + gathered.shape[2:])
    mats = gathered
    prior = initial - log_sum_exp(initial, 0)
    prior_in = jnp.broadcast_to(prior[:, None], (STATES, recordings))
    count = gathered.shape[0]
    incoming, total = pl.pallas_call(
        chain_kernel,
        out_shape=(
            jax.ShapeDtypeStruct((count, STATES, recordings), jnp.float32),
            jax.ShapeDtypeStruct((1, recordings), jnp.float32),
        ),
    )(prior_in, mats)
    here = lax.dynamic_slice_in_dim(incoming, rec_index * pieces, pieces, 0)[:, :, :recordings]
    weights = here[None, None] + offset_j[:, None] + prefix_sj
    reached = log_sum_exp(weights, 3)
    totals = log_sum_exp(reached, 1)
    normalized = reached - totals[:, None]
    filtered = jnp.transpose(normalized, (3, 1, 2, 0)).reshape(recordings, STATES, patches)
    return filtered, total[0, :recordings]

def neighbour_shift(block, axis, distance):
    devices = range(lax.axis_size(axis))
    route = [(i - distance, i) for i in devices if i - distance in devices]
    return lax.ppermute(block, axis, route)


def halo_rows(patch_rows, halo):
    patches = patch_rows.shape[2]
    from_left = neighbour_shift(patch_rows[:, :, patches - halo :], "rec", 1)
    from_right = neighbour_shift(patch_rows[:, :, :halo], "rec", -1)
    return jnp.concatenate([from_left, patch_rows, from_right], axis=2)

def rolled_taps(rows, weight_of, taps):
    reach = taps // 2
    count = rows.shape[0]
    accumulated = None
    for offset in range(taps):
        product = jnp.dot(rows, weight_of(offset), preferred_element_type=jnp.float32)
        shift = (reach - offset) % count
        if shift:
            product = pltpu.roll(product, shift, 0)
        accumulated = product if accumulated is None else accumulated + product
    return accumulated


def merged(ref):
    shape = ref.shape
    return ref[0].reshape(shape[1] * shape[2], shape[3])


def first_kernel(rows_ref, taps_ref, keep_ref, out_ref):
    value = jax.nn.gelu(rolled_taps(merged(rows_ref), lambda k: taps_ref[0, k], taps_ref.shape[1]))
    value = jnp.where(keep_ref[...] > 0.5, value.astype(jnp.bfloat16), jnp.zeros((), jnp.bfloat16))
    out_ref[0] = value.reshape(out_ref.shape[1:])


def residual_layer(current, taps_ref):
    update = jax.nn.gelu(rolled_taps(current, lambda k: taps_ref[0, 0, k], taps_ref.shape[2]))
    return (current.astype(jnp.float32) + update).astype(jnp.bfloat16)


def hidden_kernel(rows_ref, taps_ref, keep_ref, out_ref):
    value = residual_layer(merged(rows_ref), taps_ref)
    value = jnp.where(keep_ref[...] > 0.5, value, jnp.zeros((), jnp.bfloat16))
    out_ref[0] = value.reshape(out_ref.shape[1:])


def last_kernel(rows_ref, taps_ref, keep_ref, mix_ref, out_ref):
    @pl.when(pl.program_id(0) == 0)
    def _():
        out_ref[...] = jnp.zeros_like(out_ref)

    span = rows_ref.shape[2]
    chunks, recordings, piece = out_ref.shape[:3]
    patches = chunks * piece
    margin = (span - patches) // 2
    value = merged(rows_ref)
    layers = taps_ref.shape[0]
    for depth_index in range(layers):
        value = residual_layer(value, taps_ref.at[depth_index : depth_index + 1])
        if depth_index + 1 < layers:
            value = jnp.where(keep_ref[...] > 0.5, value, jnp.zeros((), jnp.bfloat16))
    mixed = jnp.dot(value, mix_ref[0], preferred_element_type=jnp.float32)
    for item in range(recordings):
        for chunk in range(chunks):
            start = item * span + margin + chunk * piece
            out_ref[chunk, item] += mixed[start : start + piece]


def edge_keep(span, margin, rec_index, patches, recordings):
    total = patches * lax.axis_size("rec")
    spot = rec_index * patches - margin + jnp.arange(span, dtype=jnp.int32)
    keep = ((spot >= 0) & (spot < total)).astype(jnp.float32)
    return jnp.tile(jnp.broadcast_to(keep[:, None], (span, EMB)), (recordings, 1))


def per_type_call(kernel, rows, taps, side, out_block, out_shape, out_map, flops, layer=None):
    types, recordings = rows.shape[:2]
    side_spec = (
        pl.BlockSpec((1,) + side.shape[1:], lambda m: (m, 0, 0))
        if kernel is last_kernel
        else pl.BlockSpec(side.shape, lambda m: (0, 0))
    )
    return pl.pallas_call(
        kernel,
        grid=(types,),
        in_specs=[
            pl.BlockSpec((1,) + rows.shape[1:], lambda m: (m, 0, 0, 0)),
            pl.BlockSpec((1,) + taps.shape[1:], lambda m: (m, 0, 0, 0))
            if layer is None
            else pl.BlockSpec((1, 1) + taps.shape[2:], lambda m: (layer, m, 0, 0, 0)),
            side_spec,
        ],
        out_specs=pl.BlockSpec(out_block, out_map),
        out_shape=out_shape,
        compiler_params=pltpu.CompilerParams(dimension_semantics=("arbitrary",)),
        cost_estimate=pl.CostEstimate(
            flops=flops, transcendentals=rows.shape[0] * rows.shape[1] * rows.shape[2] * EMB,
            bytes_accessed=rows.size * 2 + taps.size * 2 // (1 if layer is None else taps.shape[0]) + side.size * 2 + out_shape.size * 4,
        ),
    )(rows, taps, side)


def conv_mix(extended, first_taps, hidden_taps, mix, rec_index, patches):
    types, recordings, span, width = extended.shape
    taps = first_taps.shape[1]
    layers = hidden_taps.shape[0]
    margin = (span - patches) // 2
    keep = edge_keep(span, margin, rec_index, patches, recordings)
    block = (1, recordings, span, EMB)
    inner = jax.ShapeDtypeStruct((types, recordings, span, EMB), jnp.bfloat16)
    current = per_type_call(
        first_kernel, extended, first_taps, keep, block, inner,
        lambda m: (m, 0, 0, 0), 2 * types * recordings * span * width * EMB * taps,
    )
    mix_width = mix.shape[-1]
    spread = lax.axis_size("chan")
    return pl.pallas_call(
        last_kernel,
        grid=(types,),
        in_specs=[
            pl.BlockSpec((1,) + current.shape[1:], lambda m: (m, 0, 0, 0)),
            pl.BlockSpec((layers, 1) + hidden_taps.shape[2:], lambda m: (0, m, 0, 0, 0)),
            pl.BlockSpec(keep.shape, lambda m: (0, 0)),
            pl.BlockSpec((1,) + mix.shape[1:], lambda m: (m, 0, 0)),
        ],
        out_specs=pl.BlockSpec((spread, recordings, patches // spread, mix_width), lambda m: (0, 0, 0, 0)),
        out_shape=jax.ShapeDtypeStruct((spread, recordings, patches // spread, mix_width), jnp.float32),
        compiler_params=pltpu.CompilerParams(dimension_semantics=("arbitrary",)),
        cost_estimate=pl.CostEstimate(
            flops=2 * types * recordings * span * EMB * (layers * EMB * taps + mix_width),
            transcendentals=layers * types * recordings * span * EMB,
            bytes_accessed=current.size * 2 + hidden_taps.size * 2 + mix.size * 2 + recordings * patches * mix_width * 4,
        ),
    )(current, hidden_taps, keep, mix)

def torus_gather(block, rec_index, side):
    inner = rec_index % side
    outer = rec_index // side
    devices = side * side

    def shifted(values, step, stride):
        route = []
        for source in range(devices):
            row, col = source // side, source % side
            if stride == 1:
                target = row * side + (col + step) % side
            else:
                target = ((row + step) % side) * side + col
            route.append((source, target))
        return lax.ppermute(values, "rec", route)

    along = jnp.concatenate([block] + [shifted(block, step, 1) for step in range(1, side)], axis=0)
    whole = jnp.concatenate([along] + [shifted(along, step, side) for step in range(1, side)], axis=0)
    types = jnp.arange(devices, dtype=jnp.int32)
    position = ((outer - types // side) % side) * side + (inner - types % side) % side
    return jnp.take(whole, position, axis=0)


def local(
    signal,
    montage,
    channels,
    lengths,
    boundary,
    conv_in,
    conv_hid,
    mix_weight,
    norm_gain,
    emit_weight,
    trans_within,
    trans_between,
    initial,
):
    groups = lax.axis_size("rec")
    chan_index = lax.axis_index("chan")
    rec_index = lax.axis_index("rec")
    recordings = signal.shape[0]
    patches = signal.shape[2] // SAMP
    slot_ids = chan_index * groups + jnp.arange(groups, dtype=jnp.int32)
    live_slots = slot_ids[None, :] < channels[:, None]
    places = jnp.arange(groups, dtype=jnp.int32)
    pick = (montage[:, 0, None, :] == places[None, :, None]) & live_slots[:, None, :]
    rows = jnp.einsum(
        "bms,bst->mbt", pick.astype(jnp.bfloat16), signal, preferred_element_type=jnp.float32
    ).astype(jnp.bfloat16)
    patch_rows = rows.reshape(groups, recordings, patches, SAMP)
    first_taps = lax.all_gather(conv_in[:, 0], "rec", tiled=True)
    hidden_taps = lax.all_gather(jnp.swapaxes(conv_hid[:, 0], 0, 1), "rec", axis=1, tiled=True)
    extended = halo_rows(patch_rows, HALO)
    partial_value = conv_mix(extended, first_taps, hidden_taps, mix_weight[:, 0], rec_index, patches)
    spread = lax.axis_size("chan")
    pieces = lax.all_to_all(partial_value, "chan", 0, 0, tiled=True)
    summed = jnp.sum(pieces, axis=0)
    average = jnp.mean(summed, axis=-1, keepdims=True)
    centred = summed - average
    variance = jnp.mean(centred * centred, axis=-1, keepdims=True)
    activated = jax.nn.gelu(centred * lax.rsqrt(variance + EPSILON) * norm_gain)
    emission = jnp.einsum("bpo,os->bps", activated, emit_weight, precision=lax.Precision.HIGHEST)
    shared = lax.all_to_all(jnp.broadcast_to(emission[None], (spread,) + emission.shape), "chan", 0, 0, tiled=True)
    emission = jnp.swapaxes(shared, 0, 1).reshape(recordings, patches, STATES)
    positions = rec_index * patches + jnp.arange(patches, dtype=jnp.int32)
    valid = positions[None, :] < lengths[:, None]
    cross = boundary == 1
    filtered, log_partition = crf_forward(
        emission, cross, valid, trans_within, trans_between, initial, rec_index
    )
    return (filtered, log_partition / lengths.astype(jnp.float32))


def solution(mesh):
    placed = (
        P(None, "chan", "rec"),
        P(None, "chan", None),
        P(),
        P(),
        P(None, "rec"),
        P("rec", "chan", None, None, None),
        P("rec", "chan", None, None, None, None),
        P(None, "chan", None, None),
        P(),
        P(),
        P(),
        P(),
        P(),
    )
    return jax.shard_map(
        local, mesh=mesh, in_specs=placed, out_specs=(P(None, None, "rec"), P()), check_vma=False
    )
```
